128 devices in a mesh: role: 2 (over core), slab: 64 (over x, y, z).
Axes of the slice: x: 4, y: 4, z: 4, core: 2. Of those that a mesh axis runs over, the one named last changes fastest.
Arguments:
- velocity: float32 [4, 128, 128, 256], P(None, 'slab', 'role'), may hold values from -18 to 18
- basis: bfloat16 [256, 128, 128, 256], P(None, 'slab', 'role'), may hold values from -1 to 1, as said below
- mean_flow: float32 [128], replicated, may hold values from 0.2 to 2
- shear: float32 [128], replicated, may hold values from -1 to 1
Outputs:
- advanced: float32 [4, 128, 128, 256], P(None, 'slab', 'role')
- coeffs: float32 [256, 8], replicated
- rfactor: float32 [8, 8], replicated
- directions: float32 [8, 128, 128, 256], P(None, 'slab', 'role')
The draws below stay inside these ranges and needn't reach their ends.
Inputs may be any that keep to these rules, and one draw needn't show every extreme that they name: Every column of the basis has length within a few percent of one, and distinct columns are nearly orthogonal.
All inputs are finite; a program needn't handle non-finite values.
Results may differ from the reference program's by a relative error of at most 0.00035.
The reference program's roundings to bfloat16 on the way count: a program that leaves them out, or rounds other values in their place, can miss the bound.
Values sent between devices are 32-bit elements; how exact they have to be, the bound alone decides.
No kernel may reach another device: no remote copies, remote signals or barrier semaphores. Data moves between devices by JAX's collectives and lax.ppermute only.
A program may use at most 128 MiB of HBM per device.

```python
import math
import jax
import jax.numpy as jnp
from jax import lax

NZ = 256
NQ = 4
K = 256
NX = 128
NY = 128


def column_values(key, column_index):
    column_key = jax.random.fold_in(jax.random.fold_in(key, 7001), column_index)
    return jax.random.truncated_normal(column_key, -4.0, 4.0, (NX, NY, NZ), jnp.float32)


def draw_basis(key, part):
    column_scale = 1.0 / math.sqrt(NX * NY * NZ)
    return lax.map(lambda column_index: column_values(key, column_index) * column_scale, jnp.arange(K, dtype=jnp.int32)).astype(jnp.bfloat16)


def draw_velocity(key, part):
    picked = jax.random.permutation(jax.random.fold_in(key, 7002), K)[:NQ * 8].reshape(NQ, 8)
    sign_values = (jax.random.randint(jax.random.fold_in(key, 7003), (NQ, 8), 0, 2) * 2 - 1).astype(jnp.float32)
    weights = sign_values * jax.random.uniform(jax.random.fold_in(key, 7004), (NQ, 8), jnp.float32, 0.25, 0.5)
    noise_key = jax.random.fold_in(key, 7005)
    noise_part = 0.5 * jax.random.truncated_normal(noise_key, -4.0, 4.0, (NQ, NX, NY, NZ), jnp.float32)
    fields = []
    for field_index in range(NQ):
        running = noise_part[field_index]
        for term_index in range(8):
            running = running + weights[field_index, term_index] * column_values(key, picked[field_index, term_index])
        fields.append(running)
    return jnp.stack(fields)


def setup_inputs(seed: int = 0) -> dict:
    seeds = jax.random.split(jax.random.key(seed), 5)
    velocity = draw_velocity(jax.random.fold_in(seeds[4], 71), 0)
    basis = draw_basis(jax.random.fold_in(seeds[4], 71), 0)
    mean_flow = jnp.clip(jnp.exp(jax.random.uniform(seeds[2], (NY,), jnp.float32, math.log(0.2), math.log(2.0))), 0.2, 2.0)
    shear = jnp.clip(jax.random.uniform(seeds[3], (NY,), jnp.float32, -1.0, 1.0), -1.0, 1.0)
    return dict(velocity=velocity, basis=basis, mean_flow=mean_flow, shear=shear)


viscosity = 0.1
time_step = 0.4

def offset_slice(padded, offset, dimension, length):
    return lax.slice_in_dim(padded, 2 + offset, 2 + offset + length, axis=dimension)

def second_diff(padded, center, dimension, length):
    return (-offset_slice(padded, 2, dimension, length) + 16.0 * offset_slice(padded, 1, dimension, length) - 30.0 * center + 16.0 * offset_slice(padded, -1, dimension, length) - offset_slice(padded, -2, dimension, length)) / 12.0

def tendency(center, xpadded, ypadded, mean_flow, shear):
    nx_loc = center.shape[1]
    ny_loc = center.shape[2]
    nz_loc = center.shape[3]
    zpadded = jnp.concatenate([center[..., -2:], center, center[..., :2]], axis=3)
    first_x = (-offset_slice(xpadded, 2, 1, nx_loc) + 8.0 * offset_slice(xpadded, 1, 1, nx_loc) - 8.0 * offset_slice(xpadded, -1, 1, nx_loc) + offset_slice(xpadded, -2, 1, nx_loc)) / 12.0
    laplace = second_diff(xpadded, center, 1, nx_loc) + second_diff(ypadded, center, 2, ny_loc) + second_diff(zpadded, center, 3, nz_loc)
    profile = mean_flow[None, None, :, None]
    result = -profile * first_x + viscosity * laplace
    shear_term = shear[None, None, :, None] * center[1:2]
    return jnp.concatenate([result[:1] - shear_term, result[1:]], axis=0)

def full_tendency(state, mean_flow, shear):
    xpadded = jnp.pad(state, ((0, 0), (2, 2), (0, 0), (0, 0)), mode='wrap')
    ypadded = jnp.pad(state, ((0, 0), (0, 0), (2, 2), (0, 0)))
    return tendency(state, xpadded, ypadded, mean_flow, shear)

def reference(velocity, basis, mean_flow, shear):
    tend_zero = full_tendency(velocity, mean_flow, shear)
    segment_one = velocity + time_step * (8.0 / 15.0) * tend_zero
    tend_one = full_tendency(segment_one, mean_flow, shear)
    advanced = segment_one + time_step * (5.0 / 12.0 * tend_one - 17.0 / 60.0 * tend_zero)
    snapshots = jnp.concatenate([segment_one, advanced], axis=0)
    flat_snaps = snapshots.reshape(snapshots.shape[0], -1)
    snaps_bf = flat_snaps.astype(jnp.bfloat16)
    basis_rows = basis.reshape(basis.shape[0], -1)
    coeffs = jnp.dot(basis_rows.astype(jnp.float32), snaps_bf.T.astype(jnp.float32), preferred_element_type=jnp.float32)
    coeffs_bf = coeffs.astype(jnp.bfloat16)
    residual = flat_snaps - jnp.dot(coeffs_bf.T.astype(jnp.float32), basis_rows.astype(jnp.float32), preferred_element_type=jnp.float32)
    gram_matrix = jnp.dot(residual, residual.T, precision=lax.Precision.HIGHEST)
    lower_factor = jnp.linalg.cholesky(gram_matrix)
    directions = jax.scipy.linalg.solve_triangular(lower_factor, residual, lower=True)
    return (advanced, coeffs, lower_factor.T, directions.reshape(snapshots.shape))
```

```python
import jax
import jax.numpy as jnp
from jax import lax
from jax.sharding import PartitionSpec as P

viscosity = 0.1
time_step = 0.4


def extended(cells, sides, width, closed):
    for axis, dim in sides:
        count = lax.axis_size(axis)
        ends = count if closed else count - 1
        head = lax.slice_in_dim(cells, 0, width, axis=dim)
        tail = lax.slice_in_dim(cells, cells.shape[dim] - width, cells.shape[dim], axis=dim)
        cells = jnp.concatenate(
            [
                lax.ppermute(tail, axis, [(i, (i + 1) % count) for i in range(ends)]),
                cells,
                lax.ppermute(head, axis, [((i + 1) % count, i) for i in range(ends)]),
            ],
            axis=dim,
        )
    return cells


def ring_pairs(size, stride, count, second):
    pairs = []
    for i in range(count):
        digit = (i // stride) % size
        if size == 2 or not second:
            partner = digit ^ 1
        else:
            partner = (digit + 1) % size if digit % 2 else (digit - 1) % size
        pairs.append((i, i + (partner - digit) * stride))
    return pairs


def exchange_rounds(axis, count):
    rounds = []
    stride = 1
    while stride < count:
        size = 4 if count % (stride * 4) == 0 else 2
        rounds.append(ring_pairs(size, stride, count, False))
        if size == 4:
            rounds.append(ring_pairs(size, stride, count, True))
        stride *= size
    return [(axis, pairs) for pairs in rounds]


def allreduce(value, axes):
    sizes = [lax.axis_size(axis) for axis in axes]
    if any(size & (size - 1) for size in sizes):
        return lax.psum(value, axes)
    for axis, size in zip(axes, sizes):
        for name, pairs in exchange_rounds(axis, size):
            value = value + lax.ppermute(value, name, pairs)
    return value


def offset_slice(padded, offset, dimension, length):
    return lax.slice_in_dim(padded, 2 + offset, 2 + offset + length, axis=dimension)


def second_diff(padded, center, dimension, length):
    return (
        -offset_slice(padded, 2, dimension, length)
        + 16.0 * offset_slice(padded, 1, dimension, length)
        - 30.0 * center
        + 16.0 * offset_slice(padded, -1, dimension, length)
        - offset_slice(padded, -2, dimension, length)
    ) / 12.0


def stencil(center, xpadded, ypadded, flow_rows, shear_rows):
    nx_loc = center.shape[1]
    ny_loc = center.shape[2]
    nz_loc = center.shape[3]
    zpadded = jnp.concatenate([center[..., -2:], center, center[..., :2]], axis=3)
    first_x = (
        -offset_slice(xpadded, 2, 1, nx_loc)
        + 8.0 * offset_slice(xpadded, 1, 1, nx_loc)
        - 8.0 * offset_slice(xpadded, -1, 1, nx_loc)
        + offset_slice(xpadded, -2, 1, nx_loc)
    ) / 12.0
    laplace = (
        second_diff(xpadded, center, 1, nx_loc)
        + second_diff(ypadded, center, 2, ny_loc)
        + second_diff(zpadded, center, 3, nz_loc)
    )
    profile = flow_rows[None, None, :, None]
    result = -profile * first_x + viscosity * laplace
    shear_term = shear_rows[None, None, :, None] * center[1:2]
    return jnp.concatenate([result[:1] - shear_term, result[1:]], axis=0)


def segmented_tendency(center, flow_rows, shear_rows):
    xpadded = extended(center, (("slab", 1),), 2, True)
    ypadded = extended(center, (("role", 2),), 2, False)
    return stencil(center, xpadded, ypadded, flow_rows, shear_rows)


def on_device(velocity, basis, mean_flow, shear):
    ny_loc = velocity.shape[2]
    role_index = lax.axis_index("role")
    flow_rows = lax.dynamic_slice_in_dim(mean_flow, role_index * ny_loc, ny_loc)
    shear_rows = lax.dynamic_slice_in_dim(shear, role_index * ny_loc, ny_loc)
    tend_zero = segmented_tendency(velocity, flow_rows, shear_rows)
    segment_one = velocity + time_step * (8.0 / 15.0) * tend_zero
    tend_one = segmented_tendency(segment_one, flow_rows, shear_rows)
    advanced = segment_one + time_step * (5.0 / 12.0 * tend_one - 17.0 / 60.0 * tend_zero)
    snapshots = jnp.concatenate([segment_one, advanced], axis=0)
    flat_snaps = snapshots.reshape(snapshots.shape[0], -1)
    snaps_bf = flat_snaps.astype(jnp.bfloat16)
    basis_rows = basis.reshape(basis.shape[0], -1)
    partial_proj = jnp.einsum("km,sm->ks", basis_rows, snaps_bf, preferred_element_type=jnp.float32)
    coeffs = allreduce(partial_proj, ("role", "slab"))
    coeffs_bf = coeffs.astype(jnp.bfloat16)
    residual = flat_snaps - jnp.einsum(
        "ks,km->sm", coeffs_bf, basis_rows, preferred_element_type=jnp.float32
    )
    local_gram = jnp.dot(residual, residual.T, precision=lax.Precision.HIGHEST)
    total_gram = allreduce(local_gram, ("role", "slab"))
    lower_factor = jnp.linalg.cholesky(total_gram)
    directions = jax.scipy.linalg.solve_triangular(lower_factor, residual, lower=True)
    return (advanced, coeffs, lower_factor.T, directions.reshape(snapshots.shape))


def solution(mesh):
    return jax.shard_map(
        on_device,
        mesh=mesh,
        in_specs=(P(None, "slab", "role", None), P(None, "slab", "role", None), P(), P()),
        out_specs=(P(None, "slab", "role", None), P(), P(), P(None, "slab", "role", None)),
        check_vma=False,
    )
```

```python
import jax
import jax.numpy as jnp
from jax import lax
from jax.experimental import pallas as pl
from jax.sharding import PartitionSpec as P

viscosity = 0.1
ROWS = 16
time_step = 0.4


def extended(cells, sides, width, closed):
    for axis, dim in sides:
        count = lax.axis_size(axis)
        ends = count if closed else count - 1
        head = lax.slice_in_dim(cells, 0, width, axis=dim)
        tail = lax.slice_in_dim(cells, cells.shape[dim] - width, cells.shape[dim], axis=dim)
        cells = jnp.concatenate(
            [
                lax.ppermute(tail, axis, [(i, (i + 1) % count) for i in range(ends)]),
                cells,
                lax.ppermute(head, axis, [((i + 1) % count, i) for i in range(ends)]),
            ],
            axis=dim,
        )
    return cells


def ring_pairs(size, stride, count, second):
    pairs = []
    for i in range(count):
        digit = (i // stride) % size
        if size == 2 or not second:
            partner = digit ^ 1
        else:
            partner = (digit + 1) % size if digit % 2 else (digit - 1) % size
        pairs.append((i, i + (partner - digit) * stride))
    return pairs


def exchange_rounds(axis, count):
    rounds = []
    stride = 1
    while stride < count:
        size = 4 if count % (stride * 4) == 0 else 2
        rounds.append(ring_pairs(size, stride, count, False))
        if size == 4:
            rounds.append(ring_pairs(size, stride, count, True))
        stride *= size
    return [(axis, pairs) for pairs in rounds]


def allreduce(value, axes):
    sizes = [lax.axis_size(axis) for axis in axes]
    if any(size & (size - 1) for size in sizes):
        return lax.psum(value, axes)
    for axis, size in zip(axes, sizes):
        for name, pairs in exchange_rounds(axis, size):
            value = value + lax.ppermute(value, name, pairs)
    return value


def project_kernel(b_ref, s_ref, o_ref):
    tk, nr, nz = b_ref.shape
    ns = s_ref.shape[0]
    acc = jnp.zeros((tk * ROWS, ns * ROWS), jnp.float32)
    for j in range(nr // ROWS):
        rows = pl.ds(j * ROWS, ROWS)
        lhs = b_ref[:, rows, :].reshape(tk * ROWS, nz)
        rhs = s_ref[:, rows, :].reshape(ns * ROWS, nz)
        acc = acc + lax.dot_general(lhs, rhs, (((1,), (1,)), ((), ())), preferred_element_type=jnp.float32)
    row_t = lax.broadcasted_iota(jnp.int32, acc.shape, 0) % ROWS
    col_t = lax.broadcasted_iota(jnp.int32, acc.shape, 1) % ROWS
    acc = jnp.where(row_t == col_t, acc, 0.0)
    o_ref[...] = jnp.sum(acc.reshape(tk, ROWS, ns * ROWS), axis=1)


def project(basis3, snaps3, tk=32):
    nk, nr, nz = basis3.shape
    ns = snaps3.shape[0]
    out = pl.pallas_call(
        project_kernel,
        grid=(nk // tk,),
        in_specs=[pl.BlockSpec((tk, nr, nz), lambda i: (i, 0, 0)),
                  pl.BlockSpec((ns, nr, nz), lambda i: (0, 0, 0))],
        out_specs=pl.BlockSpec((tk, ns * ROWS), lambda i: (i, 0)),
        out_shape=jax.ShapeDtypeStruct((nk, ns * ROWS), jnp.float32),
        cost_estimate=pl.CostEstimate(flops=2 * nk * nr * nz * ns * ROWS, transcendentals=0,
                                      bytes_accessed=nk * nr * nz * 2 + ns * nr * nz * 2 + nk * ns * ROWS * 4),
    )(basis3, snaps3)
    return jnp.sum(out.reshape(nk, ns, ROWS), axis=2)


def residual_kernel(l_ref, b_ref, s_ref, o_ref):
    nk, rows, nz = b_ref.shape
    ns = s_ref.shape[0]
    prod = jnp.dot(l_ref[...], b_ref[...].reshape(nk * rows, nz), preferred_element_type=jnp.float32)
    o_ref[...] = s_ref[...] - prod.reshape(ns, rows, nz)


def residual(coeffs_bf, basis3, snaps3):
    nk, nr, nz = basis3.shape
    ns = snaps3.shape[0]
    eye = jnp.eye(ROWS, dtype=jnp.bfloat16)
    spread = (coeffs_bf.T[:, None, :, None] * eye[None, :, None, :]).reshape(ns * ROWS, nk * ROWS)
    return pl.pallas_call(
        residual_kernel,
        grid=(nr // ROWS,),
        in_specs=[pl.BlockSpec((ns * ROWS, nk * ROWS), lambda j: (0, 0)),
                  pl.BlockSpec((nk, ROWS, nz), lambda j: (0, j, 0)),
                  pl.BlockSpec((ns, ROWS, nz), lambda j: (0, j, 0))],
        out_specs=pl.BlockSpec((ns, ROWS, nz), lambda j: (0, j, 0)),
        out_shape=jax.ShapeDtypeStruct((ns, nr, nz), jnp.float32),
        cost_estimate=pl.CostEstimate(flops=2 * ns * ROWS * nk * ROWS * nz * (nr // ROWS), transcendentals=0,
                                      bytes_accessed=nk * nr * nz * 2 + 2 * ns * nr * nz * 4),
    )(spread, basis3, snaps3)


def offset_slice(padded, offset, dimension, length):
    return lax.slice_in_dim(padded, 2 + offset, 2 + offset + length, axis=dimension)


def second_diff(padded, center, dimension, length):
    return (
        -offset_slice(padded, 2, dimension, length)
        + 16.0 * offset_slice(padded, 1, dimension, length)
        - 30.0 * center
        + 16.0 * offset_slice(padded, -1, dimension, length)
        - offset_slice(padded, -2, dimension, length)
    ) / 12.0


def stencil(center, xpadded, ypadded, flow_rows, shear_rows):
    nx_loc = center.shape[1]
    ny_loc = center.shape[2]
    nz_loc = center.shape[3]
    zpadded = jnp.concatenate([center[..., -2:], center, center[..., :2]], axis=3)
    first_x = (
        -offset_slice(xpadded, 2, 1, nx_loc)
        + 8.0 * offset_slice(xpadded, 1, 1, nx_loc)
        - 8.0 * offset_slice(xpadded, -1, 1, nx_loc)
        + offset_slice(xpadded, -2, 1, nx_loc)
    ) / 12.0
    laplace = (
        second_diff(xpadded, center, 1, nx_loc)
        + second_diff(ypadded, center, 2, ny_loc)
        + second_diff(zpadded, center, 3, nz_loc)
    )
    profile = flow_rows[None, None, :, None]
    result = -profile * first_x + viscosity * laplace
    shear_term = shear_rows[None, None, :, None] * center[1:2]
    return jnp.concatenate([result[:1] - shear_term, result[1:]], axis=0)


def segmented_tendency(center, flow_rows, shear_rows):
    xpadded = extended(center, (("slab", 1),), 2, True)
    ypadded = extended(center, (("role", 2),), 2, False)
    return stencil(center, xpadded, ypadded, flow_rows, shear_rows)


def on_device(velocity, basis, mean_flow, shear):
    ny_loc = velocity.shape[2]
    role_index = lax.axis_index("role")
    flow_rows = lax.dynamic_slice_in_dim(mean_flow, role_index * ny_loc, ny_loc)
    shear_rows = lax.dynamic_slice_in_dim(shear, role_index * ny_loc, ny_loc)
    tend_zero = segmented_tendency(velocity, flow_rows, shear_rows)
    segment_one = velocity + time_step * (8.0 / 15.0) * tend_zero
    tend_one = segmented_tendency(segment_one, flow_rows, shear_rows)
    advanced = segment_one + time_step * (5.0 / 12.0 * tend_one - 17.0 / 60.0 * tend_zero)
    snapshots = jnp.concatenate([segment_one, advanced], axis=0)
    ns = snapshots.shape[0]
    snaps3 = snapshots.reshape(ns, -1, snapshots.shape[3])
    basis3 = basis.reshape(basis.shape[0], -1, basis.shape[3])
    partial_proj = project(basis3, snaps3.astype(jnp.bfloat16))
    coeffs = allreduce(partial_proj, ("role", "slab"))
    coeffs_bf = coeffs.astype(jnp.bfloat16)
    residual3 = residual(coeffs_bf, basis3, snaps3)
    local_gram = jnp.einsum("srz,trz->st", residual3, residual3, precision=lax.Precision.HIGHEST)
    total_gram = allreduce(local_gram, ("role", "slab"))
    lower_factor = jnp.linalg.cholesky(total_gram)
    directions = jax.scipy.linalg.solve_triangular(lower_factor, residual3.reshape(ns, -1), lower=True)
    return (advanced, coeffs, lower_factor.T, directions.reshape(snapshots.shape))


def solution(mesh):
    return jax.shard_map(
        on_device,
        mesh=mesh,
        in_specs=(P(None, "slab", "role", None), P(None, "slab", "role", None), P(), P()),
        out_specs=(P(None, "slab", "role", None), P(), P(), P(None, "slab", "role", None)),
        check_vma=False,
    )
```

```python
import numpy as np
import jax
import jax.numpy as jnp
from jax import lax
from jax.experimental import pallas as pl
from jax.experimental.pallas import tpu as pltpu
from jax.sharding import PartitionSpec as P

viscosity = 0.1
ROWS = 16
time_step = 0.4


def extended(cells, sides, width, closed):
    for axis, dim in sides:
        count = lax.axis_size(axis)
        ends = count if closed else count - 1
        head = lax.slice_in_dim(cells, 0, width, axis=dim)
        tail = lax.slice_in_dim(cells, cells.shape[dim] - width, cells.shape[dim], axis=dim)
        cells = jnp.concatenate(
            [
                lax.ppermute(tail, axis, [(i, (i + 1) % count) for i in range(ends)]),
                cells,
                lax.ppermute(head, axis, [((i + 1) % count, i) for i in range(ends)]),
            ],
            axis=dim,
        )
    return cells


def ring_pairs(size, stride, count, second):
    pairs = []
    for i in range(count):
        digit = (i // stride) % size
        if size == 2 or not second:
            partner = digit ^ 1
        else:
            partner = (digit + 1) % size if digit % 2 else (digit - 1) % size
        pairs.append((i, i + (partner - digit) * stride))
    return pairs


def exchange_rounds(axis, count):
    rounds = []
    stride = 1
    while stride < count:
        size = 4 if count % (stride * 4) == 0 else 2
        rounds.append(ring_pairs(size, stride, count, False))
        if size == 4:
            rounds.append(ring_pairs(size, stride, count, True))
        stride *= size
    return [(axis, pairs) for pairs in rounds]


def allreduce(value, axes):
    sizes = [lax.axis_size(axis) for axis in axes]
    if any(size & (size - 1) for size in sizes):
        return lax.psum(value, axes)
    for axis, size in zip(axes, sizes):
        for name, pairs in exchange_rounds(axis, size):
            value = value + lax.ppermute(value, name, pairs)
    return value


def project_kernel(b_ref, s_ref, o_ref):
    tk, nr, nz = b_ref.shape
    ns = s_ref.shape[0]
    acc = jnp.zeros((tk * ROWS, ns * ROWS), jnp.float32)
    for j in range(nr // ROWS):
        rows = pl.ds(j * ROWS, ROWS)
        lhs = b_ref[:, rows, :].reshape(tk * ROWS, nz)
        rhs = s_ref[:, rows, :].reshape(ns * ROWS, nz)
        acc = acc + lax.dot_general(lhs, rhs, (((1,), (1,)), ((), ())), preferred_element_type=jnp.float32)
    row_t = lax.broadcasted_iota(jnp.int32, acc.shape, 0) % ROWS
    col_t = lax.broadcasted_iota(jnp.int32, acc.shape, 1) % ROWS
    acc = jnp.where(row_t == col_t, acc, 0.0)
    o_ref[...] = jnp.sum(acc.reshape(tk, ROWS, ns * ROWS), axis=1)


def project(basis3, snaps3, tk=32):
    nk, nr, nz = basis3.shape
    ns = snaps3.shape[0]
    out = pl.pallas_call(
        project_kernel,
        grid=(nk // tk,),
        in_specs=[pl.BlockSpec((tk, nr, nz), lambda i: (i, 0, 0)),
                  pl.BlockSpec((ns, nr, nz), lambda i: (0, 0, 0))],
        out_specs=pl.BlockSpec((tk, ns * ROWS), lambda i: (i, 0)),
        out_shape=jax.ShapeDtypeStruct((nk, ns * ROWS), jnp.float32),
        cost_estimate=pl.CostEstimate(flops=2 * nk * nr * nz * ns * ROWS, transcendentals=0,
                                      bytes_accessed=nk * nr * nz * 2 + ns * nr * nz * 2 + nk * ns * ROWS * 4),
    )(basis3, snaps3)
    return jnp.sum(out.reshape(nk, ns, ROWS), axis=2)


def residual_kernel(c_ref, b_ref, s_ref, o_ref, g_ref, spread_ref, acc_ref):
    nk, rows, nz = b_ref.shape
    ns = s_ref.shape[0]
    step = pl.program_id(0)

    @pl.when(step == 0)
    def _():
        col = lax.broadcasted_iota(jnp.int32, (nk, nk * rows), 1)
        row = lax.broadcasted_iota(jnp.int32, (nk, nk * rows), 0)
        expand = jnp.where(col // rows == row, 1.0, 0.0).astype(jnp.bfloat16)
        wide = jnp.dot(c_ref[...], expand, preferred_element_type=jnp.float32)
        tall = jnp.broadcast_to(wide[:, None, :], (ns, rows, nk * rows)).reshape(ns * rows, nk * rows)
        r_t = lax.broadcasted_iota(jnp.int32, tall.shape, 0) % rows
        c_t = lax.broadcasted_iota(jnp.int32, tall.shape, 1) % rows
        spread_ref[...] = jnp.where(r_t == c_t, tall, 0.0).astype(jnp.bfloat16)
        acc_ref[...] = jnp.zeros_like(acc_ref)

    prod = jnp.dot(spread_ref[...], b_ref[...].reshape(nk * rows, nz), preferred_element_type=jnp.float32)
    w = s_ref[...] - prod.reshape(ns, rows, nz)
    o_ref[...] = w
    p = 0
    for a in range(ns):
        for b in range(a, ns):
            term = w[a] * w[b]
            acc_ref[p] += term[: rows // 2] + term[rows // 2:]
            p += 1

    @pl.when(step == pl.num_programs(0) - 1)
    def _():
        g_ref[...] = jnp.sum(acc_ref[...], axis=1)


def residual(coeffs_bf, basis3, snaps3):
    nk, nr, nz = basis3.shape
    ns = snaps3.shape[0]
    pairs = ns * (ns + 1) // 2
    w, g = pl.pallas_call(
        residual_kernel,
        grid=(nr // ROWS,),
        in_specs=[pl.BlockSpec((ns, nk), lambda j: (0, 0)),
                  pl.BlockSpec((nk, ROWS, nz), lambda j: (0, j, 0)),
                  pl.BlockSpec((ns, ROWS, nz), lambda j: (0, j, 0))],
        out_specs=[pl.BlockSpec((ns, ROWS, nz), lambda j: (0, j, 0)),
                   pl.BlockSpec((pairs, nz), lambda j: (0, 0))],
        out_shape=[jax.ShapeDtypeStruct((ns, nr, nz), jnp.float32),
                   jax.ShapeDtypeStruct((pairs, nz), jnp.float32)],
        scratch_shapes=[pltpu.VMEM((ns * ROWS, nk * ROWS), jnp.bfloat16),
                        pltpu.VMEM((pairs, ROWS // 2, nz), jnp.float32)],
        compiler_params=pltpu.CompilerParams(dimension_semantics=("arbitrary",)),
        cost_estimate=pl.CostEstimate(flops=2 * ns * ROWS * nk * ROWS * nz * (nr // ROWS), transcendentals=0,
                                      bytes_accessed=nk * nr * nz * 2 + 2 * ns * nr * nz * 4),
    )(coeffs_bf.T, basis3, snaps3)
    sums = jnp.sum(g, axis=1)
    table = np.zeros((ns, ns), np.int32)
    p = 0
    for a in range(ns):
        for b in range(a, ns):
            table[a, b] = p; table[b, a] = p; p += 1
    gram = sums[jnp.asarray(table)]
    return w, gram


def offset_slice(padded, offset, dimension, length):
    return lax.slice_in_dim(padded, 2 + offset, 2 + offset + length, axis=dimension)


def second_diff(padded, center, dimension, length):
    return (
        -offset_slice(padded, 2, dimension, length)
        + 16.0 * offset_slice(padded, 1, dimension, length)
        - 30.0 * center
        + 16.0 * offset_slice(padded, -1, dimension, length)
        - offset_slice(padded, -2, dimension, length)
    ) / 12.0


def stencil(center, xpadded, ypadded, flow_rows, shear_rows):
    nx_loc = center.shape[1]
    ny_loc = center.shape[2]
    nz_loc = center.shape[3]
    zpadded = jnp.concatenate([center[..., -2:], center, center[..., :2]], axis=3)
    first_x = (
        -offset_slice(xpadded, 2, 1, nx_loc)
        + 8.0 * offset_slice(xpadded, 1, 1, nx_loc)
        - 8.0 * offset_slice(xpadded, -1, 1, nx_loc)
        + offset_slice(xpadded, -2, 1, nx_loc)
    ) / 12.0
    laplace = (
        second_diff(xpadded, center, 1, nx_loc)
        + second_diff(ypadded, center, 2, ny_loc)
        + second_diff(zpadded, center, 3, nz_loc)
    )
    profile = flow_rows[None, None, :, None]
    result = -profile * first_x + viscosity * laplace
    shear_term = shear_rows[None, None, :, None] * center[1:2]
    return jnp.concatenate([result[:1] - shear_term, result[1:]], axis=0)


def segmented_tendency(center, flow_rows, shear_rows):
    xpadded = extended(center, (("slab", 1),), 2, True)
    ypadded = extended(center, (("role", 2),), 2, False)
    return stencil(center, xpadded, ypadded, flow_rows, shear_rows)


def on_device(velocity, basis, mean_flow, shear):
    ny_loc = velocity.shape[2]
    role_index = lax.axis_index("role")
    flow_rows = lax.dynamic_slice_in_dim(mean_flow, role_index * ny_loc, ny_loc)
    shear_rows = lax.dynamic_slice_in_dim(shear, role_index * ny_loc, ny_loc)
    tend_zero = segmented_tendency(velocity, flow_rows, shear_rows)
    segment_one = velocity + time_step * (8.0 / 15.0) * tend_zero
    tend_one = segmented_tendency(segment_one, flow_rows, shear_rows)
    advanced = segment_one + time_step * (5.0 / 12.0 * tend_one - 17.0 / 60.0 * tend_zero)
    snapshots = jnp.concatenate([segment_one, advanced], axis=0)
    ns = snapshots.shape[0]
    snaps3 = snapshots.reshape(ns, -1, snapshots.shape[3])
    basis3 = basis.reshape(basis.shape[0], -1, basis.shape[3])
    partial_proj = project(basis3, snaps3.astype(jnp.bfloat16))
    coeffs = allreduce(partial_proj, ("role", "slab"))
    coeffs_bf = coeffs.astype(jnp.bfloat16)
    residual3, local_gram = residual(coeffs_bf, basis3, snaps3)
    total_gram = allreduce(local_gram, ("role", "slab"))
    lower_factor = jnp.linalg.cholesky(total_gram)
    directions = jax.scipy.linalg.solve_triangular(lower_factor, residual3.reshape(ns, -1), lower=True)
    return (advanced, coeffs, lower_factor.T, directions.reshape(snapshots.shape))


def solution(mesh):
    return jax.shard_map(
        on_device,
        mesh=mesh,
        in_specs=(P(None, "slab", "role", None), P(None, "slab", "role", None), P(), P()),
        out_specs=(P(None, "slab", "role", None), P(), P(), P(None, "slab", "role", None)),
        check_vma=False,
    )
```

```python
import numpy as np
import jax
import jax.numpy as jnp
from jax import lax
from jax.experimental import pallas as pl
from jax.experimental.pallas import tpu as pltpu
from jax.sharding import PartitionSpec as P

viscosity = 0.1
ROWS = 16
time_step = 0.4


def extended(cells, sides, width, closed):
    for axis, dim in sides:
        count = lax.axis_size(axis)
        ends = count if closed else count - 1
        head = lax.slice_in_dim(cells, 0, width, axis=dim)
        tail = lax.slice_in_dim(cells, cells.shape[dim] - width, cells.shape[dim], axis=dim)
        cells = jnp.concatenate(
            [
                lax.ppermute(tail, axis, [(i, (i + 1) % count) for i in range(ends)]),
                cells,
                lax.ppermute(head, axis, [((i + 1) % count, i) for i in range(ends)]),
            ],
            axis=dim,
        )
    return cells


def ring_pairs(size, stride, count, second):
    pairs = []
    for i in range(count):
        digit = (i // stride) % size
        if size == 2 or not second:
            partner = digit ^ 1
        else:
            partner = (digit + 1) % size if digit % 2 else (digit - 1) % size
        pairs.append((i, i + (partner - digit) * stride))
    return pairs


def exchange_rounds(axis, count):
    rounds = []
    stride = 1
    while stride < count:
        size = 4 if count % (stride * 4) == 0 else 2
        rounds.append(ring_pairs(size, stride, count, False))
        if size == 4:
            rounds.append(ring_pairs(size, stride, count, True))
        stride *= size
    return [(axis, pairs) for pairs in rounds]


def allreduce(value, axes):
    sizes = [lax.axis_size(axis) for axis in axes]
    if any(size & (size - 1) for size in sizes):
        return lax.psum(value, axes)
    for axis, size in zip(axes, sizes):
        for name, pairs in exchange_rounds(axis, size):
            value = value + lax.ppermute(value, name, pairs)
    return value


def project_kernel(b_ref, s_ref, o_ref):
    tk, nr, nz = b_ref.shape
    ns = s_ref.shape[0]
    acc = jnp.zeros((tk * ROWS, ns * ROWS), jnp.float32)
    for j in range(nr // ROWS):
        rows = pl.ds(j * ROWS, ROWS)
        lhs = b_ref[:, rows, :].reshape(tk * ROWS, nz)
        rhs = s_ref[:, rows, :].reshape(ns * ROWS, nz)
        acc = acc + lax.dot_general(lhs, rhs, (((1,), (1,)), ((), ())), preferred_element_type=jnp.float32)
    row_t = lax.broadcasted_iota(jnp.int32, acc.shape, 0) % ROWS
    col_t = lax.broadcasted_iota(jnp.int32, acc.shape, 1) % ROWS
    acc = jnp.where(row_t == col_t, acc, 0.0)
    o_ref[...] = jnp.sum(acc.reshape(tk, ROWS, ns * ROWS), axis=1)


def project(basis3, snaps3, tk=64):
    nk, nr, nz = basis3.shape
    ns = snaps3.shape[0]
    out = pl.pallas_call(
        project_kernel,
        grid=(nk // tk,),
        in_specs=[pl.BlockSpec((tk, nr, nz), lambda i: (i, 0, 0)),
                  pl.BlockSpec((ns, nr, nz), lambda i: (0, 0, 0))],
        out_specs=pl.BlockSpec((tk, ns * ROWS), lambda i: (i, 0)),
        out_shape=jax.ShapeDtypeStruct((nk, ns * ROWS), jnp.float32),
        cost_estimate=pl.CostEstimate(flops=2 * nk * nr * nz * ns * ROWS, transcendentals=0,
                                      bytes_accessed=nk * nr * nz * 2 + ns * nr * nz * 2 + nk * ns * ROWS * 4),
    )(basis3, snaps3)
    return jnp.sum(out.reshape(nk, ns, ROWS), axis=2)


def residual_kernel(c_ref, b_ref, s_ref, o_ref, g_ref, spread_ref, acc_ref):
    nk, _, nz = b_ref.shape
    ns = s_ref.shape[0]
    rows = ROWS
    step = pl.program_id(0)

    @pl.when(step == 0)
    def _():
        col = lax.broadcasted_iota(jnp.int32, (nk, nk * rows), 1)
        row = lax.broadcasted_iota(jnp.int32, (nk, nk * rows), 0)
        expand = jnp.where(col // rows == row, 1.0, 0.0).astype(jnp.bfloat16)
        wide = jnp.dot(c_ref[...], expand, preferred_element_type=jnp.float32)
        tall = jnp.broadcast_to(wide[:, None, :], (ns, rows, nk * rows)).reshape(ns * rows, nk * rows)
        r_t = lax.broadcasted_iota(jnp.int32, tall.shape, 0) % rows
        c_t = lax.broadcasted_iota(jnp.int32, tall.shape, 1) % rows
        spread_ref[...] = jnp.where(r_t == c_t, tall, 0.0).astype(jnp.bfloat16)
        acc_ref[...] = jnp.zeros_like(acc_ref)

    for part in range(b_ref.shape[1] // ROWS):
        window = pl.ds(part * ROWS, ROWS)
        block = b_ref[:, window, :].reshape(nk * ROWS, nz)
        prod = jnp.dot(spread_ref[...], block, preferred_element_type=jnp.float32)
        w = s_ref[:, window, :] - prod.reshape(ns, ROWS, nz)
        o_ref[:, window, :] = w
        p = 0
        for a in range(ns):
            for b in range(a, ns):
                term = w[a] * w[b]
                acc_ref[p] += term[: ROWS // 2] + term[ROWS // 2:]
                p += 1

    @pl.when(step == pl.num_programs(0) - 1)
    def _():
        g_ref[...] = jnp.sum(acc_ref[...], axis=1)


def residual(coeffs_bf, basis3, snaps3, block_rows=2 * ROWS):
    nk, nr, nz = basis3.shape
    ns = snaps3.shape[0]
    pairs = ns * (ns + 1) // 2
    w, g = pl.pallas_call(
        residual_kernel,
        grid=(nr // block_rows,),
        in_specs=[pl.BlockSpec((ns, nk), lambda j: (0, 0)),
                  pl.BlockSpec((nk, block_rows, nz), lambda j: (0, j, 0)),
                  pl.BlockSpec((ns, block_rows, nz), lambda j: (0, j, 0))],
        out_specs=[pl.BlockSpec((ns, block_rows, nz), lambda j: (0, j, 0)),
                   pl.BlockSpec((pairs, nz), lambda j: (0, 0))],
        out_shape=[jax.ShapeDtypeStruct((ns, nr, nz), jnp.float32),
                   jax.ShapeDtypeStruct((pairs, nz), jnp.float32)],
        scratch_shapes=[pltpu.VMEM((ns * ROWS, nk * ROWS), jnp.bfloat16),
                        pltpu.VMEM((pairs, ROWS // 2, nz), jnp.float32)],
        compiler_params=pltpu.CompilerParams(dimension_semantics=("arbitrary",)),
        cost_estimate=pl.CostEstimate(flops=2 * ns * ROWS * nk * ROWS * nz * (nr // ROWS), transcendentals=0,
                                      bytes_accessed=nk * nr * nz * 2 + 2 * ns * nr * nz * 4),
    )(coeffs_bf.T, basis3, snaps3)
    sums = jnp.sum(g, axis=1)
    table = np.zeros((ns, ns), np.int32)
    p = 0
    for a in range(ns):
        for b in range(a, ns):
            table[a, b] = p; table[b, a] = p; p += 1
    gram = sums[jnp.asarray(table)]
    return w, gram


def offset_slice(padded, offset, dimension, length):
    return lax.slice_in_dim(padded, 2 + offset, 2 + offset + length, axis=dimension)


def second_diff(padded, center, dimension, length):
    return (
        -offset_slice(padded, 2, dimension, length)
        + 16.0 * offset_slice(padded, 1, dimension, length)
        - 30.0 * center
        + 16.0 * offset_slice(padded, -1, dimension, length)
        - offset_slice(padded, -2, dimension, length)
    ) / 12.0


def stencil(center, xpadded, ypadded, flow_rows, shear_rows):
    nx_loc = center.shape[1]
    ny_loc = center.shape[2]
    nz_loc = center.shape[3]
    zpadded = jnp.concatenate([center[..., -2:], center, center[..., :2]], axis=3)
    first_x = (
        -offset_slice(xpadded, 2, 1, nx_loc)
        + 8.0 * offset_slice(xpadded, 1, 1, nx_loc)
        - 8.0 * offset_slice(xpadded, -1, 1, nx_loc)
        + offset_slice(xpadded, -2, 1, nx_loc)
    ) / 12.0
    laplace = (
        second_diff(xpadded, center, 1, nx_loc)
        + second_diff(ypadded, center, 2, ny_loc)
        + second_diff(zpadded, center, 3, nz_loc)
    )
    profile = flow_rows[None, None, :, None]
    result = -profile * first_x + viscosity * laplace
    shear_term = shear_rows[None, None, :, None] * center[1:2]
    return jnp.concatenate([result[:1] - shear_term, result[1:]], axis=0)


def segmented_tendency(center, flow_rows, shear_rows):
    xpadded = extended(center, (("slab", 1),), 2, True)
    ypadded = extended(center, (("role", 2),), 2, False)
    return stencil(center, xpadded, ypadded, flow_rows, shear_rows)


def on_device(velocity, basis, mean_flow, shear):
    ny_loc = velocity.shape[2]
    role_index = lax.axis_index("role")
    flow_rows = lax.dynamic_slice_in_dim(mean_flow, role_index * ny_loc, ny_loc)
    shear_rows = lax.dynamic_slice_in_dim(shear, role_index * ny_loc, ny_loc)
    tend_zero = segmented_tendency(velocity, flow_rows, shear_rows)
    segment_one = velocity + time_step * (8.0 / 15.0) * tend_zero
    tend_one = segmented_tendency(segment_one, flow_rows, shear_rows)
    advanced = segment_one + time_step * (5.0 / 12.0 * tend_one - 17.0 / 60.0 * tend_zero)
    snapshots = jnp.concatenate([segment_one, advanced], axis=0)
    ns = snapshots.shape[0]
    snaps3 = snapshots.reshape(ns, -1, snapshots.shape[3])
    basis3 = basis.reshape(basis.shape[0], -1, basis.shape[3])
    partial_proj = project(basis3, snaps3.astype(jnp.bfloat16))
    coeffs = allreduce(partial_proj, ("role", "slab"))
    coeffs_bf = coeffs.astype(jnp.bfloat16)
    residual3, local_gram = residual(coeffs_bf, basis3, snaps3)
    total_gram = allreduce(local_gram, ("role", "slab"))
    lower_factor = jnp.linalg.cholesky(total_gram)
    directions = jax.scipy.linalg.solve_triangular(lower_factor, residual3.reshape(ns, -1), lower=True)
    return (advanced, coeffs, lower_factor.T, directions.reshape(snapshots.shape))


def solution(mesh):
    return jax.shard_map(
        on_device,
        mesh=mesh,
        in_specs=(P(None, "slab", "role", None), P(None, "slab", "role", None), P(), P()),
        out_specs=(P(None, "slab", "role", None), P(), P(), P(None, "slab", "role", None)),
        check_vma=False,
    )
```

```python
import numpy as np
import jax
import jax.numpy as jnp
from jax import lax
from jax.experimental import pallas as pl
from jax.experimental.pallas import tpu as pltpu
from jax.sharding import PartitionSpec as P

viscosity = 0.1
ROWS = 16
time_step = 0.4


def extended(cells, sides, width, closed):
    for axis, dim in sides:
        count = lax.axis_size(axis)
        ends = count if closed else count - 1
        head = lax.slice_in_dim(cells, 0, width, axis=dim)
        tail = lax.slice_in_dim(cells, cells.shape[dim] - width, cells.shape[dim], axis=dim)
        if count == 2 and not closed:
            lower_side = lax.axis_index(axis) == 0
            got = lax.ppermute(jnp.where(lower_side, tail, head), axis, [(0, 1), (1, 0)])
            zeros = jnp.zeros_like(got)
            cells = jnp.concatenate(
                [jnp.where(lower_side, zeros, got), cells, jnp.where(lower_side, got, zeros)], axis=dim
            )
            continue
        cells = jnp.concatenate(
            [
                lax.ppermute(tail, axis, [(i, (i + 1) % count) for i in range(ends)]),
                cells,
                lax.ppermute(head, axis, [((i + 1) % count, i) for i in range(ends)]),
            ],
            axis=dim,
        )
    return cells


def ring_pairs(size, stride, count, second):
    pairs = []
    for i in range(count):
        digit = (i // stride) % size
        if size == 2 or not second:
            partner = digit ^ 1
        else:
            partner = (digit + 1) % size if digit % 2 else (digit - 1) % size
        pairs.append((i, i + (partner - digit) * stride))
    return pairs


def exchange_rounds(axis, count):
    rounds = []
    stride = 1
    while stride < count:
        size = 4 if count % (stride * 4) == 0 else 2
        rounds.append(ring_pairs(size, stride, count, False))
        if size == 4:
            rounds.append(ring_pairs(size, stride, count, True))
        stride *= size
    return [(axis, pairs) for pairs in rounds]


def allreduce(value, axes):
    sizes = [lax.axis_size(axis) for axis in axes]
    if any(size & (size - 1) for size in sizes):
        return lax.psum(value, axes)
    for axis, size in zip(axes, sizes):
        for name, pairs in exchange_rounds(axis, size):
            value = value + lax.ppermute(value, name, pairs)
    return value


def project_kernel(b_ref, s_ref, o_ref):
    tk, nr, nz = b_ref.shape
    ns = s_ref.shape[0]
    acc = jnp.zeros((tk * ROWS, ns * ROWS), jnp.float32)
    for j in range(nr // ROWS):
        rows = pl.ds(j * ROWS, ROWS)
        lhs = b_ref[:, rows, :].reshape(tk * ROWS, nz)
        rhs = s_ref[:, rows, :].reshape(ns * ROWS, nz)
        acc = acc + lax.dot_general(lhs, rhs, (((1,), (1,)), ((), ())), preferred_element_type=jnp.float32)
    row_t = lax.broadcasted_iota(jnp.int32, acc.shape, 0) % ROWS
    col_t = lax.broadcasted_iota(jnp.int32, acc.shape, 1) % ROWS
    acc = jnp.where(row_t == col_t, acc, 0.0)
    o_ref[...] = jnp.sum(acc.reshape(tk, ROWS, ns * ROWS), axis=1)


def project(basis3, snaps3, tk=64):
    nk, nr, nz = basis3.shape
    ns = snaps3.shape[0]
    out = pl.pallas_call(
        project_kernel,
        grid=(nk // tk,),
        in_specs=[pl.BlockSpec((tk, nr, nz), lambda i: (i, 0, 0)),
                  pl.BlockSpec((ns, nr, nz), lambda i: (0, 0, 0))],
        out_specs=pl.BlockSpec((tk, ns * ROWS), lambda i: (i, 0)),
        out_shape=jax.ShapeDtypeStruct((nk, ns * ROWS), jnp.float32),
        cost_estimate=pl.CostEstimate(flops=2 * nk * nr * nz * ns * ROWS, transcendentals=0,
                                      bytes_accessed=nk * nr * nz * 2 + ns * nr * nz * 2 + nk * ns * ROWS * 4),
    )(basis3, snaps3)
    return jnp.sum(out.reshape(nk, ns, ROWS), axis=2)


def residual_kernel(c_ref, b_ref, s_ref, o_ref, g_ref, spread_ref, acc_ref):
    nk, _, nz = b_ref.shape
    ns = s_ref.shape[0]
    rows = ROWS
    step = pl.program_id(0)

    @pl.when(step == 0)
    def _():
        col = lax.broadcasted_iota(jnp.int32, (nk, nk * rows), 1)
        row = lax.broadcasted_iota(jnp.int32, (nk, nk * rows), 0)
        expand = jnp.where(col // rows == row, 1.0, 0.0).astype(jnp.bfloat16)
        wide = jnp.dot(c_ref[...], expand, preferred_element_type=jnp.float32)
        tall = jnp.broadcast_to(wide[:, None, :], (ns, rows, nk * rows)).reshape(ns * rows, nk * rows)
        r_t = lax.broadcasted_iota(jnp.int32, tall.shape, 0) % rows
        c_t = lax.broadcasted_iota(jnp.int32, tall.shape, 1) % rows
        spread_ref[...] = jnp.where(r_t == c_t, tall, 0.0).astype(jnp.bfloat16)
        acc_ref[...] = jnp.zeros_like(acc_ref)

    for part in range(b_ref.shape[1] // ROWS):
        window = pl.ds(part * ROWS, ROWS)
        block = b_ref[:, window, :].reshape(nk * ROWS, nz)
        prod = jnp.dot(spread_ref[...], block, preferred_element_type=jnp.float32)
        w = s_ref[:, window, :] - prod.reshape(ns, ROWS, nz)
        o_ref[:, window, :] = w
        p = 0
        for a in range(ns):
            for b in range(a, ns):
                term = w[a] * w[b]
                acc_ref[p] += term[: ROWS // 2] + term[ROWS // 2:]
                p += 1

    @pl.when(step == pl.num_programs(0) - 1)
    def _():
        g_ref[...] = jnp.sum(acc_ref[...], axis=1)


def residual(coeffs_bf, basis3, snaps3, block_rows=2 * ROWS):
    nk, nr, nz = basis3.shape
    ns = snaps3.shape[0]
    pairs = ns * (ns + 1) // 2
    w, g = pl.pallas_call(
        residual_kernel,
        grid=(nr // block_rows,),
        in_specs=[pl.BlockSpec((ns, nk), lambda j: (0, 0)),
                  pl.BlockSpec((nk, block_rows, nz), lambda j: (0, j, 0)),
                  pl.BlockSpec((ns, block_rows, nz), lambda j: (0, j, 0))],
        out_specs=[pl.BlockSpec((ns, block_rows, nz), lambda j: (0, j, 0)),
                   pl.BlockSpec((pairs, nz), lambda j: (0, 0))],
        out_shape=[jax.ShapeDtypeStruct((ns, nr, nz), jnp.float32),
                   jax.ShapeDtypeStruct((pairs, nz), jnp.float32)],
        scratch_shapes=[pltpu.VMEM((ns * ROWS, nk * ROWS), jnp.bfloat16),
                        pltpu.VMEM((pairs, ROWS // 2, nz), jnp.float32)],
        compiler_params=pltpu.CompilerParams(dimension_semantics=("arbitrary",)),
        cost_estimate=pl.CostEstimate(flops=2 * ns * ROWS * nk * ROWS * nz * (nr // ROWS), transcendentals=0,
                                      bytes_accessed=nk * nr * nz * 2 + 2 * ns * nr * nz * 4),
    )(coeffs_bf.T, basis3, snaps3)
    sums = jnp.sum(g, axis=1)
    table = np.zeros((ns, ns), np.int32)
    p = 0
    for a in range(ns):
        for b in range(a, ns):
            table[a, b] = p; table[b, a] = p; p += 1
    gram = sums[jnp.asarray(table)]
    return w, gram


def offset_slice(padded, offset, dimension, length):
    return lax.slice_in_dim(padded, 2 + offset, 2 + offset + length, axis=dimension)


def second_diff(padded, center, dimension, length):
    return (
        -offset_slice(padded, 2, dimension, length)
        + 16.0 * offset_slice(padded, 1, dimension, length)
        - 30.0 * center
        + 16.0 * offset_slice(padded, -1, dimension, length)
        - offset_slice(padded, -2, dimension, length)
    ) / 12.0


def stencil(center, xpadded, ypadded, flow_rows, shear_rows):
    nx_loc = center.shape[1]
    ny_loc = center.shape[2]
    nz_loc = center.shape[3]
    zpadded = jnp.concatenate([center[..., -2:], center, center[..., :2]], axis=3)
    first_x = (
        -offset_slice(xpadded, 2, 1, nx_loc)
        + 8.0 * offset_slice(xpadded, 1, 1, nx_loc)
        - 8.0 * offset_slice(xpadded, -1, 1, nx_loc)
        + offset_slice(xpadded, -2, 1, nx_loc)
    ) / 12.0
    laplace = (
        second_diff(xpadded, center, 1, nx_loc)
        + second_diff(ypadded, center, 2, ny_loc)
        + second_diff(zpadded, center, 3, nz_loc)
    )
    profile = flow_rows[None, None, :, None]
    result = -profile * first_x + viscosity * laplace
    shear_term = shear_rows[None, None, :, None] * center[1:2]
    return jnp.concatenate([result[:1] - shear_term, result[1:]], axis=0)


def segmented_tendency(center, flow_rows, shear_rows):
    xpadded = extended(center, (("slab", 1),), 2, True)
    ypadded = extended(center, (("role", 2),), 2, False)
    return stencil(center, xpadded, ypadded, flow_rows, shear_rows)


def on_device(velocity, basis, mean_flow, shear):
    ny_loc = velocity.shape[2]
    role_index = lax.axis_index("role")
    flow_rows = lax.dynamic_slice_in_dim(mean_flow, role_index * ny_loc, ny_loc)
    shear_rows = lax.dynamic_slice_in_dim(shear, role_index * ny_loc, ny_loc)
    tend_zero = segmented_tendency(velocity, flow_rows, shear_rows)
    segment_one = velocity + time_step * (8.0 / 15.0) * tend_zero
    tend_one = segmented_tendency(segment_one, flow_rows, shear_rows)
    advanced = segment_one + time_step * (5.0 / 12.0 * tend_one - 17.0 / 60.0 * tend_zero)
    snapshots = jnp.concatenate([segment_one, advanced], axis=0)
    ns = snapshots.shape[0]
    snaps3 = snapshots.reshape(ns, -1, snapshots.shape[3])
    basis3 = basis.reshape(basis.shape[0], -1, basis.shape[3])
    partial_proj = project(basis3, snaps3.astype(jnp.bfloat16))
    coeffs = allreduce(partial_proj, ("role", "slab"))
    coeffs_bf = coeffs.astype(jnp.bfloat16)
    residual3, local_gram = residual(coeffs_bf, basis3, snaps3)
    total_gram = allreduce(local_gram, ("role", "slab"))
    lower_factor = jnp.linalg.cholesky(total_gram)
    directions = jax.scipy.linalg.solve_triangular(lower_factor, residual3.reshape(ns, -1), lower=True)
    return (advanced, coeffs, lower_factor.T, directions.reshape(snapshots.shape))


def solution(mesh):
    return jax.shard_map(
        on_device,
        mesh=mesh,
        in_specs=(P(None, "slab", "role", None), P(None, "slab", "role", None), P(), P()),
        out_specs=(P(None, "slab", "role", None), P(), P(), P(None, "slab", "role", None)),
        check_vma=False,
    )
```

```python
import numpy as np
import jax
import jax.numpy as jnp
from jax import lax
from jax.experimental import pallas as pl
from jax.experimental.pallas import tpu as pltpu
from jax.sharding import PartitionSpec as P

viscosity = 0.1
ROWS = 16
time_step = 0.4


def extended(cells, sides, width, closed):
    for axis, dim in sides:
        count = lax.axis_size(axis)
        ends = count if closed else count - 1
        head = lax.slice_in_dim(cells, 0, width, axis=dim)
        tail = lax.slice_in_dim(cells, cells.shape[dim] - width, cells.shape[dim], axis=dim)
        if count == 2 and not closed:
            lower_side = lax.axis_index(axis) == 0
            got = lax.ppermute(jnp.where(lower_side, tail, head), axis, [(0, 1), (1, 0)])
            zeros = jnp.zeros_like(got)
            cells = jnp.concatenate(
                [jnp.where(lower_side, zeros, got), cells, jnp.where(lower_side, got, zeros)], axis=dim
            )
            continue
        cells = jnp.concatenate(
            [
                lax.ppermute(tail, axis, [(i, (i + 1) % count) for i in range(ends)]),
                cells,
                lax.ppermute(head, axis, [((i + 1) % count, i) for i in range(ends)]),
            ],
            axis=dim,
        )
    return cells


def ring_pairs(size, stride, count, second):
    pairs = []
    for i in range(count):
        digit = (i // stride) % size
        if size == 2 or not second:
            partner = digit ^ 1
        else:
            partner = (digit + 1) % size if digit % 2 else (digit - 1) % size
        pairs.append((i, i + (partner - digit) * stride))
    return pairs


def exchange_rounds(axis, count):
    rounds = []
    stride = 1
    while stride < count:
        size = 4 if count % (stride * 4) == 0 else 2
        rounds.append(ring_pairs(size, stride, count, False))
        if size == 4:
            rounds.append(ring_pairs(size, stride, count, True))
        stride *= size
    return [(axis, pairs) for pairs in rounds]


def allreduce(value, axes):
    sizes = [lax.axis_size(axis) for axis in axes]
    if any(size & (size - 1) for size in sizes):
        return lax.psum(value, axes)
    for axis, size in zip(axes, sizes):
        for name, pairs in exchange_rounds(axis, size):
            value = value + lax.ppermute(value, name, pairs)
    return value


def project_kernel(b_ref, s_ref, o_ref):
    tk, nr, nz = b_ref.shape
    ns = s_ref.shape[0]
    acc = jnp.zeros((tk * ROWS, ns * ROWS), jnp.float32)
    for j in range(nr // ROWS):
        rows = pl.ds(j * ROWS, ROWS)
        lhs = b_ref[:, rows, :].reshape(tk * ROWS, nz)
        rhs = s_ref[:, rows, :].reshape(ns * ROWS, nz)
        acc = acc + lax.dot_general(lhs, rhs, (((1,), (1,)), ((), ())), preferred_element_type=jnp.float32)
    row_t = lax.broadcasted_iota(jnp.int32, acc.shape, 0) % ROWS
    col_t = lax.broadcasted_iota(jnp.int32, acc.shape, 1) % ROWS
    acc = jnp.where(row_t == col_t, acc, 0.0)
    o_ref[...] = jnp.sum(acc.reshape(tk, ROWS, ns * ROWS), axis=1)


def project(basis3, snaps3, tk=64):
    nk, nr, nz = basis3.shape
    ns = snaps3.shape[0]
    out = pl.pallas_call(
        project_kernel,
        grid=(nk // tk,),
        in_specs=[pl.BlockSpec((tk, nr, nz), lambda i: (i, 0, 0)),
                  pl.BlockSpec((ns, nr, nz), lambda i: (0, 0, 0))],
        out_specs=pl.BlockSpec((tk, ns * ROWS), lambda i: (i, 0)),
        out_shape=jax.ShapeDtypeStruct((nk, ns * ROWS), jnp.float32),
        cost_estimate=pl.CostEstimate(flops=2 * nk * nr * nz * ns * ROWS, transcendentals=0,
                                      bytes_accessed=nk * nr * nz * 2 + ns * nr * nz * 2 + nk * ns * ROWS * 4),
    )(basis3, snaps3)
    return jnp.sum(out.reshape(nk, ns, ROWS), axis=2)


def residual_kernel(c_ref, b_ref, s_ref, o_ref, g_ref, spread_ref, acc_ref):
    nk, _, nz = b_ref.shape
    ns = s_ref.shape[0]
    rows = ROWS
    step = pl.program_id(0)

    @pl.when(step == 0)
    def _():
        col = lax.broadcasted_iota(jnp.int32, (nk, nk * rows), 1)
        row = lax.broadcasted_iota(jnp.int32, (nk, nk * rows), 0)
        expand = jnp.where(col // rows == row, 1.0, 0.0).astype(jnp.bfloat16)
        wide = jnp.dot(c_ref[...], expand, preferred_element_type=jnp.float32)
        tall = jnp.broadcast_to(wide[:, None, :], (ns, rows, nk * rows)).reshape(ns * rows, nk * rows)
        r_t = lax.broadcasted_iota(jnp.int32, tall.shape, 0) % rows
        c_t = lax.broadcasted_iota(jnp.int32, tall.shape, 1) % rows
        spread_ref[...] = jnp.where(r_t == c_t, tall, 0.0).astype(jnp.bfloat16)
        acc_ref[...] = jnp.zeros_like(acc_ref)

    for part in range(b_ref.shape[1] // ROWS):
        window = pl.ds(part * ROWS, ROWS)
        block = b_ref[:, window, :].reshape(nk * ROWS, nz)
        prod = jnp.dot(spread_ref[...], block, preferred_element_type=jnp.float32)
        w = s_ref[:, window, :] - prod.reshape(ns, ROWS, nz)
        o_ref[:, window, :] = w
        p = 0
        for a in range(ns):
            for b in range(a, ns):
                term = w[a] * w[b]
                acc_ref[p] += term[: ROWS // 2] + term[ROWS // 2:]
                p += 1

    @pl.when(step == pl.num_programs(0) - 1)
    def _():
        g_ref[...] = jnp.sum(acc_ref[...], axis=1)


def residual(coeffs_bf, basis3, snaps3, block_rows=2 * ROWS):
    nk, nr, nz = basis3.shape
    ns = snaps3.shape[0]
    pairs = ns * (ns + 1) // 2
    w, g = pl.pallas_call(
        residual_kernel,
        grid=(nr // block_rows,),
        in_specs=[pl.BlockSpec((ns, nk), lambda j: (0, 0)),
                  pl.BlockSpec((nk, block_rows, nz), lambda j: (0, j, 0)),
                  pl.BlockSpec((ns, block_rows, nz), lambda j: (0, j, 0))],
        out_specs=[pl.BlockSpec((ns, block_rows, nz), lambda j: (0, j, 0)),
                   pl.BlockSpec((pairs, nz), lambda j: (0, 0))],
        out_shape=[jax.ShapeDtypeStruct((ns, nr, nz), jnp.float32),
                   jax.ShapeDtypeStruct((pairs, nz), jnp.float32)],
        scratch_shapes=[pltpu.VMEM((ns * ROWS, nk * ROWS), jnp.bfloat16),
                        pltpu.VMEM((pairs, ROWS // 2, nz), jnp.float32)],
        compiler_params=pltpu.CompilerParams(dimension_semantics=("arbitrary",)),
        cost_estimate=pl.CostEstimate(flops=2 * ns * ROWS * nk * ROWS * nz * (nr // ROWS), transcendentals=0,
                                      bytes_accessed=nk * nr * nz * 2 + 2 * ns * nr * nz * 4),
    )(coeffs_bf.T, basis3, snaps3)
    sums = jnp.sum(g, axis=1)
    table = np.zeros((ns, ns), np.int32)
    p = 0
    for a in range(ns):
        for b in range(a, ns):
            table[a, b] = p; table[b, a] = p; p += 1
    gram = sums[jnp.asarray(table)]
    return w, gram


def offset_slice(padded, offset, dimension, length):
    return lax.slice_in_dim(padded, 2 + offset, 2 + offset + length, axis=dimension)


def second_diff(padded, center, dimension, length):
    return (
        -offset_slice(padded, 2, dimension, length)
        + 16.0 * offset_slice(padded, 1, dimension, length)
        - 30.0 * center
        + 16.0 * offset_slice(padded, -1, dimension, length)
        - offset_slice(padded, -2, dimension, length)
    ) / 12.0


def stencil(center, xpadded, ypadded, flow_rows, shear_rows):
    nx_loc = center.shape[1]
    ny_loc = center.shape[2]
    nz_loc = center.shape[3]
    zpadded = jnp.concatenate([center[..., -2:], center, center[..., :2]], axis=3)
    first_x = (
        -offset_slice(xpadded, 2, 1, nx_loc)
        + 8.0 * offset_slice(xpadded, 1, 1, nx_loc)
        - 8.0 * offset_slice(xpadded, -1, 1, nx_loc)
        + offset_slice(xpadded, -2, 1, nx_loc)
    ) / 12.0
    laplace = (
        second_diff(xpadded, center, 1, nx_loc)
        + second_diff(ypadded, center, 2, ny_loc)
        + second_diff(zpadded, center, 3, nz_loc)
    )
    profile = flow_rows[None, None, :, None]
    result = -profile * first_x + viscosity * laplace
    shear_term = shear_rows[None, None, :, None] * center[1:2]
    return jnp.concatenate([result[:1] - shear_term, result[1:]], axis=0)


def segmented_tendency(center, flow_rows, shear_rows):
    xpadded = extended(center, (("slab", 1),), 2, True)
    ypadded = extended(center, (("role", 2),), 2, False)
    return stencil(center, xpadded, ypadded, flow_rows, shear_rows)


def on_device(velocity, basis, mean_flow, shear):
    ny_loc = velocity.shape[2]
    role_index = lax.axis_index("role")
    flow_rows = lax.dynamic_slice_in_dim(mean_flow, role_index * ny_loc, ny_loc)
    shear_rows = lax.dynamic_slice_in_dim(shear, role_index * ny_loc, ny_loc)
    tend_zero = segmented_tendency(velocity, flow_rows, shear_rows)
    segment_one = velocity + time_step * (8.0 / 15.0) * tend_zero
    tend_one = segmented_tendency(segment_one, flow_rows, shear_rows)
    advanced = segment_one + time_step * (5.0 / 12.0 * tend_one - 17.0 / 60.0 * tend_zero)
    snapshots = jnp.concatenate([segment_one, advanced], axis=0)
    ns = snapshots.shape[0]
    snaps3 = snapshots.reshape(ns, -1, snapshots.shape[3])
    basis3 = basis.reshape(basis.shape[0], -1, basis.shape[3])
    partial_proj = project(basis3, snaps3.astype(jnp.bfloat16))
    coeffs = allreduce(partial_proj, ("role", "slab"))
    coeffs_bf = coeffs.astype(jnp.bfloat16)
    residual3, local_gram = residual(coeffs_bf, basis3, snaps3)
    total_gram = allreduce(local_gram, ("role", "slab"))
    lower_factor = jnp.linalg.cholesky(total_gram)
    inverse_factor = jax.scipy.linalg.solve_triangular(lower_factor, jnp.eye(ns, dtype=jnp.float32), lower=True)
    directions = jnp.sum(inverse_factor[:, :, None, None] * residual3[None], axis=1)
    return (advanced, coeffs, lower_factor.T, directions.reshape(snapshots.shape))


def solution(mesh):
    return jax.shard_map(
        on_device,
        mesh=mesh,
        in_specs=(P(None, "slab", "role", None), P(None, "slab", "role", None), P(), P()),
        out_specs=(P(None, "slab", "role", None), P(), P(), P(None, "slab", "role", None)),
        check_vma=False,
    )
```

```python
import numpy as np
import jax
import jax.numpy as jnp
from jax import lax
from jax.experimental import pallas as pl
from jax.experimental.pallas import tpu as pltpu
from jax.sharding import PartitionSpec as P

viscosity = 0.1
ROWS = 16
time_step = 0.4


def extended(cells, sides, width, closed):
    for axis, dim in sides:
        count = lax.axis_size(axis)
        ends = count if closed else count - 1
        head = lax.slice_in_dim(cells, 0, width, axis=dim)
        tail = lax.slice_in_dim(cells, cells.shape[dim] - width, cells.shape[dim], axis=dim)
        if count == 2 and not closed:
            lower_side = lax.axis_index(axis) == 0
            got = lax.ppermute(jnp.where(lower_side, tail, head), axis, [(0, 1), (1, 0)])
            zeros = jnp.zeros_like(got)
            cells = jnp.concatenate(
                [jnp.where(lower_side, zeros, got), cells, jnp.where(lower_side, got, zeros)], axis=dim
            )
            continue
        cells = jnp.concatenate(
            [
                lax.ppermute(tail, axis, [(i, (i + 1) % count) for i in range(ends)]),
                cells,
                lax.ppermute(head, axis, [((i + 1) % count, i) for i in range(ends)]),
            ],
            axis=dim,
        )
    return cells


def ring_pairs(size, stride, count, second):
    pairs = []
    for i in range(count):
        digit = (i // stride) % size
        if size == 2 or not second:
            partner = digit ^ 1
        else:
            partner = (digit + 1) % size if digit % 2 else (digit - 1) % size
        pairs.append((i, i + (partner - digit) * stride))
    return pairs


def exchange_rounds(axis, count):
    rounds = []
    stride = 1
    while stride < count:
        size = 4 if count % (stride * 4) == 0 else 2
        rounds.append(ring_pairs(size, stride, count, False))
        if size == 4:
            rounds.append(ring_pairs(size, stride, count, True))
        stride *= size
    return [(axis, pairs) for pairs in rounds]


def allreduce(value, axes):
    sizes = [lax.axis_size(axis) for axis in axes]
    if any(size & (size - 1) for size in sizes):
        return lax.psum(value, axes)
    for axis, size in zip(axes, sizes):
        for name, pairs in exchange_rounds(axis, size):
            value = value + lax.ppermute(value, name, pairs)
    return value


def project_kernel(b_ref, s_ref, o_ref):
    tk, nr, nz = b_ref.shape
    ns = s_ref.shape[0]
    acc = jnp.zeros((tk * ROWS, ns * ROWS), jnp.float32)
    for j in range(nr // ROWS):
        rows = pl.ds(j * ROWS, ROWS)
        lhs = b_ref[:, rows, :].reshape(tk * ROWS, nz)
        rhs = s_ref[:, rows, :].reshape(ns * ROWS, nz)
        acc = acc + lax.dot_general(lhs, rhs, (((1,), (1,)), ((), ())), preferred_element_type=jnp.float32)
    row_t = lax.broadcasted_iota(jnp.int32, acc.shape, 0) % ROWS
    col_t = lax.broadcasted_iota(jnp.int32, acc.shape, 1) % ROWS
    acc = jnp.where(row_t == col_t, acc, 0.0)
    o_ref[...] = jnp.sum(acc.reshape(tk, ROWS, ns * ROWS), axis=1)


def project(basis3, snaps3, tk=64):
    nk, nr, nz = basis3.shape
    ns = snaps3.shape[0]
    out = pl.pallas_call(
        project_kernel,
        grid=(nk // tk,),
        in_specs=[pl.BlockSpec((tk, nr, nz), lambda i: (i, 0, 0)),
                  pl.BlockSpec((ns, nr, nz), lambda i: (0, 0, 0))],
        out_specs=pl.BlockSpec((tk, ns * ROWS), lambda i: (i, 0)),
        out_shape=jax.ShapeDtypeStruct((nk, ns * ROWS), jnp.float32),
        cost_estimate=pl.CostEstimate(flops=2 * nk * nr * nz * ns * ROWS, transcendentals=0,
                                      bytes_accessed=nk * nr * nz * 2 + ns * nr * nz * 2 + nk * ns * ROWS * 4),
    )(basis3, snaps3)
    return jnp.sum(out.reshape(nk, ns, ROWS), axis=2)


def residual_kernel(c_ref, b_ref, s_ref, o_ref, g_ref, spread_ref, acc_ref):
    nk, _, nz = b_ref.shape
    ns = s_ref.shape[0]
    rows = ROWS
    step = pl.program_id(0)

    @pl.when(step == 0)
    def _():
        col = lax.broadcasted_iota(jnp.int32, (nk, nk * rows), 1)
        row = lax.broadcasted_iota(jnp.int32, (nk, nk * rows), 0)
        expand = jnp.where(col // rows == row, 1.0, 0.0).astype(jnp.bfloat16)
        wide = jnp.dot(c_ref[...], expand, preferred_element_type=jnp.float32)
        tall = jnp.broadcast_to(wide[:, None, :], (ns, rows, nk * rows)).reshape(ns * rows, nk * rows)
        r_t = lax.broadcasted_iota(jnp.int32, tall.shape, 0) % rows
        c_t = lax.broadcasted_iota(jnp.int32, tall.shape, 1) % rows
        spread_ref[...] = jnp.where(r_t == c_t, tall, 0.0).astype(jnp.bfloat16)
        acc_ref[...] = jnp.zeros_like(acc_ref)

    for part in range(b_ref.shape[1] // ROWS):
        window = pl.ds(part * ROWS, ROWS)
        block = b_ref[:, window, :].reshape(nk * ROWS, nz)
        prod = jnp.dot(spread_ref[...], block, preferred_element_type=jnp.float32)
        w = s_ref[:, window, :] - prod.reshape(ns, ROWS, nz)
        o_ref[:, window, :] = w
        p = 0
        for a in range(ns):
            for b in range(a, ns):
                term = w[a] * w[b]
                acc_ref[p] += term[: ROWS // 2] + term[ROWS // 2:]
                p += 1

    @pl.when(step == pl.num_programs(0) - 1)
    def _():
        g_ref[...] = jnp.sum(acc_ref[...], axis=1)


def residual(coeffs_bf, basis3, snaps3, block_rows=2 * ROWS):
    nk, nr, nz = basis3.shape
    ns = snaps3.shape[0]
    pairs = ns * (ns + 1) // 2
    w, g = pl.pallas_call(
        residual_kernel,
        grid=(nr // block_rows,),
        in_specs=[pl.BlockSpec((ns, nk), lambda j: (0, 0)),
                  pl.BlockSpec((nk, block_rows, nz), lambda j: (0, j, 0)),
                  pl.BlockSpec((ns, block_rows, nz), lambda j: (0, j, 0))],
        out_specs=[pl.BlockSpec((ns, block_rows, nz), lambda j: (0, j, 0)),
                   pl.BlockSpec((pairs, nz), lambda j: (0, 0))],
        out_shape=[jax.ShapeDtypeStruct((ns, nr, nz), jnp.float32),
                   jax.ShapeDtypeStruct((pairs, nz), jnp.float32)],
        scratch_shapes=[pltpu.VMEM((ns * ROWS, nk * ROWS), jnp.bfloat16),
                        pltpu.VMEM((pairs, ROWS // 2, nz), jnp.float32)],
        compiler_params=pltpu.CompilerParams(dimension_semantics=("arbitrary",)),
        cost_estimate=pl.CostEstimate(flops=2 * ns * ROWS * nk * ROWS * nz * (nr // ROWS), transcendentals=0,
                                      bytes_accessed=nk * nr * nz * 2 + 2 * ns * nr * nz * 4),
    )(coeffs_bf.T, basis3, snaps3)
    sums = jnp.sum(g, axis=1)
    table = np.zeros((ns, ns), np.int32)
    p = 0
    for a in range(ns):
        for b in range(a, ns):
            table[a, b] = p; table[b, a] = p; p += 1
    gram = sums[jnp.asarray(table)]
    return w, gram


def offset_slice(padded, offset, dimension, length):
    return lax.slice_in_dim(padded, 2 + offset, 2 + offset + length, axis=dimension)


def second_diff(padded, center, dimension, length):
    return (
        -offset_slice(padded, 2, dimension, length)
        + 16.0 * offset_slice(padded, 1, dimension, length)
        - 30.0 * center
        + 16.0 * offset_slice(padded, -1, dimension, length)
        - offset_slice(padded, -2, dimension, length)
    ) / 12.0


def local_terms(center, ypadded, flow_rows, shear_rows):
    ny_loc = center.shape[2]
    nz_loc = center.shape[3]
    zpadded = jnp.concatenate([center[..., -2:], center, center[..., :2]], axis=3)
    local = viscosity * (second_diff(ypadded, center, 2, ny_loc) + second_diff(zpadded, center, 3, nz_loc))
    shear_term = shear_rows[None, None, :, None] * center[1:2]
    return jnp.concatenate([local[:1] - shear_term, local[1:]], axis=0)


def streamwise_terms(center, xpadded, flow_rows):
    nx_loc = center.shape[1]
    first_x = (
        -offset_slice(xpadded, 2, 1, nx_loc)
        + 8.0 * offset_slice(xpadded, 1, 1, nx_loc)
        - 8.0 * offset_slice(xpadded, -1, 1, nx_loc)
        + offset_slice(xpadded, -2, 1, nx_loc)
    ) / 12.0
    profile = flow_rows[None, None, :, None]
    return -profile * first_x + viscosity * second_diff(xpadded, center, 1, nx_loc)


def segmented_tendency(center, flow_rows, shear_rows):
    xpadded = extended(center, (("slab", 1),), 2, True)
    ypadded = extended(center, (("role", 2),), 2, False)
    local = local_terms(center, ypadded, flow_rows, shear_rows)
    return streamwise_terms(center, xpadded, flow_rows) + local


def on_device(velocity, basis, mean_flow, shear):
    ny_loc = velocity.shape[2]
    role_index = lax.axis_index("role")
    flow_rows = lax.dynamic_slice_in_dim(mean_flow, role_index * ny_loc, ny_loc)
    shear_rows = lax.dynamic_slice_in_dim(shear, role_index * ny_loc, ny_loc)
    tend_zero = segmented_tendency(velocity, flow_rows, shear_rows)
    segment_one = velocity + time_step * (8.0 / 15.0) * tend_zero
    tend_one = segmented_tendency(segment_one, flow_rows, shear_rows)
    advanced = segment_one + time_step * (5.0 / 12.0 * tend_one - 17.0 / 60.0 * tend_zero)
    snapshots = jnp.concatenate([segment_one, advanced], axis=0)
    ns = snapshots.shape[0]
    snaps3 = snapshots.reshape(ns, -1, snapshots.shape[3])
    basis3 = basis.reshape(basis.shape[0], -1, basis.shape[3])
    partial_proj = project(basis3, snaps3.astype(jnp.bfloat16))
    coeffs = allreduce(partial_proj, ("role", "slab"))
    coeffs_bf = coeffs.astype(jnp.bfloat16)
    residual3, local_gram = residual(coeffs_bf, basis3, snaps3)
    total_gram = allreduce(local_gram, ("role", "slab"))
    lower_factor = jnp.linalg.cholesky(total_gram)
    inverse_factor = jax.scipy.linalg.solve_triangular(lower_factor, jnp.eye(ns, dtype=jnp.float32), lower=True)
    directions = jnp.sum(inverse_factor[:, :, None, None] * residual3[None], axis=1)
    return (advanced, coeffs, lower_factor.T, directions.reshape(snapshots.shape))


def solution(mesh):
    return jax.shard_map(
        on_device,
        mesh=mesh,
        in_specs=(P(None, "slab", "role", None), P(None, "slab", "role", None), P(), P()),
        out_specs=(P(None, "slab", "role", None), P(), P(), P(None, "slab", "role", None)),
        check_vma=False,
    )
```

```python
import numpy as np
import jax
import jax.numpy as jnp
from jax import lax
from jax.experimental import pallas as pl
from jax.experimental.pallas import tpu as pltpu
from jax.sharding import PartitionSpec as P

viscosity = 0.1
ROWS = 16
time_step = 0.4


def extended(cells, sides, width, closed):
    for axis, dim in sides:
        count = lax.axis_size(axis)
        ends = count if closed else count - 1
        head = lax.slice_in_dim(cells, 0, width, axis=dim)
        tail = lax.slice_in_dim(cells, cells.shape[dim] - width, cells.shape[dim], axis=dim)
        if count == 2 and not closed:
            lower_side = lax.axis_index(axis) == 0
            got = lax.ppermute(jnp.where(lower_side, tail, head), axis, [(0, 1), (1, 0)])
            zeros = jnp.zeros_like(got)
            cells = jnp.concatenate(
                [jnp.where(lower_side, zeros, got), cells, jnp.where(lower_side, got, zeros)], axis=dim
            )
            continue
        cells = jnp.concatenate(
            [
                lax.ppermute(tail, axis, [(i, (i + 1) % count) for i in range(ends)]),
                cells,
                lax.ppermute(head, axis, [((i + 1) % count, i) for i in range(ends)]),
            ],
            axis=dim,
        )
    return cells


def ring_pairs(size, stride, count, second):
    pairs = []
    for i in range(count):
        digit = (i // stride) % size
        if size == 2 or not second:
            partner = digit ^ 1
        else:
            partner = (digit + 1) % size if digit % 2 else (digit - 1) % size
        pairs.append((i, i + (partner - digit) * stride))
    return pairs


def exchange_rounds(axis, count):
    rounds = []
    stride = 1
    while stride < count:
        size = 4 if count % (stride * 4) == 0 else 2
        rounds.append(ring_pairs(size, stride, count, False))
        if size == 4:
            rounds.append(ring_pairs(size, stride, count, True))
        stride *= size
    return [(axis, pairs) for pairs in rounds]


def allreduce(value, axes):
    sizes = [lax.axis_size(axis) for axis in axes]
    if any(size & (size - 1) for size in sizes):
        return lax.psum(value, axes)
    for axis, size in zip(axes, sizes):
        for name, pairs in exchange_rounds(axis, size):
            value = value + lax.ppermute(value, name, pairs)
    return value


def project_kernel(b_ref, first_ref, second_ref, o_ref):
    tk, nr, nz = b_ref.shape
    ns = first_ref.shape[0] + second_ref.shape[0]
    acc = jnp.zeros((tk * ROWS, ns * ROWS), jnp.float32)
    for j in range(nr // ROWS):
        rows = pl.ds(j * ROWS, ROWS)
        lhs = b_ref[:, rows, :].reshape(tk * ROWS, nz)
        both = jnp.concatenate([first_ref[:, rows, :], second_ref[:, rows, :]], axis=0)
        rhs = both.astype(jnp.bfloat16).reshape(ns * ROWS, nz)
        acc = acc + lax.dot_general(lhs, rhs, (((1,), (1,)), ((), ())), preferred_element_type=jnp.float32)
    row_t = lax.broadcasted_iota(jnp.int32, acc.shape, 0) % ROWS
    col_t = lax.broadcasted_iota(jnp.int32, acc.shape, 1) % ROWS
    acc = jnp.where(row_t == col_t, acc, 0.0)
    lanes = jnp.sum(acc.reshape(tk, ROWS, ns * ROWS), axis=1)
    group = lax.broadcasted_iota(jnp.int32, (ns * ROWS, ns), 0) // ROWS
    column = lax.broadcasted_iota(jnp.int32, (ns * ROWS, ns), 1)
    gather = jnp.where(group == column, 1.0, 0.0)
    o_ref[...] = jnp.dot(lanes, gather, precision=lax.Precision.HIGHEST, preferred_element_type=jnp.float32)


def project(basis3, first3, second3, tk=64):
    nk, nr, nz = basis3.shape
    ns = first3.shape[0] + second3.shape[0]
    return pl.pallas_call(
        project_kernel,
        grid=(nk // tk,),
        in_specs=[pl.BlockSpec((tk, nr, nz), lambda i: (i, 0, 0)),
                  pl.BlockSpec(first3.shape, lambda i: (0, 0, 0)),
                  pl.BlockSpec(second3.shape, lambda i: (0, 0, 0))],
        out_specs=pl.BlockSpec((tk, ns), lambda i: (i, 0)),
        out_shape=jax.ShapeDtypeStruct((nk, ns), jnp.float32),
        cost_estimate=pl.CostEstimate(flops=2 * nk * nr * nz * ns * ROWS, transcendentals=0,
                                      bytes_accessed=nk * nr * nz * 2 + ns * nr * nz * 4 + nk * ns * 4),
    )(basis3, first3, second3)


def directions_kernel(l_ref, w_ref, o_ref):
    ns = w_ref.shape[0]
    for s in range(ns):
        acc = l_ref[s, 0] * w_ref[0]
        for t in range(1, s + 1):
            acc = acc + l_ref[s, t] * w_ref[t]
        o_ref[s] = acc


def apply_inverse(inverse_factor, residual3, block_rows=2 * ROWS):
    ns, nr, nz = residual3.shape
    return pl.pallas_call(
        directions_kernel,
        grid=(nr // block_rows,),
        in_specs=[pl.BlockSpec(memory_space=pltpu.SMEM),
                  pl.BlockSpec((ns, block_rows, nz), lambda j: (0, j, 0))],
        out_specs=pl.BlockSpec((ns, block_rows, nz), lambda j: (0, j, 0)),
        out_shape=jax.ShapeDtypeStruct(residual3.shape, jnp.float32),
        cost_estimate=pl.CostEstimate(flops=ns * ns * nr * nz, transcendentals=0, bytes_accessed=2 * ns * nr * nz * 4),
    )(inverse_factor, residual3)


def residual_kernel(c_ref, b_ref, s_ref, o_ref, g_ref, spread_ref, acc_ref):
    nk, _, nz = b_ref.shape
    ns = s_ref.shape[0]
    rows = ROWS
    step = pl.program_id(0)

    @pl.when(step == 0)
    def _():
        col = lax.broadcasted_iota(jnp.int32, (nk, nk * rows), 1)
        row = lax.broadcasted_iota(jnp.int32, (nk, nk * rows), 0)
        expand = jnp.where(col // rows == row, 1.0, 0.0).astype(jnp.bfloat16)
        wide = jnp.dot(c_ref[...], expand, preferred_element_type=jnp.float32)
        tall = jnp.broadcast_to(wide[:, None, :], (ns, rows, nk * rows)).reshape(ns * rows, nk * rows)
        r_t = lax.broadcasted_iota(jnp.int32, tall.shape, 0) % rows
        c_t = lax.broadcasted_iota(jnp.int32, tall.shape, 1) % rows
        spread_ref[...] = jnp.where(r_t == c_t, tall, 0.0).astype(jnp.bfloat16)
        acc_ref[...] = jnp.zeros_like(acc_ref)

    for part in range(b_ref.shape[1] // ROWS):
        window = pl.ds(part * ROWS, ROWS)
        block = b_ref[:, window, :].reshape(nk * ROWS, nz)
        prod = jnp.dot(spread_ref[...], block, preferred_element_type=jnp.float32)
        w = s_ref[:, window, :] - prod.reshape(ns, ROWS, nz)
        o_ref[:, window, :] = w
        p = 0
        for a in range(ns):
            for b in range(a, ns):
                term = w[a] * w[b]
                acc_ref[p] += term[: ROWS // 2] + term[ROWS // 2:]
                p += 1

    @pl.when(step == pl.num_programs(0) - 1)
    def _():
        g_ref[...] = jnp.sum(acc_ref[...], axis=1)


def residual(coeffs_bf, basis3, snaps3, block_rows=2 * ROWS):
    nk, nr, nz = basis3.shape
    ns = snaps3.shape[0]
    pairs = ns * (ns + 1) // 2
    w, g = pl.pallas_call(
        residual_kernel,
        grid=(nr // block_rows,),
        in_specs=[pl.BlockSpec((ns, nk), lambda j: (0, 0)),
                  pl.BlockSpec((nk, block_rows, nz), lambda j: (0, j, 0)),
                  pl.BlockSpec((ns, block_rows, nz), lambda j: (0, j, 0))],
        out_specs=[pl.BlockSpec((ns, block_rows, nz), lambda j: (0, j, 0)),
                   pl.BlockSpec((pairs, nz), lambda j: (0, 0))],
        out_shape=[jax.ShapeDtypeStruct((ns, nr, nz), jnp.float32),
                   jax.ShapeDtypeStruct((pairs, nz), jnp.float32)],
        scratch_shapes=[pltpu.VMEM((ns * ROWS, nk * ROWS), jnp.bfloat16),
                        pltpu.VMEM((pairs, ROWS // 2, nz), jnp.float32)],
        compiler_params=pltpu.CompilerParams(dimension_semantics=("arbitrary",)),
        cost_estimate=pl.CostEstimate(flops=2 * ns * ROWS * nk * ROWS * nz * (nr // ROWS), transcendentals=0,
                                      bytes_accessed=nk * nr * nz * 2 + 2 * ns * nr * nz * 4),
    )(coeffs_bf.T, basis3, snaps3)
    sums = jnp.sum(g, axis=1)
    table = np.zeros((ns, ns), np.int32)
    p = 0
    for a in range(ns):
        for b in range(a, ns):
            table[a, b] = p; table[b, a] = p; p += 1
    gram = sums[jnp.asarray(table)]
    return w, gram


def offset_slice(padded, offset, dimension, length):
    return lax.slice_in_dim(padded, 2 + offset, 2 + offset + length, axis=dimension)


def second_diff(padded, center, dimension, length):
    return (
        -offset_slice(padded, 2, dimension, length)
        + 16.0 * offset_slice(padded, 1, dimension, length)
        - 30.0 * center
        + 16.0 * offset_slice(padded, -1, dimension, length)
        - offset_slice(padded, -2, dimension, length)
    ) / 12.0


def local_terms(center, ypadded, flow_rows, shear_rows):
    ny_loc = center.shape[2]
    nz_loc = center.shape[3]
    zpadded = jnp.concatenate([center[..., -2:], center, center[..., :2]], axis=3)
    local = viscosity * (second_diff(ypadded, center, 2, ny_loc) + second_diff(zpadded, center, 3, nz_loc))
    shear_term = shear_rows[None, None, :, None] * center[1:2]
    return jnp.concatenate([local[:1] - shear_term, local[1:]], axis=0)


def streamwise_terms(center, xpadded, flow_rows):
    nx_loc = center.shape[1]
    first_x = (
        -offset_slice(xpadded, 2, 1, nx_loc)
        + 8.0 * offset_slice(xpadded, 1, 1, nx_loc)
        - 8.0 * offset_slice(xpadded, -1, 1, nx_loc)
        + offset_slice(xpadded, -2, 1, nx_loc)
    ) / 12.0
    profile = flow_rows[None, None, :, None]
    return -profile * first_x + viscosity * second_diff(xpadded, center, 1, nx_loc)


def segmented_tendency(center, flow_rows, shear_rows):
    xpadded = extended(center, (("slab", 1),), 2, True)
    ypadded = extended(center, (("role", 2),), 2, False)
    local = local_terms(center, ypadded, flow_rows, shear_rows)
    return streamwise_terms(center, xpadded, flow_rows) + local


def on_device(velocity, basis, mean_flow, shear):
    ny_loc = velocity.shape[2]
    role_index = lax.axis_index("role")
    flow_rows = lax.dynamic_slice_in_dim(mean_flow, role_index * ny_loc, ny_loc)
    shear_rows = lax.dynamic_slice_in_dim(shear, role_index * ny_loc, ny_loc)
    tend_zero = segmented_tendency(velocity, flow_rows, shear_rows)
    segment_one = velocity + time_step * (8.0 / 15.0) * tend_zero
    tend_one = segmented_tendency(segment_one, flow_rows, shear_rows)
    advanced = segment_one + time_step * (5.0 / 12.0 * tend_one - 17.0 / 60.0 * tend_zero)
    snapshots = jnp.concatenate([segment_one, advanced], axis=0)
    ns = snapshots.shape[0]
    snaps3 = snapshots.reshape(ns, -1, snapshots.shape[3])
    basis3 = basis.reshape(basis.shape[0], -1, basis.shape[3])
    first3 = segment_one.reshape(segment_one.shape[0], -1, segment_one.shape[3])
    second3 = advanced.reshape(advanced.shape[0], -1, advanced.shape[3])
    partial_proj = project(basis3, first3, second3)
    coeffs = allreduce(partial_proj, ("role", "slab"))
    coeffs_bf = coeffs.astype(jnp.bfloat16)
    residual3, local_gram = residual(coeffs_bf, basis3, snaps3)
    total_gram = allreduce(local_gram, ("role", "slab"))
    lower_factor = jnp.linalg.cholesky(total_gram)
    inverse_factor = jax.scipy.linalg.solve_triangular(lower_factor, jnp.eye(ns, dtype=jnp.float32), lower=True)
    directions = apply_inverse(inverse_factor, residual3)
    return (advanced, coeffs, lower_factor.T, directions.reshape(snapshots.shape))


def solution(mesh):
    return jax.shard_map(
        on_device,
        mesh=mesh,
        in_specs=(P(None, "slab", "role", None), P(None, "slab", "role", None), P(), P()),
        out_specs=(P(None, "slab", "role", None), P(), P(), P(None, "slab", "role", None)),
        check_vma=False,
    )
```

```python
import numpy as np
import jax
import jax.numpy as jnp
from jax import lax
from jax.experimental import pallas as pl
from jax.experimental.pallas import tpu as pltpu
from jax.sharding import PartitionSpec as P

viscosity = 0.1
ROWS = 16
time_step = 0.4


def extended(cells, sides, width, closed):
    for axis, dim in sides:
        count = lax.axis_size(axis)
        ends = count if closed else count - 1
        head = lax.slice_in_dim(cells, 0, width, axis=dim)
        tail = lax.slice_in_dim(cells, cells.shape[dim] - width, cells.shape[dim], axis=dim)
        if count == 2 and not closed:
            lower_side = lax.axis_index(axis) == 0
            got = lax.ppermute(jnp.where(lower_side, tail, head), axis, [(0, 1), (1, 0)])
            zeros = jnp.zeros_like(got)
            cells = jnp.concatenate(
                [jnp.where(lower_side, zeros, got), cells, jnp.where(lower_side, got, zeros)], axis=dim
            )
            continue
        cells = jnp.concatenate(
            [
                lax.ppermute(tail, axis, [(i, (i + 1) % count) for i in range(ends)]),
                cells,
                lax.ppermute(head, axis, [((i + 1) % count, i) for i in range(ends)]),
            ],
            axis=dim,
        )
    return cells


def ring_pairs(size, stride, count, second):
    pairs = []
    for i in range(count):
        digit = (i // stride) % size
        if size == 2 or not second:
            partner = digit ^ 1
        else:
            partner = (digit + 1) % size if digit % 2 else (digit - 1) % size
        pairs.append((i, i + (partner - digit) * stride))
    return pairs


def exchange_rounds(axis, count):
    rounds = []
    stride = 1
    while stride < count:
        size = 4 if count % (stride * 4) == 0 else 2
        rounds.append(ring_pairs(size, stride, count, False))
        if size == 4:
            rounds.append(ring_pairs(size, stride, count, True))
        stride *= size
    return [(axis, pairs) for pairs in rounds]


def allreduce(value, axes):
    sizes = [lax.axis_size(axis) for axis in axes]
    if any(size & (size - 1) for size in sizes):
        return lax.psum(value, axes)
    for axis, size in zip(axes, sizes):
        for name, pairs in exchange_rounds(axis, size):
            value = value + lax.ppermute(value, name, pairs)
    return value


def project_kernel(b_ref, s_ref, o_ref):
    tk, nr, nz = b_ref.shape
    ns = s_ref.shape[0]
    acc = jnp.zeros((tk * ROWS, ns * ROWS), jnp.float32)
    for j in range(nr // ROWS):
        rows = pl.ds(j * ROWS, ROWS)
        lhs = b_ref[:, rows, :].reshape(tk * ROWS, nz)
        rhs = s_ref[:, rows, :].reshape(ns * ROWS, nz)
        acc = acc + lax.dot_general(lhs, rhs, (((1,), (1,)), ((), ())), preferred_element_type=jnp.float32)
    row_t = lax.broadcasted_iota(jnp.int32, acc.shape, 0) % ROWS
    col_t = lax.broadcasted_iota(jnp.int32, acc.shape, 1) % ROWS
    acc = jnp.where(row_t == col_t, acc, 0.0)
    lanes = jnp.sum(acc.reshape(tk, ROWS, ns * ROWS), axis=1)
    group = lax.broadcasted_iota(jnp.int32, (ns, ns * ROWS), 1) // ROWS
    snapshot = lax.broadcasted_iota(jnp.int32, (ns, ns * ROWS), 0)
    gather = jnp.where(group == snapshot, 1.0, 0.0)
    o_ref[...] = lax.dot_general(gather, lanes, (((1,), (1,)), ((), ())),
                                 precision=lax.Precision.HIGHEST, preferred_element_type=jnp.float32)


def project(basis3, snaps3, tk=128):
    nk, nr, nz = basis3.shape
    ns = snaps3.shape[0]
    return pl.pallas_call(
        project_kernel,
        grid=(nk // tk,),
        in_specs=[pl.BlockSpec((tk, nr, nz), lambda i: (i, 0, 0)),
                  pl.BlockSpec((ns, nr, nz), lambda i: (0, 0, 0))],
        out_specs=pl.BlockSpec((ns, tk), lambda i: (0, i)),
        out_shape=jax.ShapeDtypeStruct((ns, nk), jnp.float32),
        cost_estimate=pl.CostEstimate(flops=2 * nk * nr * nz * ns * ROWS, transcendentals=0,
                                      bytes_accessed=nk * nr * nz * 2 + ns * nr * nz * 2 + nk * ns * 4),
    )(basis3, snaps3)


def residual_kernel(c_ref, b_ref, s_ref, o_ref, g_ref, spread_ref, acc_ref):
    nk, _, nz = b_ref.shape
    ns = s_ref.shape[0]
    rows = ROWS
    step = pl.program_id(0)

    @pl.when(step == 0)
    def _():
        col = lax.broadcasted_iota(jnp.int32, (nk, nk * rows), 1)
        row = lax.broadcasted_iota(jnp.int32, (nk, nk * rows), 0)
        expand = jnp.where(col // rows == row, 1.0, 0.0).astype(jnp.bfloat16)
        wide = jnp.dot(c_ref[...].astype(jnp.bfloat16), expand, preferred_element_type=jnp.float32)
        tall = jnp.broadcast_to(wide[:, None, :], (ns, rows, nk * rows)).reshape(ns * rows, nk * rows)
        r_t = lax.broadcasted_iota(jnp.int32, tall.shape, 0) % rows
        c_t = lax.broadcasted_iota(jnp.int32, tall.shape, 1) % rows
        spread_ref[...] = jnp.where(r_t == c_t, tall, 0.0).astype(jnp.bfloat16)
        acc_ref[...] = jnp.zeros_like(acc_ref)

    for part in range(b_ref.shape[1] // ROWS):
        window = pl.ds(part * ROWS, ROWS)
        block = b_ref[:, window, :].reshape(nk * ROWS, nz)
        prod = jnp.dot(spread_ref[...], block, preferred_element_type=jnp.float32)
        w = s_ref[:, window, :] - prod.reshape(ns, ROWS, nz)
        o_ref[:, window, :] = w
        p = 0
        for a in range(ns):
            for b in range(a, ns):
                term = w[a] * w[b]
                acc_ref[p] += term[: ROWS // 2] + term[ROWS // 2:]
                p += 1

    @pl.when(step == pl.num_programs(0) - 1)
    def _():
        g_ref[...] = jnp.sum(acc_ref[...], axis=1)


def residual(coeffs_t, basis3, snaps3, block_rows=2 * ROWS):
    nk, nr, nz = basis3.shape
    ns = snaps3.shape[0]
    pairs = ns * (ns + 1) // 2
    w, g = pl.pallas_call(
        residual_kernel,
        grid=(nr // block_rows,),
        in_specs=[pl.BlockSpec((ns, nk), lambda j: (0, 0)),
                  pl.BlockSpec((nk, block_rows, nz), lambda j: (0, j, 0)),
                  pl.BlockSpec((ns, block_rows, nz), lambda j: (0, j, 0))],
        out_specs=[pl.BlockSpec((ns, block_rows, nz), lambda j: (0, j, 0)),
                   pl.BlockSpec((pairs, nz), lambda j: (0, 0))],
        out_shape=[jax.ShapeDtypeStruct((ns, nr, nz), jnp.float32),
                   jax.ShapeDtypeStruct((pairs, nz), jnp.float32)],
        scratch_shapes=[pltpu.VMEM((ns * ROWS, nk * ROWS), jnp.bfloat16),
                        pltpu.VMEM((pairs, ROWS // 2, nz), jnp.float32)],
        compiler_params=pltpu.CompilerParams(dimension_semantics=("arbitrary",)),
        cost_estimate=pl.CostEstimate(flops=2 * ns * ROWS * nk * ROWS * nz * (nr // ROWS), transcendentals=0,
                                      bytes_accessed=nk * nr * nz * 2 + 2 * ns * nr * nz * 4),
    )(coeffs_t, basis3, snaps3)
    sums = jnp.sum(g, axis=1)
    table = np.zeros((ns, ns), np.int32)
    p = 0
    for a in range(ns):
        for b in range(a, ns):
            table[a, b] = p; table[b, a] = p; p += 1
    gram = sums[jnp.asarray(table)]
    return w, gram


def offset_slice(padded, offset, dimension, length):
    return lax.slice_in_dim(padded, 2 + offset, 2 + offset + length, axis=dimension)


def second_diff(padded, center, dimension, length):
    return (
        -offset_slice(padded, 2, dimension, length)
        + 16.0 * offset_slice(padded, 1, dimension, length)
        - 30.0 * center
        + 16.0 * offset_slice(padded, -1, dimension, length)
        - offset_slice(padded, -2, dimension, length)
    ) / 12.0


def local_terms(center, ypadded, flow_rows, shear_rows):
    ny_loc = center.shape[2]
    nz_loc = center.shape[3]
    zpadded = jnp.concatenate([center[..., -2:], center, center[..., :2]], axis=3)
    local = viscosity * (second_diff(ypadded, center, 2, ny_loc) + second_diff(zpadded, center, 3, nz_loc))
    shear_term = shear_rows[None, None, :, None] * center[1:2]
    return jnp.concatenate([local[:1] - shear_term, local[1:]], axis=0)


def streamwise_terms(center, xpadded, flow_rows):
    nx_loc = center.shape[1]
    first_x = (
        -offset_slice(xpadded, 2, 1, nx_loc)
        + 8.0 * offset_slice(xpadded, 1, 1, nx_loc)
        - 8.0 * offset_slice(xpadded, -1, 1, nx_loc)
        + offset_slice(xpadded, -2, 1, nx_loc)
    ) / 12.0
    profile = flow_rows[None, None, :, None]
    return -profile * first_x + viscosity * second_diff(xpadded, center, 1, nx_loc)


def segmented_tendency(center, flow_rows, shear_rows):
    xpadded = extended(center, (("slab", 1),), 2, True)
    ypadded = extended(center, (("role", 2),), 2, False)
    local = local_terms(center, ypadded, flow_rows, shear_rows)
    return streamwise_terms(center, xpadded, flow_rows) + local


def on_device(velocity, basis, mean_flow, shear):
    ny_loc = velocity.shape[2]
    role_index = lax.axis_index("role")
    flow_rows = lax.dynamic_slice_in_dim(mean_flow, role_index * ny_loc, ny_loc)
    shear_rows = lax.dynamic_slice_in_dim(shear, role_index * ny_loc, ny_loc)
    tend_zero = segmented_tendency(velocity, flow_rows, shear_rows)
    segment_one = velocity + time_step * (8.0 / 15.0) * tend_zero
    tend_one = segmented_tendency(segment_one, flow_rows, shear_rows)
    advanced = segment_one + time_step * (5.0 / 12.0 * tend_one - 17.0 / 60.0 * tend_zero)
    snapshots = jnp.concatenate([segment_one, advanced], axis=0)
    ns = snapshots.shape[0]
    snaps3 = snapshots.reshape(ns, -1, snapshots.shape[3])
    basis3 = basis.reshape(basis.shape[0], -1, basis.shape[3])
    partial_proj = project(basis3, snaps3.astype(jnp.bfloat16))
    coeffs_t = allreduce(partial_proj, ("role", "slab"))
    coeffs = coeffs_t.T
    residual3, local_gram = residual(coeffs_t, basis3, snaps3)
    total_gram = allreduce(local_gram, ("role", "slab"))
    lower_factor = jnp.linalg.cholesky(total_gram)
    inverse_factor = jax.scipy.linalg.solve_triangular(lower_factor, jnp.eye(ns, dtype=jnp.float32), lower=True)
    directions = jnp.sum(inverse_factor[:, :, None, None] * residual3[None], axis=1)
    return (advanced, coeffs, lower_factor.T, directions.reshape(snapshots.shape))


def solution(mesh):
    return jax.shard_map(
        on_device,
        mesh=mesh,
        in_specs=(P(None, "slab", "role", None), P(None, "slab", "role", None), P(), P()),
        out_specs=(P(None, "slab", "role", None), P(), P(), P(None, "slab", "role", None)),
        check_vma=False,
    )
```

```python
import numpy as np
import jax
import jax.numpy as jnp
from jax import lax
from jax.experimental import pallas as pl
from jax.experimental.pallas import tpu as pltpu
from jax.sharding import PartitionSpec as P

viscosity = 0.1
ROWS = 16
time_step = 0.4


def extended(cells, sides, width, closed):
    for axis, dim in sides:
        count = lax.axis_size(axis)
        ends = count if closed else count - 1
        head = lax.slice_in_dim(cells, 0, width, axis=dim)
        tail = lax.slice_in_dim(cells, cells.shape[dim] - width, cells.shape[dim], axis=dim)
        if count == 2 and not closed:
            lower_side = lax.axis_index(axis) == 0
            got = lax.ppermute(jnp.where(lower_side, tail, head), axis, [(0, 1), (1, 0)])
            zeros = jnp.zeros_like(got)
            cells = jnp.concatenate(
                [jnp.where(lower_side, zeros, got), cells, jnp.where(lower_side, got, zeros)], axis=dim
            )
            continue
        cells = jnp.concatenate(
            [
                lax.ppermute(tail, axis, [(i, (i + 1) % count) for i in range(ends)]),
                cells,
                lax.ppermute(head, axis, [((i + 1) % count, i) for i in range(ends)]),
            ],
            axis=dim,
        )
    return cells


def ring_pairs(size, stride, count, second):
    pairs = []
    for i in range(count):
        digit = (i // stride) % size
        if size == 2 or not second:
            partner = digit ^ 1
        else:
            partner = (digit + 1) % size if digit % 2 else (digit - 1) % size
        pairs.append((i, i + (partner - digit) * stride))
    return pairs


def exchange_rounds(axis, count):
    rounds = []
    stride = 1
    while stride < count:
        size = 4 if count % (stride * 4) == 0 else 2
        rounds.append(ring_pairs(size, stride, count, False))
        if size == 4:
            rounds.append(ring_pairs(size, stride, count, True))
        stride *= size
    return [(axis, pairs) for pairs in rounds]


def allreduce(value, axes):
    sizes = [lax.axis_size(axis) for axis in axes]
    if any(size & (size - 1) for size in sizes):
        return lax.psum(value, axes)
    for axis, size in zip(axes, sizes):
        for name, pairs in exchange_rounds(axis, size):
            value = value + lax.ppermute(value, name, pairs)
    return value


def project_kernel(b_ref, s_ref, o_ref):
    tk, nr, nz = b_ref.shape
    ns = s_ref.shape[0]
    acc = jnp.zeros((tk * ROWS, ns * ROWS), jnp.float32)
    for j in range(nr // ROWS):
        rows = pl.ds(j * ROWS, ROWS)
        lhs = b_ref[:, rows, :].reshape(tk * ROWS, nz)
        rhs = s_ref[:, rows, :].reshape(ns * ROWS, nz)
        acc = acc + lax.dot_general(lhs, rhs, (((1,), (1,)), ((), ())), preferred_element_type=jnp.float32)
    row_t = lax.broadcasted_iota(jnp.int32, acc.shape, 0) % ROWS
    col_t = lax.broadcasted_iota(jnp.int32, acc.shape, 1) % ROWS
    acc = jnp.where(row_t == col_t, acc, 0.0)
    lanes = jnp.sum(acc.reshape(tk, ROWS, ns * ROWS), axis=1)
    group = lax.broadcasted_iota(jnp.int32, (ns, ns * ROWS), 1) // ROWS
    snapshot = lax.broadcasted_iota(jnp.int32, (ns, ns * ROWS), 0)
    gather = jnp.where(group == snapshot, 1.0, 0.0)
    o_ref[...] = lax.dot_general(gather, lanes, (((1,), (1,)), ((), ())),
                                 precision=lax.Precision.HIGHEST, preferred_element_type=jnp.float32)


def project(basis3, snaps3, tk=128):
    nk, nr, nz = basis3.shape
    ns = snaps3.shape[0]
    return pl.pallas_call(
        project_kernel,
        grid=(nk // tk,),
        in_specs=[pl.BlockSpec((tk, nr, nz), lambda i: (i, 0, 0)),
                  pl.BlockSpec((ns, nr, nz), lambda i: (0, 0, 0))],
        out_specs=pl.BlockSpec((ns, tk), lambda i: (0, i)),
        out_shape=jax.ShapeDtypeStruct((ns, nk), jnp.float32),
        cost_estimate=pl.CostEstimate(flops=2 * nk * nr * nz * ns * ROWS, transcendentals=0,
                                      bytes_accessed=nk * nr * nz * 2 + ns * nr * nz * 2 + nk * ns * 4),
    )(basis3, snaps3)


def residual_kernel(c_ref, b_ref, s_ref, o_ref, g_ref, spread_ref, acc_ref):
    nk, _, nz = b_ref.shape
    ns = s_ref.shape[0]
    rows = ROWS
    step = pl.program_id(0)

    @pl.when(step == 0)
    def _():
        col = lax.broadcasted_iota(jnp.int32, (nk, nk * rows), 1)
        row = lax.broadcasted_iota(jnp.int32, (nk, nk * rows), 0)
        expand = jnp.where(col // rows == row, 1.0, 0.0).astype(jnp.bfloat16)
        wide = jnp.dot(c_ref[...].astype(jnp.bfloat16), expand, preferred_element_type=jnp.float32)
        tall = jnp.broadcast_to(wide[:, None, :], (ns, rows, nk * rows)).reshape(ns * rows, nk * rows)
        r_t = lax.broadcasted_iota(jnp.int32, tall.shape, 0) % rows
        c_t = lax.broadcasted_iota(jnp.int32, tall.shape, 1) % rows
        spread_ref[...] = jnp.where(r_t == c_t, tall, 0.0).astype(jnp.bfloat16)
        acc_ref[...] = jnp.zeros_like(acc_ref)

    for part in range(b_ref.shape[1] // ROWS):
        window = pl.ds(part * ROWS, ROWS)
        block = b_ref[:, window, :].reshape(nk * ROWS, nz)
        prod = jnp.dot(spread_ref[...], block, preferred_element_type=jnp.float32)
        w = s_ref[:, window, :] - prod.reshape(ns, ROWS, nz)
        o_ref[:, window, :] = w
        p = 0
        for a in range(ns):
            for b in range(a, ns):
                term = w[a] * w[b]
                acc_ref[p] += term[: ROWS // 2] + term[ROWS // 2:]
                p += 1

    @pl.when(step == pl.num_programs(0) - 1)
    def _():
        row = lax.broadcasted_iota(jnp.int32, (ns, ns), 0)
        col = lax.broadcasted_iota(jnp.int32, (ns, ns), 1)
        gram = jnp.zeros((ns, ns), jnp.float32)
        p = 0
        for a in range(ns):
            for b in range(a, ns):
                total = jnp.sum(acc_ref[p])
                hit = ((row == a) & (col == b)) | ((row == b) & (col == a))
                gram = jnp.where(hit, total, gram)
                p += 1
        g_ref[...] = gram


def residual(coeffs_t, basis3, snaps3, block_rows=2 * ROWS):
    nk, nr, nz = basis3.shape
    ns = snaps3.shape[0]
    pairs = ns * (ns + 1) // 2
    w, g = pl.pallas_call(
        residual_kernel,
        grid=(nr // block_rows,),
        in_specs=[pl.BlockSpec((ns, nk), lambda j: (0, 0)),
                  pl.BlockSpec((nk, block_rows, nz), lambda j: (0, j, 0)),
                  pl.BlockSpec((ns, block_rows, nz), lambda j: (0, j, 0))],
        out_specs=[pl.BlockSpec((ns, block_rows, nz), lambda j: (0, j, 0)),
                   pl.BlockSpec((ns, ns), lambda j: (0, 0))],
        out_shape=[jax.ShapeDtypeStruct((ns, nr, nz), jnp.float32),
                   jax.ShapeDtypeStruct((ns, ns), jnp.float32)],
        scratch_shapes=[pltpu.VMEM((ns * ROWS, nk * ROWS), jnp.bfloat16),
                        pltpu.VMEM((pairs, ROWS // 2, nz), jnp.float32)],
        compiler_params=pltpu.CompilerParams(dimension_semantics=("arbitrary",)),
        cost_estimate=pl.CostEstimate(flops=2 * ns * ROWS * nk * ROWS * nz * (nr // ROWS), transcendentals=0,
                                      bytes_accessed=nk * nr * nz * 2 + 2 * ns * nr * nz * 4),
    )(coeffs_t, basis3, snaps3)
    return w, g


def offset_slice(padded, offset, dimension, length):
    return lax.slice_in_dim(padded, 2 + offset, 2 + offset + length, axis=dimension)


def second_diff(padded, center, dimension, length):
    return (
        -offset_slice(padded, 2, dimension, length)
        + 16.0 * offset_slice(padded, 1, dimension, length)
        - 30.0 * center
        + 16.0 * offset_slice(padded, -1, dimension, length)
        - offset_slice(padded, -2, dimension, length)
    ) / 12.0


def local_terms(center, ypadded, flow_rows, shear_rows):
    ny_loc = center.shape[2]
    nz_loc = center.shape[3]
    zpadded = jnp.concatenate([center[..., -2:], center, center[..., :2]], axis=3)
    local = viscosity * (second_diff(ypadded, center, 2, ny_loc) + second_diff(zpadded, center, 3, nz_loc))
    shear_term = shear_rows[None, None, :, None] * center[1:2]
    return jnp.concatenate([local[:1] - shear_term, local[1:]], axis=0)


def streamwise_terms(center, xpadded, flow_rows):
    nx_loc = center.shape[1]
    first_x = (
        -offset_slice(xpadded, 2, 1, nx_loc)
        + 8.0 * offset_slice(xpadded, 1, 1, nx_loc)
        - 8.0 * offset_slice(xpadded, -1, 1, nx_loc)
        + offset_slice(xpadded, -2, 1, nx_loc)
    ) / 12.0
    profile = flow_rows[None, None, :, None]
    return -profile * first_x + viscosity * second_diff(xpadded, center, 1, nx_loc)


def segmented_tendency(center, flow_rows, shear_rows):
    xpadded = extended(center, (("slab", 1),), 2, True)
    ypadded = extended(center, (("role", 2),), 2, False)
    local = local_terms(center, ypadded, flow_rows, shear_rows)
    return streamwise_terms(center, xpadded, flow_rows) + local


def on_device(velocity, basis, mean_flow, shear):
    ny_loc = velocity.shape[2]
    role_index = lax.axis_index("role")
    flow_rows = lax.dynamic_slice_in_dim(mean_flow, role_index * ny_loc, ny_loc)
    shear_rows = lax.dynamic_slice_in_dim(shear, role_index * ny_loc, ny_loc)
    tend_zero = segmented_tendency(velocity, flow_rows, shear_rows)
    segment_one = velocity + time_step * (8.0 / 15.0) * tend_zero
    tend_one = segmented_tendency(segment_one, flow_rows, shear_rows)
    advanced = segment_one + time_step * (5.0 / 12.0 * tend_one - 17.0 / 60.0 * tend_zero)
    snapshots = jnp.concatenate([segment_one, advanced], axis=0)
    ns = snapshots.shape[0]
    snaps3 = snapshots.reshape(ns, -1, snapshots.shape[3])
    basis3 = basis.reshape(basis.shape[0], -1, basis.shape[3])
    partial_proj = project(basis3, snaps3.astype(jnp.bfloat16))
    coeffs_t = allreduce(partial_proj, ("role", "slab"))
    coeffs = coeffs_t.T
    residual3, local_gram = residual(coeffs_t, basis3, snaps3)
    total_gram = allreduce(local_gram, ("role", "slab"))
    lower_factor = jnp.linalg.cholesky(total_gram)
    inverse_factor = jax.scipy.linalg.solve_triangular(lower_factor, jnp.eye(ns, dtype=jnp.float32), lower=True)
    directions = jnp.sum(inverse_factor[:, :, None, None] * residual3[None], axis=1)
    return (advanced, coeffs, lower_factor.T, directions.reshape(snapshots.shape))


def solution(mesh):
    return jax.shard_map(
        on_device,
        mesh=mesh,
        in_specs=(P(None, "slab", "role", None), P(None, "slab", "role", None), P(), P()),
        out_specs=(P(None, "slab", "role", None), P(), P(), P(None, "slab", "role", None)),
        check_vma=False,
    )
```

```python
import numpy as np
import jax
import jax.numpy as jnp
from jax import lax
from jax.experimental import pallas as pl
from jax.experimental.pallas import tpu as pltpu
from jax.sharding import PartitionSpec as P

viscosity = 0.1
ROWS = 16
time_step = 0.4


def extended(cells, sides, width, closed):
    for axis, dim in sides:
        count = lax.axis_size(axis)
        ends = count if closed else count - 1
        head = lax.slice_in_dim(cells, 0, width, axis=dim)
        tail = lax.slice_in_dim(cells, cells.shape[dim] - width, cells.shape[dim], axis=dim)
        if count == 2 and not closed:
            lower_side = lax.axis_index(axis) == 0
            got = lax.ppermute(jnp.where(lower_side, tail, head), axis, [(0, 1), (1, 0)])
            zeros = jnp.zeros_like(got)
            cells = jnp.concatenate(
                [jnp.where(lower_side, zeros, got), cells, jnp.where(lower_side, got, zeros)], axis=dim
            )
            continue
        cells = jnp.concatenate(
            [
                lax.ppermute(tail, axis, [(i, (i + 1) % count) for i in range(ends)]),
                cells,
                lax.ppermute(head, axis, [((i + 1) % count, i) for i in range(ends)]),
            ],
            axis=dim,
        )
    return cells


def ring_pairs(size, stride, count, second):
    pairs = []
    for i in range(count):
        digit = (i // stride) % size
        if size == 2 or not second:
            partner = digit ^ 1
        else:
            partner = (digit + 1) % size if digit % 2 else (digit - 1) % size
        pairs.append((i, i + (partner - digit) * stride))
    return pairs


def exchange_rounds(axis, count):
    rounds = []
    stride = 1
    while stride < count:
        size = 4 if count % (stride * 4) == 0 else 2
        rounds.append(ring_pairs(size, stride, count, False))
        if size == 4:
            rounds.append(ring_pairs(size, stride, count, True))
        stride *= size
    return [(axis, pairs) for pairs in rounds]


def allreduce(value, axes):
    sizes = [lax.axis_size(axis) for axis in axes]
    if any(size & (size - 1) for size in sizes):
        return lax.psum(value, axes)
    for axis, size in zip(axes, sizes):
        for name, pairs in exchange_rounds(axis, size):
            value = value + lax.ppermute(value, name, pairs)
    return value


def project_kernel(b_ref, s_ref, o_ref):
    tk, nr, nz = b_ref.shape
    ns = s_ref.shape[0]
    acc = jnp.zeros((tk * ROWS, ns * ROWS), jnp.float32)
    for j in range(nr // ROWS):
        rows = pl.ds(j * ROWS, ROWS)
        lhs = b_ref[:, rows, :].reshape(tk * ROWS, nz)
        rhs = s_ref[:, rows, :].reshape(ns * ROWS, nz)
        acc = acc + lax.dot_general(lhs, rhs, (((1,), (1,)), ((), ())), preferred_element_type=jnp.float32)
    row_t = lax.broadcasted_iota(jnp.int32, acc.shape, 0) % ROWS
    col_t = lax.broadcasted_iota(jnp.int32, acc.shape, 1) % ROWS
    acc = jnp.where(row_t == col_t, acc, 0.0)
    lanes = jnp.sum(acc.reshape(tk, ROWS, ns * ROWS), axis=1)
    group = lax.broadcasted_iota(jnp.int32, (ns, ns * ROWS), 1) // ROWS
    snapshot = lax.broadcasted_iota(jnp.int32, (ns, ns * ROWS), 0)
    gather = jnp.where(group == snapshot, 1.0, 0.0)
    o_ref[...] = lax.dot_general(gather, lanes, (((1,), (1,)), ((), ())),
                                 precision=lax.Precision.HIGHEST, preferred_element_type=jnp.float32)


def project(basis3, snaps3, tk=128):
    nk, nr, nz = basis3.shape
    ns = snaps3.shape[0]
    return pl.pallas_call(
        project_kernel,
        grid=(nk // tk,),
        in_specs=[pl.BlockSpec((tk, nr, nz), lambda i: (i, 0, 0)),
                  pl.BlockSpec((ns, nr, nz), lambda i: (0, 0, 0))],
        out_specs=pl.BlockSpec((ns, tk), lambda i: (0, i)),
        out_shape=jax.ShapeDtypeStruct((ns, nk), jnp.float32),
        cost_estimate=pl.CostEstimate(flops=2 * nk * nr * nz * ns * ROWS, transcendentals=0,
                                      bytes_accessed=nk * nr * nz * 2 + ns * nr * nz * 2 + nk * ns * 4),
    )(basis3, snaps3)


def residual_kernel(c_ref, b_ref, s_ref, o_ref, g_ref, spread_ref, acc_ref):
    nk, _, nz = b_ref.shape
    ns = s_ref.shape[0]
    rows = ROWS
    step = pl.program_id(0)

    @pl.when(step == 0)
    def _():
        col = lax.broadcasted_iota(jnp.int32, (nk, nk * rows), 1)
        row = lax.broadcasted_iota(jnp.int32, (nk, nk * rows), 0)
        expand = jnp.where(col // rows == row, 1.0, 0.0).astype(jnp.bfloat16)
        wide = jnp.dot(c_ref[...].astype(jnp.bfloat16), expand, preferred_element_type=jnp.float32)
        tall = jnp.broadcast_to(wide[:, None, :], (ns, rows, nk * rows)).reshape(ns * rows, nk * rows)
        r_t = lax.broadcasted_iota(jnp.int32, tall.shape, 0) % rows
        c_t = lax.broadcasted_iota(jnp.int32, tall.shape, 1) % rows
        spread_ref[...] = jnp.where(r_t == c_t, tall, 0.0).astype(jnp.bfloat16)
        acc_ref[...] = jnp.zeros_like(acc_ref)

    for part in range(b_ref.shape[1] // ROWS):
        window = pl.ds(part * ROWS, ROWS)
        block = b_ref[:, window, :].reshape(nk * ROWS, nz)
        prod = jnp.dot(spread_ref[...], block, preferred_element_type=jnp.float32)
        w = s_ref[:, window, :] - prod.reshape(ns, ROWS, nz)
        o_ref[:, window, :] = w
        p = 0
        for a in range(ns):
            for b in range(a, ns):
                term = w[a] * w[b]
                acc_ref[p] += term[: ROWS // 2] + term[ROWS // 2:]
                p += 1

    @pl.when(step == pl.num_programs(0) - 1)
    def _():
        row = lax.broadcasted_iota(jnp.int32, (ns, ns), 0)
        col = lax.broadcasted_iota(jnp.int32, (ns, ns), 1)
        gram = jnp.zeros((ns, ns), jnp.float32)
        p = 0
        for a in range(ns):
            for b in range(a, ns):
                total = jnp.sum(acc_ref[p])
                hit = ((row == a) & (col == b)) | ((row == b) & (col == a))
                gram = jnp.where(hit, total, gram)
                p += 1
        g_ref[...] = gram


def residual(coeffs_t, basis3, snaps3, block_rows=2 * ROWS):
    nk, nr, nz = basis3.shape
    ns = snaps3.shape[0]
    pairs = ns * (ns + 1) // 2
    w, g = pl.pallas_call(
        residual_kernel,
        grid=(nr // block_rows,),
        in_specs=[pl.BlockSpec((ns, nk), lambda j: (0, 0)),
                  pl.BlockSpec((nk, block_rows, nz), lambda j: (0, j, 0)),
                  pl.BlockSpec((ns, block_rows, nz), lambda j: (0, j, 0))],
        out_specs=[pl.BlockSpec((ns, block_rows, nz), lambda j: (0, j, 0)),
                   pl.BlockSpec((ns, ns), lambda j: (0, 0))],
        out_shape=[jax.ShapeDtypeStruct((ns, nr, nz), jnp.float32),
                   jax.ShapeDtypeStruct((ns, ns), jnp.float32)],
        scratch_shapes=[pltpu.VMEM((ns * ROWS, nk * ROWS), jnp.bfloat16),
                        pltpu.VMEM((pairs, ROWS // 2, nz), jnp.float32)],
        compiler_params=pltpu.CompilerParams(dimension_semantics=("arbitrary",)),
        cost_estimate=pl.CostEstimate(flops=2 * ns * ROWS * nk * ROWS * nz * (nr // ROWS), transcendentals=0,
                                      bytes_accessed=nk * nr * nz * 2 + 2 * ns * nr * nz * 4),
    )(coeffs_t, basis3, snaps3)
    return w, g


def factor_kernel(g_ref, w_ref, u_ref, d_ref):
    ns = g_ref.shape[0]
    gram = g_ref[...]
    row = lax.broadcasted_iota(jnp.int32, (ns, ns), 0)
    col = lax.broadcasted_iota(jnp.int32, (ns, ns), 1)
    upper = jnp.zeros((ns, ns), jnp.float32)
    for j in range(ns):
        grow = jnp.sum(jnp.where(row == j, gram, 0.0), axis=0, keepdims=True)
        ucol = jnp.sum(jnp.where(col == j, upper, 0.0), axis=1, keepdims=True)
        v = grow - jnp.sum(upper * ucol, axis=0, keepdims=True)
        root = jnp.sqrt(jnp.sum(jnp.where(col[:1] == j, v, 0.0)))
        newrow = jnp.where(col[:1] > j, v / root, jnp.where(col[:1] == j, root, 0.0))
        upper = jnp.where(row == j, newrow, upper)
    u_ref[...] = upper

    def entry(s, t):
        return jnp.sum(jnp.where((row == t) & (col == s), upper, 0.0))

    for s in range(ns):
        acc = w_ref[s]
        for t in range(s):
            acc = acc - entry(s, t) * d_ref[t]
        d_ref[s] = acc / entry(s, s)


def factor_and_solve(gram, residual3):
    ns = gram.shape[0]
    vmem = pl.BlockSpec(memory_space=pltpu.VMEM)
    return pl.pallas_call(
        factor_kernel,
        in_specs=[vmem, vmem],
        out_specs=[vmem, vmem],
        out_shape=[jax.ShapeDtypeStruct((ns, ns), jnp.float32),
                   jax.ShapeDtypeStruct(residual3.shape, jnp.float32)],
        cost_estimate=pl.CostEstimate(flops=ns * ns * residual3[0].size, transcendentals=ns,
                                      bytes_accessed=2 * residual3.size * 4),
    )(gram, residual3)


def offset_slice(padded, offset, dimension, length):
    return lax.slice_in_dim(padded, 2 + offset, 2 + offset + length, axis=dimension)


def second_diff(padded, center, dimension, length):
    return (
        -offset_slice(padded, 2, dimension, length)
        + 16.0 * offset_slice(padded, 1, dimension, length)
        - 30.0 * center
        + 16.0 * offset_slice(padded, -1, dimension, length)
        - offset_slice(padded, -2, dimension, length)
    ) / 12.0


def local_terms(center, ypadded, flow_rows, shear_rows):
    ny_loc = center.shape[2]
    nz_loc = center.shape[3]
    zpadded = jnp.concatenate([center[..., -2:], center, center[..., :2]], axis=3)
    local = viscosity * (second_diff(ypadded, center, 2, ny_loc) + second_diff(zpadded, center, 3, nz_loc))
    shear_term = shear_rows[None, None, :, None] * center[1:2]
    return jnp.concatenate([local[:1] - shear_term, local[1:]], axis=0)


def streamwise_terms(center, xpadded, flow_rows):
    nx_loc = center.shape[1]
    first_x = (
        -offset_slice(xpadded, 2, 1, nx_loc)
        + 8.0 * offset_slice(xpadded, 1, 1, nx_loc)
        - 8.0 * offset_slice(xpadded, -1, 1, nx_loc)
        + offset_slice(xpadded, -2, 1, nx_loc)
    ) / 12.0
    profile = flow_rows[None, None, :, None]
    return -profile * first_x + viscosity * second_diff(xpadded, center, 1, nx_loc)


def segmented_tendency(center, flow_rows, shear_rows):
    xpadded = extended(center, (("slab", 1),), 2, True)
    ypadded = extended(center, (("role", 2),), 2, False)
    local = local_terms(center, ypadded, flow_rows, shear_rows)
    return streamwise_terms(center, xpadded, flow_rows) + local


def on_device(velocity, basis, mean_flow, shear):
    ny_loc = velocity.shape[2]
    role_index = lax.axis_index("role")
    flow_rows = lax.dynamic_slice_in_dim(mean_flow, role_index * ny_loc, ny_loc)
    shear_rows = lax.dynamic_slice_in_dim(shear, role_index * ny_loc, ny_loc)
    tend_zero = segmented_tendency(velocity, flow_rows, shear_rows)
    segment_one = velocity + time_step * (8.0 / 15.0) * tend_zero
    tend_one = segmented_tendency(segment_one, flow_rows, shear_rows)
    advanced = segment_one + time_step * (5.0 / 12.0 * tend_one - 17.0 / 60.0 * tend_zero)
    snapshots = jnp.concatenate([segment_one, advanced], axis=0)
    ns = snapshots.shape[0]
    snaps3 = snapshots.reshape(ns, -1, snapshots.shape[3])
    basis3 = basis.reshape(basis.shape[0], -1, basis.shape[3])
    partial_proj = project(basis3, snaps3.astype(jnp.bfloat16))
    coeffs_t = allreduce(partial_proj, ("role", "slab"))
    coeffs = coeffs_t.T
    residual3, local_gram = residual(coeffs_t, basis3, snaps3)
    total_gram = allreduce(local_gram, ("role", "slab"))
    upper_factor, directions = factor_and_solve(total_gram, residual3)
    return (advanced, coeffs, upper_factor, directions.reshape(snapshots.shape))


def solution(mesh):
    return jax.shard_map(
        on_device,
        mesh=mesh,
        in_specs=(P(None, "slab", "role", None), P(None, "slab", "role", None), P(), P()),
        out_specs=(P(None, "slab", "role", None), P(), P(), P(None, "slab", "role", None)),
        check_vma=False,
    )
```

```python
import numpy as np
import jax
import jax.numpy as jnp
from jax import lax
from jax.experimental import pallas as pl
from jax.experimental.pallas import tpu as pltpu
from jax.sharding import PartitionSpec as P

viscosity = 0.1
ROWS = 16
time_step = 0.4


def extended(cells, sides, width, closed):
    for axis, dim in sides:
        count = lax.axis_size(axis)
        ends = count if closed else count - 1
        head = lax.slice_in_dim(cells, 0, width, axis=dim)
        tail = lax.slice_in_dim(cells, cells.shape[dim] - width, cells.shape[dim], axis=dim)
        if count == 2 and not closed:
            lower_side = lax.axis_index(axis) == 0
            got = lax.ppermute(jnp.where(lower_side, tail, head), axis, [(0, 1), (1, 0)])
            zeros = jnp.zeros_like(got)
            cells = jnp.concatenate(
                [jnp.where(lower_side, zeros, got), cells, jnp.where(lower_side, got, zeros)], axis=dim
            )
            continue
        cells = jnp.concatenate(
            [
                lax.ppermute(tail, axis, [(i, (i + 1) % count) for i in range(ends)]),
                cells,
                lax.ppermute(head, axis, [((i + 1) % count, i) for i in range(ends)]),
            ],
            axis=dim,
        )
    return cells


def ring_pairs(size, stride, count, second):
    pairs = []
    for i in range(count):
        digit = (i // stride) % size
        if size == 2 or not second:
            partner = digit ^ 1
        else:
            partner = (digit + 1) % size if digit % 2 else (digit - 1) % size
        pairs.append((i, i + (partner - digit) * stride))
    return pairs


def exchange_rounds(axis, count):
    rounds = []
    stride = 1
    while stride < count:
        size = 4 if count % (stride * 4) == 0 else 2
        rounds.append(ring_pairs(size, stride, count, False))
        if size == 4:
            rounds.append(ring_pairs(size, stride, count, True))
        stride *= size
    return [(axis, pairs) for pairs in rounds]


def allreduce(value, axes):
    sizes = [lax.axis_size(axis) for axis in axes]
    if any(size & (size - 1) for size in sizes):
        return lax.psum(value, axes)
    for axis, size in zip(axes, sizes):
        for name, pairs in exchange_rounds(axis, size):
            value = value + lax.ppermute(value, name, pairs)
    return value


def project_kernel(b_ref, s_ref, o_ref):
    tk, nr, nz = b_ref.shape
    ns = s_ref.shape[0]
    acc = jnp.zeros((tk * ROWS, ns * ROWS), jnp.float32)
    for j in range(nr // ROWS):
        rows = pl.ds(j * ROWS, ROWS)
        lhs = b_ref[:, rows, :].reshape(tk * ROWS, nz)
        rhs = s_ref[:, rows, :].reshape(ns * ROWS, nz)
        acc = acc + lax.dot_general(lhs, rhs, (((1,), (1,)), ((), ())), preferred_element_type=jnp.float32)
    row_t = lax.broadcasted_iota(jnp.int32, acc.shape, 0) % ROWS
    col_t = lax.broadcasted_iota(jnp.int32, acc.shape, 1) % ROWS
    acc = jnp.where(row_t == col_t, acc, 0.0)
    lanes = jnp.sum(acc.reshape(tk, ROWS, ns * ROWS), axis=1)
    group = lax.broadcasted_iota(jnp.int32, (ns, ns * ROWS), 1) // ROWS
    snapshot = lax.broadcasted_iota(jnp.int32, (ns, ns * ROWS), 0)
    gather = jnp.where(group == snapshot, 1.0, 0.0)
    o_ref[...] = lax.dot_general(gather, lanes, (((1,), (1,)), ((), ())),
                                 precision=lax.Precision.HIGHEST, preferred_element_type=jnp.float32)


def project(basis3, snaps3, tk=128):
    nk, nr, nz = basis3.shape
    ns = snaps3.shape[0]
    return pl.pallas_call(
        project_kernel,
        grid=(nk // tk,),
        in_specs=[pl.BlockSpec((tk, nr, nz), lambda i: (i, 0, 0)),
                  pl.BlockSpec((ns, nr, nz), lambda i: (0, 0, 0))],
        out_specs=pl.BlockSpec((ns, tk), lambda i: (0, i)),
        out_shape=jax.ShapeDtypeStruct((ns, nk), jnp.float32),
        cost_estimate=pl.CostEstimate(flops=2 * nk * nr * nz * ns * ROWS, transcendentals=0,
                                      bytes_accessed=nk * nr * nz * 2 + ns * nr * nz * 2 + nk * ns * 4),
    )(basis3, snaps3)


def residual_kernel(c_ref, b_ref, s_ref, o_ref, g_ref, spread_ref, acc_ref):
    nk, _, nz = b_ref.shape
    ns = s_ref.shape[0]
    rows = ROWS
    step = pl.program_id(0)

    @pl.when(step == 0)
    def _():
        col = lax.broadcasted_iota(jnp.int32, (nk, nk * rows), 1)
        row = lax.broadcasted_iota(jnp.int32, (nk, nk * rows), 0)
        expand = jnp.where(col // rows == row, 1.0, 0.0).astype(jnp.bfloat16)
        wide = jnp.dot(c_ref[...].astype(jnp.bfloat16), expand, preferred_element_type=jnp.float32)
        tall = jnp.broadcast_to(wide[:, None, :], (ns, rows, nk * rows)).reshape(ns * rows, nk * rows)
        r_t = lax.broadcasted_iota(jnp.int32, tall.shape, 0) % rows
        c_t = lax.broadcasted_iota(jnp.int32, tall.shape, 1) % rows
        spread_ref[...] = jnp.where(r_t == c_t, tall, 0.0).astype(jnp.bfloat16)
        acc_ref[...] = jnp.zeros_like(acc_ref)

    for part in range(b_ref.shape[1] // ROWS):
        window = pl.ds(part * ROWS, ROWS)
        block = b_ref[:, window, :].reshape(nk * ROWS, nz)
        prod = jnp.dot(spread_ref[...], block, preferred_element_type=jnp.float32)
        w = s_ref[:, window, :] - prod.reshape(ns, ROWS, nz)
        o_ref[:, window, :] = w
        p = 0
        for a in range(ns):
            for b in range(a, ns):
                term = w[a] * w[b]
                acc_ref[p] += term[: ROWS // 2] + term[ROWS // 2:]
                p += 1

    @pl.when(step == pl.num_programs(0) - 1)
    def _():
        row = lax.broadcasted_iota(jnp.int32, (ns, ns), 0)
        col = lax.broadcasted_iota(jnp.int32, (ns, ns), 1)
        gram = jnp.zeros((ns, ns), jnp.float32)
        p = 0
        for a in range(ns):
            for b in range(a, ns):
                total = jnp.sum(acc_ref[p])
                hit = ((row == a) & (col == b)) | ((row == b) & (col == a))
                gram = jnp.where(hit, total, gram)
                p += 1
        g_ref[...] = gram


def residual(coeffs_t, basis3, snaps3, block_rows=2 * ROWS):
    nk, nr, nz = basis3.shape
    ns = snaps3.shape[0]
    pairs = ns * (ns + 1) // 2
    w, g = pl.pallas_call(
        residual_kernel,
        grid=(nr // block_rows,),
        in_specs=[pl.BlockSpec((ns, nk), lambda j: (0, 0)),
                  pl.BlockSpec((nk, block_rows, nz), lambda j: (0, j, 0)),
                  pl.BlockSpec((ns, block_rows, nz), lambda j: (0, j, 0))],
        out_specs=[pl.BlockSpec((ns, block_rows, nz), lambda j: (0, j, 0)),
                   pl.BlockSpec((ns, ns), lambda j: (0, 0))],
        out_shape=[jax.ShapeDtypeStruct((ns, nr, nz), jnp.float32),
                   jax.ShapeDtypeStruct((ns, ns), jnp.float32)],
        scratch_shapes=[pltpu.VMEM((ns * ROWS, nk * ROWS), jnp.bfloat16),
                        pltpu.VMEM((pairs, ROWS // 2, nz), jnp.float32)],
        compiler_params=pltpu.CompilerParams(dimension_semantics=("arbitrary",)),
        cost_estimate=pl.CostEstimate(flops=2 * ns * ROWS * nk * ROWS * nz * (nr // ROWS), transcendentals=0,
                                      bytes_accessed=nk * nr * nz * 2 + 2 * ns * nr * nz * 4),
    )(coeffs_t, basis3, snaps3)
    return w, g


def factor_kernel(g_ref, w_ref, u_ref, d_ref):
    ns = g_ref.shape[0]
    gram = g_ref[...]
    row = lax.broadcasted_iota(jnp.int32, (ns, ns), 0)
    col = lax.broadcasted_iota(jnp.int32, (ns, ns), 1)
    upper = jnp.zeros((ns, ns), jnp.float32)
    for j in range(ns):
        grow = jnp.sum(jnp.where(row == j, gram, 0.0), axis=0, keepdims=True)
        ucol = jnp.sum(jnp.where(col == j, upper, 0.0), axis=1, keepdims=True)
        v = grow - jnp.sum(upper * ucol, axis=0, keepdims=True)
        root = jnp.sqrt(jnp.sum(jnp.where(col[:1] == j, v, 0.0)))
        newrow = jnp.where(col[:1] > j, v / root, jnp.where(col[:1] == j, root, 0.0))
        upper = jnp.where(row == j, newrow, upper)
    u_ref[...] = upper

    def entry(s, t):
        return jnp.sum(jnp.where((row == t) & (col == s), upper, 0.0))

    for s in range(ns):
        acc = w_ref[s]
        for t in range(s):
            acc = acc - entry(s, t) * d_ref[t]
        d_ref[s] = acc * (1.0 / entry(s, s))


def factor_and_solve(gram, residual3):
    ns = gram.shape[0]
    vmem = pl.BlockSpec(memory_space=pltpu.VMEM)
    return pl.pallas_call(
        factor_kernel,
        in_specs=[vmem, vmem],
        out_specs=[vmem, vmem],
        out_shape=[jax.ShapeDtypeStruct((ns, ns), jnp.float32),
                   jax.ShapeDtypeStruct(residual3.shape, jnp.float32)],
        cost_estimate=pl.CostEstimate(flops=ns * ns * residual3[0].size, transcendentals=ns,
                                      bytes_accessed=2 * residual3.size * 4),
    )(gram, residual3)


def offset_slice(padded, offset, dimension, length):
    return lax.slice_in_dim(padded, 2 + offset, 2 + offset + length, axis=dimension)


def second_diff(padded, center, dimension, length):
    return (
        -offset_slice(padded, 2, dimension, length)
        + 16.0 * offset_slice(padded, 1, dimension, length)
        - 30.0 * center
        + 16.0 * offset_slice(padded, -1, dimension, length)
        - offset_slice(padded, -2, dimension, length)
    ) / 12.0


def local_terms(center, ypadded, flow_rows, shear_rows):
    ny_loc = center.shape[2]
    nz_loc = center.shape[3]
    zpadded = jnp.concatenate([center[..., -2:], center, center[..., :2]], axis=3)
    local = viscosity * (second_diff(ypadded, center, 2, ny_loc) + second_diff(zpadded, center, 3, nz_loc))
    shear_term = shear_rows[None, None, :, None] * center[1:2]
    return jnp.concatenate([local[:1] - shear_term, local[1:]], axis=0)


def streamwise_terms(center, xpadded, flow_rows):
    nx_loc = center.shape[1]
    first_x = (
        -offset_slice(xpadded, 2, 1, nx_loc)
        + 8.0 * offset_slice(xpadded, 1, 1, nx_loc)
        - 8.0 * offset_slice(xpadded, -1, 1, nx_loc)
        + offset_slice(xpadded, -2, 1, nx_loc)
    ) / 12.0
    profile = flow_rows[None, None, :, None]
    return -profile * first_x + viscosity * second_diff(xpadded, center, 1, nx_loc)


def segmented_tendency(center, flow_rows, shear_rows):
    xpadded = extended(center, (("slab", 1),), 2, True)
    ypadded = extended(center, (("role", 2),), 2, False)
    local = local_terms(center, ypadded, flow_rows, shear_rows)
    return streamwise_terms(center, xpadded, flow_rows) + local


def on_device(velocity, basis, mean_flow, shear):
    ny_loc = velocity.shape[2]
    role_index = lax.axis_index("role")
    flow_rows = lax.dynamic_slice_in_dim(mean_flow, role_index * ny_loc, ny_loc)
    shear_rows = lax.dynamic_slice_in_dim(shear, role_index * ny_loc, ny_loc)
    tend_zero = segmented_tendency(velocity, flow_rows, shear_rows)
    segment_one = velocity + time_step * (8.0 / 15.0) * tend_zero
    tend_one = segmented_tendency(segment_one, flow_rows, shear_rows)
    advanced = segment_one + time_step * (5.0 / 12.0 * tend_one - 17.0 / 60.0 * tend_zero)
    snapshots = jnp.concatenate([segment_one, advanced], axis=0)
    ns = snapshots.shape[0]
    snaps3 = snapshots.reshape(ns, -1, snapshots.shape[3])
    basis3 = basis.reshape(basis.shape[0], -1, basis.shape[3])
    partial_proj = project(basis3, snaps3.astype(jnp.bfloat16))
    coeffs_t = allreduce(partial_proj, ("role", "slab"))
    coeffs = coeffs_t.T
    residual3, local_gram = residual(coeffs_t, basis3, snaps3)
    total_gram = allreduce(local_gram, ("role", "slab"))
    upper_factor, directions = factor_and_solve(total_gram, residual3)
    return (advanced, coeffs, upper_factor, directions.reshape(snapshots.shape))


def solution(mesh):
    return jax.shard_map(
        on_device,
        mesh=mesh,
        in_specs=(P(None, "slab", "role", None), P(None, "slab", "role", None), P(), P()),
        out_specs=(P(None, "slab", "role", None), P(), P(), P(None, "slab", "role", None)),
        check_vma=False,
    )
```

```python
import numpy as np
import jax
import jax.numpy as jnp
from jax import lax
from jax.experimental import pallas as pl
from jax.experimental.pallas import tpu as pltpu
from jax.sharding import PartitionSpec as P

viscosity = 0.1
ROWS = 16
time_step = 0.4


def extended(cells, sides, width, closed):
    for axis, dim in sides:
        count = lax.axis_size(axis)
        ends = count if closed else count - 1
        head = lax.slice_in_dim(cells, 0, width, axis=dim)
        tail = lax.slice_in_dim(cells, cells.shape[dim] - width, cells.shape[dim], axis=dim)
        if count == 2 and not closed:
            lower_side = lax.axis_index(axis) == 0
            got = lax.ppermute(jnp.where(lower_side, tail, head), axis, [(0, 1), (1, 0)])
            zeros = jnp.zeros_like(got)
            cells = jnp.concatenate(
                [jnp.where(lower_side, zeros, got), cells, jnp.where(lower_side, got, zeros)], axis=dim
            )
            continue
        cells = jnp.concatenate(
            [
                lax.ppermute(tail, axis, [(i, (i + 1) % count) for i in range(ends)]),
                cells,
                lax.ppermute(head, axis, [((i + 1) % count, i) for i in range(ends)]),
            ],
            axis=dim,
        )
    return cells


def ring_pairs(size, stride, count, second):
    pairs = []
    for i in range(count):
        digit = (i // stride) % size
        if size == 2 or not second:
            partner = digit ^ 1
        else:
            partner = (digit + 1) % size if digit % 2 else (digit - 1) % size
        pairs.append((i, i + (partner - digit) * stride))
    return pairs


def exchange_rounds(axis, count):
    rounds = []
    stride = 1
    while stride < count:
        size = 4 if count % (stride * 4) == 0 else 2
        rounds.append(ring_pairs(size, stride, count, False))
        if size == 4:
            rounds.append(ring_pairs(size, stride, count, True))
        stride *= size
    return [(axis, pairs) for pairs in rounds]


def allreduce(value, axes):
    sizes = [lax.axis_size(axis) for axis in axes]
    if any(size & (size - 1) for size in sizes):
        return lax.psum(value, axes)
    for axis, size in zip(axes, sizes):
        for name, pairs in exchange_rounds(axis, size):
            value = value + lax.ppermute(value, name, pairs)
    return value


def project_kernel(b_ref, first_ref, second_ref, o_ref):
    tk, nr, nz = b_ref.shape
    ns = first_ref.shape[0] + second_ref.shape[0]
    acc = jnp.zeros((tk * ROWS, ns * ROWS), jnp.float32)
    for j in range(nr // ROWS):
        rows = pl.ds(j * ROWS, ROWS)
        lhs = b_ref[:, rows, :].reshape(tk * ROWS, nz)
        rhs = jnp.concatenate([first_ref[:, rows, :], second_ref[:, rows, :]], axis=0).reshape(ns * ROWS, nz)
        acc = acc + lax.dot_general(lhs, rhs, (((1,), (1,)), ((), ())), preferred_element_type=jnp.float32)
    row_t = lax.broadcasted_iota(jnp.int32, acc.shape, 0) % ROWS
    col_t = lax.broadcasted_iota(jnp.int32, acc.shape, 1) % ROWS
    acc = jnp.where(row_t == col_t, acc, 0.0)
    lanes = jnp.sum(acc.reshape(tk, ROWS, ns * ROWS), axis=1)
    group = lax.broadcasted_iota(jnp.int32, (ns, ns * ROWS), 1) // ROWS
    snapshot = lax.broadcasted_iota(jnp.int32, (ns, ns * ROWS), 0)
    gather = jnp.where(group == snapshot, 1.0, 0.0)
    o_ref[...] = lax.dot_general(gather, lanes, (((1,), (1,)), ((), ())),
                                 precision=lax.Precision.HIGHEST, preferred_element_type=jnp.float32)


def project(basis3, first3, second3, tk=128):
    nk, nr, nz = basis3.shape
    ns = first3.shape[0] + second3.shape[0]
    return pl.pallas_call(
        project_kernel,
        grid=(nk // tk,),
        in_specs=[pl.BlockSpec((tk, nr, nz), lambda i: (i, 0, 0)),
                  pl.BlockSpec(first3.shape, lambda i: (0, 0, 0)),
                  pl.BlockSpec(second3.shape, lambda i: (0, 0, 0))],
        out_specs=pl.BlockSpec((ns, tk), lambda i: (0, i)),
        out_shape=jax.ShapeDtypeStruct((ns, nk), jnp.float32),
        cost_estimate=pl.CostEstimate(flops=2 * nk * nr * nz * ns * ROWS, transcendentals=0,
                                      bytes_accessed=nk * nr * nz * 2 + ns * nr * nz * 2 + nk * ns * 4),
    )(basis3, first3, second3)


def residual_kernel(c_ref, b_ref, s_ref, o_ref, g_ref, spread_ref, acc_ref):
    nk, _, nz = b_ref.shape
    ns = s_ref.shape[0]
    rows = ROWS
    step = pl.program_id(0)

    @pl.when(step == 0)
    def _():
        col = lax.broadcasted_iota(jnp.int32, (nk, nk * rows), 1)
        row = lax.broadcasted_iota(jnp.int32, (nk, nk * rows), 0)
        expand = jnp.where(col // rows == row, 1.0, 0.0).astype(jnp.bfloat16)
        wide = jnp.dot(c_ref[...].astype(jnp.bfloat16), expand, preferred_element_type=jnp.float32)
        tall = jnp.broadcast_to(wide[:, None, :], (ns, rows, nk * rows)).reshape(ns * rows, nk * rows)
        r_t = lax.broadcasted_iota(jnp.int32, tall.shape, 0) % rows
        c_t = lax.broadcasted_iota(jnp.int32, tall.shape, 1) % rows
        spread_ref[...] = jnp.where(r_t == c_t, tall, 0.0).astype(jnp.bfloat16)
        acc_ref[...] = jnp.zeros_like(acc_ref)

    for part in range(b_ref.shape[1] // ROWS):
        window = pl.ds(part * ROWS, ROWS)
        block = b_ref[:, window, :].reshape(nk * ROWS, nz)
        prod = jnp.dot(spread_ref[...], block, preferred_element_type=jnp.float32)
        w = s_ref[:, window, :] - prod.reshape(ns, ROWS, nz)
        o_ref[:, window, :] = w
        p = 0
        for a in range(ns):
            for b in range(a, ns):
                term = w[a] * w[b]
                acc_ref[p] += term[: ROWS // 2] + term[ROWS // 2:]
                p += 1

    @pl.when(step == pl.num_programs(0) - 1)
    def _():
        row = lax.broadcasted_iota(jnp.int32, (ns, ns), 0)
        col = lax.broadcasted_iota(jnp.int32, (ns, ns), 1)
        gram = jnp.zeros((ns, ns), jnp.float32)
        p = 0
        for a in range(ns):
            for b in range(a, ns):
                total = jnp.sum(acc_ref[p])
                hit = ((row == a) & (col == b)) | ((row == b) & (col == a))
                gram = jnp.where(hit, total, gram)
                p += 1
        g_ref[...] = gram


def residual(coeffs_t, basis3, snaps3, block_rows=2 * ROWS):
    nk, nr, nz = basis3.shape
    ns = snaps3.shape[0]
    pairs = ns * (ns + 1) // 2
    w, g = pl.pallas_call(
        residual_kernel,
        grid=(nr // block_rows,),
        in_specs=[pl.BlockSpec((ns, nk), lambda j: (0, 0)),
                  pl.BlockSpec((nk, block_rows, nz), lambda j: (0, j, 0)),
                  pl.BlockSpec((ns, block_rows, nz), lambda j: (0, j, 0))],
        out_specs=[pl.BlockSpec((ns, block_rows, nz), lambda j: (0, j, 0)),
                   pl.BlockSpec((ns, ns), lambda j: (0, 0))],
        out_shape=[jax.ShapeDtypeStruct((ns, nr, nz), jnp.float32),
                   jax.ShapeDtypeStruct((ns, ns), jnp.float32)],
        scratch_shapes=[pltpu.VMEM((ns * ROWS, nk * ROWS), jnp.bfloat16),
                        pltpu.VMEM((pairs, ROWS // 2, nz), jnp.float32)],
        compiler_params=pltpu.CompilerParams(dimension_semantics=("arbitrary",)),
        cost_estimate=pl.CostEstimate(flops=2 * ns * ROWS * nk * ROWS * nz * (nr // ROWS), transcendentals=0,
                                      bytes_accessed=nk * nr * nz * 2 + 2 * ns * nr * nz * 4),
    )(coeffs_t, basis3, snaps3)
    return w, g


def factor_kernel(g_ref, w_ref, u_ref, d_ref):
    ns = g_ref.shape[0]
    gram = g_ref[...]
    row = lax.broadcasted_iota(jnp.int32, (ns, ns), 0)
    col = lax.broadcasted_iota(jnp.int32, (ns, ns), 1)
    upper = jnp.zeros((ns, ns), jnp.float32)
    for j in range(ns):
        grow = jnp.sum(jnp.where(row == j, gram, 0.0), axis=0, keepdims=True)
        ucol = jnp.sum(jnp.where(col == j, upper, 0.0), axis=1, keepdims=True)
        v = grow - jnp.sum(upper * ucol, axis=0, keepdims=True)
        root = jnp.sqrt(jnp.sum(jnp.where(col[:1] == j, v, 0.0)))
        newrow = jnp.where(col[:1] > j, v / root, jnp.where(col[:1] == j, root, 0.0))
        upper = jnp.where(row == j, newrow, upper)
    u_ref[...] = upper

    def entry(s, t):
        return jnp.sum(jnp.where((row == t) & (col == s), upper, 0.0))

    for s in range(ns):
        acc = w_ref[s]
        for t in range(s):
            acc = acc - entry(s, t) * d_ref[t]
        d_ref[s] = acc * (1.0 / entry(s, s))


def factor_and_solve(gram, residual3):
    ns = gram.shape[0]
    vmem = pl.BlockSpec(memory_space=pltpu.VMEM)
    return pl.pallas_call(
        factor_kernel,
        in_specs=[vmem, vmem],
        out_specs=[vmem, vmem],
        out_shape=[jax.ShapeDtypeStruct((ns, ns), jnp.float32),
                   jax.ShapeDtypeStruct(residual3.shape, jnp.float32)],
        cost_estimate=pl.CostEstimate(flops=ns * ns * residual3[0].size, transcendentals=ns,
                                      bytes_accessed=2 * residual3.size * 4),
    )(gram, residual3)


def offset_slice(padded, offset, dimension, length):
    return lax.slice_in_dim(padded, 2 + offset, 2 + offset + length, axis=dimension)


def second_diff(padded, center, dimension, length):
    return (
        -offset_slice(padded, 2, dimension, length)
        + 16.0 * offset_slice(padded, 1, dimension, length)
        - 30.0 * center
        + 16.0 * offset_slice(padded, -1, dimension, length)
        - offset_slice(padded, -2, dimension, length)
    ) / 12.0


def local_terms(center, ypadded, flow_rows, shear_rows):
    ny_loc = center.shape[2]
    nz_loc = center.shape[3]
    zpadded = jnp.concatenate([center[..., -2:], center, center[..., :2]], axis=3)
    local = viscosity * (second_diff(ypadded, center, 2, ny_loc) + second_diff(zpadded, center, 3, nz_loc))
    shear_term = shear_rows[None, None, :, None] * center[1:2]
    return jnp.concatenate([local[:1] - shear_term, local[1:]], axis=0)


def streamwise_terms(center, xpadded, flow_rows):
    nx_loc = center.shape[1]
    first_x = (
        -offset_slice(xpadded, 2, 1, nx_loc)
        + 8.0 * offset_slice(xpadded, 1, 1, nx_loc)
        - 8.0 * offset_slice(xpadded, -1, 1, nx_loc)
        + offset_slice(xpadded, -2, 1, nx_loc)
    ) / 12.0
    profile = flow_rows[None, None, :, None]
    return -profile * first_x + viscosity * second_diff(xpadded, center, 1, nx_loc)


def segmented_tendency(center, flow_rows, shear_rows):
    xpadded = extended(center, (("slab", 1),), 2, True)
    ypadded = extended(center, (("role", 2),), 2, False)
    local = local_terms(center, ypadded, flow_rows, shear_rows)
    return streamwise_terms(center, xpadded, flow_rows) + local


def on_device(velocity, basis, mean_flow, shear):
    ny_loc = velocity.shape[2]
    role_index = lax.axis_index("role")
    flow_rows = lax.dynamic_slice_in_dim(mean_flow, role_index * ny_loc, ny_loc)
    shear_rows = lax.dynamic_slice_in_dim(shear, role_index * ny_loc, ny_loc)
    tend_zero = segmented_tendency(velocity, flow_rows, shear_rows)
    segment_one = velocity + time_step * (8.0 / 15.0) * tend_zero
    tend_one = segmented_tendency(segment_one, flow_rows, shear_rows)
    advanced = segment_one + time_step * (5.0 / 12.0 * tend_one - 17.0 / 60.0 * tend_zero)
    snapshots = jnp.concatenate([segment_one, advanced], axis=0)
    ns = snapshots.shape[0]
    snaps3 = snapshots.reshape(ns, -1, snapshots.shape[3])
    basis3 = basis.reshape(basis.shape[0], -1, basis.shape[3])
    first3 = segment_one.reshape(segment_one.shape[0], -1, segment_one.shape[3]).astype(jnp.bfloat16)
    second3 = advanced.reshape(advanced.shape[0], -1, advanced.shape[3]).astype(jnp.bfloat16)
    partial_proj = project(basis3, first3, second3)
    coeffs_t = allreduce(partial_proj, ("role", "slab"))
    coeffs = coeffs_t.T
    residual3, local_gram = residual(coeffs_t, basis3, snaps3)
    total_gram = allreduce(local_gram, ("role", "slab"))
    upper_factor, directions = factor_and_solve(total_gram, residual3)
    return (advanced, coeffs, upper_factor, directions.reshape(snapshots.shape))


def solution(mesh):
    return jax.shard_map(
        on_device,
        mesh=mesh,
        in_specs=(P(None, "slab", "role", None), P(None, "slab", "role", None), P(), P()),
        out_specs=(P(None, "slab", "role", None), P(), P(), P(None, "slab", "role", None)),
        check_vma=False,
    )
```

```python
import numpy as np
import jax
import jax.numpy as jnp
from jax import lax
from jax.experimental import pallas as pl
from jax.experimental.pallas import tpu as pltpu
from jax.sharding import PartitionSpec as P

viscosity = 0.1
ROWS = 16
time_step = 0.4


def extended(cells, sides, width, closed):
    for axis, dim in sides:
        count = lax.axis_size(axis)
        ends = count if closed else count - 1
        head = lax.slice_in_dim(cells, 0, width, axis=dim)
        tail = lax.slice_in_dim(cells, cells.shape[dim] - width, cells.shape[dim], axis=dim)
        if count == 2 and not closed:
            lower_side = lax.axis_index(axis) == 0
            got = lax.ppermute(jnp.where(lower_side, tail, head), axis, [(0, 1), (1, 0)])
            zeros = jnp.zeros_like(got)
            cells = jnp.concatenate(
                [jnp.where(lower_side, zeros, got), cells, jnp.where(lower_side, got, zeros)], axis=dim
            )
            continue
        cells = jnp.concatenate(
            [
                lax.ppermute(tail, axis, [(i, (i + 1) % count) for i in range(ends)]),
                cells,
                lax.ppermute(head, axis, [((i + 1) % count, i) for i in range(ends)]),
            ],
            axis=dim,
        )
    return cells


def ring_pairs(size, stride, count, second):
    pairs = []
    for i in range(count):
        digit = (i // stride) % size
        if size == 2 or not second:
            partner = digit ^ 1
        else:
            partner = (digit + 1) % size if digit % 2 else (digit - 1) % size
        pairs.append((i, i + (partner - digit) * stride))
    return pairs


def exchange_rounds(axis, count):
    rounds = []
    stride = 1
    while stride < count:
        size = 4 if count % (stride * 4) == 0 else 2
        rounds.append(ring_pairs(size, stride, count, False))
        if size == 4:
            rounds.append(ring_pairs(size, stride, count, True))
        stride *= size
    return [(axis, pairs) for pairs in rounds]


def allreduce_halves(value, axes):
    sizes = [lax.axis_size(axis) for axis in axes]
    if any(size & (size - 1) for size in sizes):
        return lax.psum(value, axes), jnp.zeros_like(value)
    rounds = [step for axis, size in zip(axes, sizes) for step in exchange_rounds(axis, size)]
    for name, pairs in rounds[:-1]:
        value = value + lax.ppermute(value, name, pairs)
    name, pairs = rounds[-1]
    return value, lax.ppermute(value, name, pairs)


def project_kernel(b_ref, s_ref, o_ref):
    tk, nr, nz = b_ref.shape
    ns = s_ref.shape[0]
    acc = jnp.zeros((tk * ROWS, ns * ROWS), jnp.float32)
    for j in range(nr // ROWS):
        rows = pl.ds(j * ROWS, ROWS)
        lhs = b_ref[:, rows, :].reshape(tk * ROWS, nz)
        rhs = s_ref[:, rows, :].reshape(ns * ROWS, nz)
        acc = acc + lax.dot_general(lhs, rhs, (((1,), (1,)), ((), ())), preferred_element_type=jnp.float32)
    row_t = lax.broadcasted_iota(jnp.int32, acc.shape, 0) % ROWS
    col_t = lax.broadcasted_iota(jnp.int32, acc.shape, 1) % ROWS
    acc = jnp.where(row_t == col_t, acc, 0.0)
    lanes = jnp.sum(acc.reshape(tk, ROWS, ns * ROWS), axis=1)
    group = lax.broadcasted_iota(jnp.int32, (ns, ns * ROWS), 1) // ROWS
    snapshot = lax.broadcasted_iota(jnp.int32, (ns, ns * ROWS), 0)
    gather = jnp.where(group == snapshot, 1.0, 0.0)
    o_ref[...] = lax.dot_general(gather, lanes, (((1,), (1,)), ((), ())),
                                 precision=lax.Precision.HIGHEST, preferred_element_type=jnp.float32)


def project(basis3, snaps3, tk=128):
    nk, nr, nz = basis3.shape
    ns = snaps3.shape[0]
    return pl.pallas_call(
        project_kernel,
        grid=(nk // tk,),
        in_specs=[pl.BlockSpec((tk, nr, nz), lambda i: (i, 0, 0)),
                  pl.BlockSpec((ns, nr, nz), lambda i: (0, 0, 0))],
        out_specs=pl.BlockSpec((ns, tk), lambda i: (0, i)),
        out_shape=jax.ShapeDtypeStruct((ns, nk), jnp.float32),
        cost_estimate=pl.CostEstimate(flops=2 * nk * nr * nz * ns * ROWS, transcendentals=0,
                                      bytes_accessed=nk * nr * nz * 2 + ns * nr * nz * 2 + nk * ns * 4),
    )(basis3, snaps3)


def residual_kernel(c_ref, d_ref, b_ref, s_ref, o_ref, g_ref, spread_ref, acc_ref):
    nk, _, nz = b_ref.shape
    ns = s_ref.shape[0]
    rows = ROWS
    step = pl.program_id(0)

    @pl.when(step == 0)
    def _():
        col = lax.broadcasted_iota(jnp.int32, (nk, nk * rows), 1)
        row = lax.broadcasted_iota(jnp.int32, (nk, nk * rows), 0)
        expand = jnp.where(col // rows == row, 1.0, 0.0).astype(jnp.bfloat16)
        wide = jnp.dot((c_ref[...] + d_ref[...]).astype(jnp.bfloat16), expand, preferred_element_type=jnp.float32)
        tall = jnp.broadcast_to(wide[:, None, :], (ns, rows, nk * rows)).reshape(ns * rows, nk * rows)
        r_t = lax.broadcasted_iota(jnp.int32, tall.shape, 0) % rows
        c_t = lax.broadcasted_iota(jnp.int32, tall.shape, 1) % rows
        spread_ref[...] = jnp.where(r_t == c_t, tall, 0.0).astype(jnp.bfloat16)
        acc_ref[...] = jnp.zeros_like(acc_ref)

    for part in range(b_ref.shape[1] // ROWS):
        window = pl.ds(part * ROWS, ROWS)
        block = b_ref[:, window, :].reshape(nk * ROWS, nz)
        prod = jnp.dot(spread_ref[...], block, preferred_element_type=jnp.float32)
        w = s_ref[:, window, :] - prod.reshape(ns, ROWS, nz)
        o_ref[:, window, :] = w
        p = 0
        for a in range(ns):
            for b in range(a, ns):
                term = w[a] * w[b]
                acc_ref[p] += term[: ROWS // 2] + term[ROWS // 2:]
                p += 1

    @pl.when(step == pl.num_programs(0) - 1)
    def _():
        row = lax.broadcasted_iota(jnp.int32, (ns, ns), 0)
        col = lax.broadcasted_iota(jnp.int32, (ns, ns), 1)
        gram = jnp.zeros((ns, ns), jnp.float32)
        p = 0
        for a in range(ns):
            for b in range(a, ns):
                total = jnp.sum(acc_ref[p])
                hit = ((row == a) & (col == b)) | ((row == b) & (col == a))
                gram = jnp.where(hit, total, gram)
                p += 1
        g_ref[...] = gram


def residual(coeffs_t, coeffs_other, basis3, snaps3, block_rows=2 * ROWS):
    nk, nr, nz = basis3.shape
    ns = snaps3.shape[0]
    pairs = ns * (ns + 1) // 2
    w, g = pl.pallas_call(
        residual_kernel,
        grid=(nr // block_rows,),
        in_specs=[pl.BlockSpec((ns, nk), lambda j: (0, 0)),
                  pl.BlockSpec((ns, nk), lambda j: (0, 0)),
                  pl.BlockSpec((nk, block_rows, nz), lambda j: (0, j, 0)),
                  pl.BlockSpec((ns, block_rows, nz), lambda j: (0, j, 0))],
        out_specs=[pl.BlockSpec((ns, block_rows, nz), lambda j: (0, j, 0)),
                   pl.BlockSpec((ns, ns), lambda j: (0, 0))],
        out_shape=[jax.ShapeDtypeStruct((ns, nr, nz), jnp.float32),
                   jax.ShapeDtypeStruct((ns, ns), jnp.float32)],
        scratch_shapes=[pltpu.VMEM((ns * ROWS, nk * ROWS), jnp.bfloat16),
                        pltpu.VMEM((pairs, ROWS // 2, nz), jnp.float32)],
        compiler_params=pltpu.CompilerParams(dimension_semantics=("arbitrary",)),
        cost_estimate=pl.CostEstimate(flops=2 * ns * ROWS * nk * ROWS * nz * (nr // ROWS), transcendentals=0,
                                      bytes_accessed=nk * nr * nz * 2 + 2 * ns * nr * nz * 4),
    )(coeffs_t, coeffs_other, basis3, snaps3)
    return w, g


def factor_kernel(g_ref, h_ref, w_ref, u_ref, d_ref):
    ns = g_ref.shape[0]
    gram = g_ref[...] + h_ref[...]
    row = lax.broadcasted_iota(jnp.int32, (ns, ns), 0)
    col = lax.broadcasted_iota(jnp.int32, (ns, ns), 1)
    upper = jnp.zeros((ns, ns), jnp.float32)
    for j in range(ns):
        grow = jnp.sum(jnp.where(row == j, gram, 0.0), axis=0, keepdims=True)
        ucol = jnp.sum(jnp.where(col == j, upper, 0.0), axis=1, keepdims=True)
        v = grow - jnp.sum(upper * ucol, axis=0, keepdims=True)
        root = jnp.sqrt(jnp.sum(jnp.where(col[:1] == j, v, 0.0)))
        newrow = jnp.where(col[:1] > j, v / root, jnp.where(col[:1] == j, root, 0.0))
        upper = jnp.where(row == j, newrow, upper)
    u_ref[...] = upper

    def entry(s, t):
        return jnp.sum(jnp.where((row == t) & (col == s), upper, 0.0))

    for s in range(ns):
        acc = w_ref[s]
        for t in range(s):
            acc = acc - entry(s, t) * d_ref[t]
        d_ref[s] = acc / entry(s, s)


def factor_and_solve(gram, gram_other, residual3):
    ns = gram.shape[0]
    vmem = pl.BlockSpec(memory_space=pltpu.VMEM)
    return pl.pallas_call(
        factor_kernel,
        in_specs=[vmem, vmem, vmem],
        out_specs=[vmem, vmem],
        out_shape=[jax.ShapeDtypeStruct((ns, ns), jnp.float32),
                   jax.ShapeDtypeStruct(residual3.shape, jnp.float32)],
        cost_estimate=pl.CostEstimate(flops=ns * ns * residual3[0].size, transcendentals=ns,
                                      bytes_accessed=2 * residual3.size * 4),
    )(gram, gram_other, residual3)


def offset_slice(padded, offset, dimension, length):
    return lax.slice_in_dim(padded, 2 + offset, 2 + offset + length, axis=dimension)


def second_diff(padded, center, dimension, length):
    return (
        -offset_slice(padded, 2, dimension, length)
        + 16.0 * offset_slice(padded, 1, dimension, length)
        - 30.0 * center
        + 16.0 * offset_slice(padded, -1, dimension, length)
        - offset_slice(padded, -2, dimension, length)
    ) / 12.0


def local_terms(center, ypadded, flow_rows, shear_rows):
    ny_loc = center.shape[2]
    nz_loc = center.shape[3]
    zpadded = jnp.concatenate([center[..., -2:], center, center[..., :2]], axis=3)
    local = viscosity * (second_diff(ypadded, center, 2, ny_loc) + second_diff(zpadded, center, 3, nz_loc))
    shear_term = shear_rows[None, None, :, None] * center[1:2]
    return jnp.concatenate([local[:1] - shear_term, local[1:]], axis=0)


def streamwise_terms(center, xpadded, flow_rows):
    nx_loc = center.shape[1]
    first_x = (
        -offset_slice(xpadded, 2, 1, nx_loc)
        + 8.0 * offset_slice(xpadded, 1, 1, nx_loc)
        - 8.0 * offset_slice(xpadded, -1, 1, nx_loc)
        + offset_slice(xpadded, -2, 1, nx_loc)
    ) / 12.0
    profile = flow_rows[None, None, :, None]
    return -profile * first_x + viscosity * second_diff(xpadded, center, 1, nx_loc)


def segmented_tendency(center, flow_rows, shear_rows):
    xpadded = extended(center, (("slab", 1),), 2, True)
    ypadded = extended(center, (("role", 2),), 2, False)
    local = local_terms(center, ypadded, flow_rows, shear_rows)
    return streamwise_terms(center, xpadded, flow_rows) + local


def on_device(velocity, basis, mean_flow, shear):
    ny_loc = velocity.shape[2]
    role_index = lax.axis_index("role")
    flow_rows = lax.dynamic_slice_in_dim(mean_flow, role_index * ny_loc, ny_loc)
    shear_rows = lax.dynamic_slice_in_dim(shear, role_index * ny_loc, ny_loc)
    tend_zero = segmented_tendency(velocity, flow_rows, shear_rows)
    segment_one = velocity + time_step * (8.0 / 15.0) * tend_zero
    tend_one = segmented_tendency(segment_one, flow_rows, shear_rows)
    advanced = segment_one + time_step * (5.0 / 12.0 * tend_one - 17.0 / 60.0 * tend_zero)
    snapshots = jnp.concatenate([segment_one, advanced], axis=0)
    ns = snapshots.shape[0]
    snaps3 = snapshots.reshape(ns, -1, snapshots.shape[3])
    basis3 = basis.reshape(basis.shape[0], -1, basis.shape[3])
    partial_proj = project(basis3, snaps3.astype(jnp.bfloat16))
    coeffs_t, coeffs_other = allreduce_halves(partial_proj, ("role", "slab"))
    coeffs = (coeffs_t + coeffs_other).T
    residual3, local_gram = residual(coeffs_t, coeffs_other, basis3, snaps3)
    gram, gram_other = allreduce_halves(local_gram, ("role", "slab"))
    upper_factor, directions = factor_and_solve(gram, gram_other, residual3)
    return (advanced, coeffs, upper_factor, directions.reshape(snapshots.shape))


def solution(mesh):
    return jax.shard_map(
        on_device,
        mesh=mesh,
        in_specs=(P(None, "slab", "role", None), P(None, "slab", "role", None), P(), P()),
        out_specs=(P(None, "slab", "role", None), P(), P(), P(None, "slab", "role", None)),
        check_vma=False,
    )
```

```python
import numpy as np
import jax
import jax.numpy as jnp
from jax import lax
from jax.experimental import pallas as pl
from jax.experimental.pallas import tpu as pltpu
from jax.sharding import PartitionSpec as P

viscosity = 0.1
ROWS = 16
time_step = 0.4


def extended(cells, sides, width, closed):
    for axis, dim in sides:
        count = lax.axis_size(axis)
        ends = count if closed else count - 1
        head = lax.slice_in_dim(cells, 0, width, axis=dim)
        tail = lax.slice_in_dim(cells, cells.shape[dim] - width, cells.shape[dim], axis=dim)
        if count == 2 and not closed:
            lower_side = lax.axis_index(axis) == 0
            got = lax.ppermute(jnp.where(lower_side, tail, head), axis, [(0, 1), (1, 0)])
            zeros = jnp.zeros_like(got)
            cells = jnp.concatenate(
                [jnp.where(lower_side, zeros, got), cells, jnp.where(lower_side, got, zeros)], axis=dim
            )
            continue
        cells = jnp.concatenate(
            [
                lax.ppermute(tail, axis, [(i, (i + 1) % count) for i in range(ends)]),
                cells,
                lax.ppermute(head, axis, [((i + 1) % count, i) for i in range(ends)]),
            ],
            axis=dim,
        )
    return cells


def ring_pairs(size, stride, count, second):
    pairs = []
    for i in range(count):
        digit = (i // stride) % size
        if size == 2 or not second:
            partner = digit ^ 1
        else:
            partner = (digit + 1) % size if digit % 2 else (digit - 1) % size
        pairs.append((i, i + (partner - digit) * stride))
    return pairs


def exchange_rounds(axis, count):
    rounds = []
    stride = 1
    while stride < count:
        size = 4 if count % (stride * 4) == 0 else 2
        rounds.append(ring_pairs(size, stride, count, False))
        if size == 4:
            rounds.append(ring_pairs(size, stride, count, True))
        stride *= size
    return [(axis, pairs) for pairs in rounds]


def mirror(index, strides, flips):
    for bit, stride in enumerate(strides):
        if flips >> bit & 1:
            digit = (index // stride) % 4
            index += (3 - 2 * digit) * stride
    return index


def allreduce(value, axes):
    sizes = [lax.axis_size(axis) for axis in axes]
    if any(size & (size - 1) for size in sizes):
        return lax.psum(value, axes)
    *pair_axes, ring_axis = axes
    for axis, size in zip(pair_axes, sizes):
        for name, pairs in exchange_rounds(axis, size):
            value = value + lax.ppermute(value, name, pairs)
    count = sizes[-1]
    strides = []
    stride = 1
    while stride < count and count % (stride * 4) == 0:
        strides.append(stride)
        stride *= 4
    if stride != count or not strides:
        for name, pairs in exchange_rounds(ring_axis, count):
            value = value + lax.ppermute(value, name, pairs)
        return value
    for stride in strides:
        value = value + lax.ppermute(value, ring_axis, ring_pairs(4, stride, count, False))
    groups = 1 << len(strides)
    gathered = [value] + [
        lax.ppermute(value, ring_axis, [(i, mirror(i, strides, flips)) for i in range(count)])
        for flips in range(1, groups)
    ]
    stacked = jnp.stack(gathered)
    index = lax.axis_index(ring_axis)
    own = sum(((index // stride) % 4 // 2) << bit for bit, stride in enumerate(strides))
    total = None
    for group in range(groups):
        term = lax.dynamic_index_in_dim(stacked, group ^ own, 0, keepdims=False)
        total = term if total is None else total + term
    return total


def project_kernel(b_ref, s_ref, o_ref):
    tk, nr, nz = b_ref.shape
    ns = s_ref.shape[0]
    acc = jnp.zeros((tk * ROWS, ns * ROWS), jnp.float32)
    for j in range(nr // ROWS):
        rows = pl.ds(j * ROWS, ROWS)
        lhs = b_ref[:, rows, :].reshape(tk * ROWS, nz)
        rhs = s_ref[:, rows, :].reshape(ns * ROWS, nz)
        acc = acc + lax.dot_general(lhs, rhs, (((1,), (1,)), ((), ())), preferred_element_type=jnp.float32)
    row_t = lax.broadcasted_iota(jnp.int32, acc.shape, 0) % ROWS
    col_t = lax.broadcasted_iota(jnp.int32, acc.shape, 1) % ROWS
    acc = jnp.where(row_t == col_t, acc, 0.0)
    lanes = jnp.sum(acc.reshape(tk, ROWS, ns * ROWS), axis=1)
    group = lax.broadcasted_iota(jnp.int32, (ns, ns * ROWS), 1) // ROWS
    snapshot = lax.broadcasted_iota(jnp.int32, (ns, ns * ROWS), 0)
    gather = jnp.where(group == snapshot, 1.0, 0.0)
    o_ref[...] = lax.dot_general(gather, lanes, (((1,), (1,)), ((), ())),
                                 precision=lax.Precision.HIGHEST, preferred_element_type=jnp.float32)


def project(basis3, snaps3, tk=128):
    nk, nr, nz = basis3.shape
    ns = snaps3.shape[0]
    return pl.pallas_call(
        project_kernel,
        grid=(nk // tk,),
        in_specs=[pl.BlockSpec((tk, nr, nz), lambda i: (i, 0, 0)),
                  pl.BlockSpec((ns, nr, nz), lambda i: (0, 0, 0))],
        out_specs=pl.BlockSpec((ns, tk), lambda i: (0, i)),
        out_shape=jax.ShapeDtypeStruct((ns, nk), jnp.float32),
        cost_estimate=pl.CostEstimate(flops=2 * nk * nr * nz * ns * ROWS, transcendentals=0,
                                      bytes_accessed=nk * nr * nz * 2 + ns * nr * nz * 2 + nk * ns * 4),
    )(basis3, snaps3)


def residual_kernel(c_ref, b_ref, s_ref, o_ref, g_ref, spread_ref, acc_ref):
    nk, _, nz = b_ref.shape
    ns = s_ref.shape[0]
    rows = ROWS
    step = pl.program_id(0)

    @pl.when(step == 0)
    def _():
        col = lax.broadcasted_iota(jnp.int32, (nk, nk * rows), 1)
        row = lax.broadcasted_iota(jnp.int32, (nk, nk * rows), 0)
        expand = jnp.where(col // rows == row, 1.0, 0.0).astype(jnp.bfloat16)
        wide = jnp.dot(c_ref[...].astype(jnp.bfloat16), expand, preferred_element_type=jnp.float32)
        tall = jnp.broadcast_to(wide[:, None, :], (ns, rows, nk * rows)).reshape(ns * rows, nk * rows)
        r_t = lax.broadcasted_iota(jnp.int32, tall.shape, 0) % rows
        c_t = lax.broadcasted_iota(jnp.int32, tall.shape, 1) % rows
        spread_ref[...] = jnp.where(r_t == c_t, tall, 0.0).astype(jnp.bfloat16)
        acc_ref[...] = jnp.zeros_like(acc_ref)

    for part in range(b_ref.shape[1] // ROWS):
        window = pl.ds(part * ROWS, ROWS)
        block = b_ref[:, window, :].reshape(nk * ROWS, nz)
        prod = jnp.dot(spread_ref[...], block, preferred_element_type=jnp.float32)
        w = s_ref[:, window, :] - prod.reshape(ns, ROWS, nz)
        o_ref[:, window, :] = w
        p = 0
        for a in range(ns):
            for b in range(a, ns):
                term = w[a] * w[b]
                acc_ref[p] += term[: ROWS // 2] + term[ROWS // 2:]
                p += 1

    @pl.when(step == pl.num_programs(0) - 1)
    def _():
        row = lax.broadcasted_iota(jnp.int32, (ns, ns), 0)
        col = lax.broadcasted_iota(jnp.int32, (ns, ns), 1)
        gram = jnp.zeros((ns, ns), jnp.float32)
        p = 0
        for a in range(ns):
            for b in range(a, ns):
                total = jnp.sum(acc_ref[p])
                hit = ((row == a) & (col == b)) | ((row == b) & (col == a))
                gram = jnp.where(hit, total, gram)
                p += 1
        g_ref[...] = gram


def residual(coeffs_t, basis3, snaps3, block_rows=2 * ROWS):
    nk, nr, nz = basis3.shape
    ns = snaps3.shape[0]
    pairs = ns * (ns + 1) // 2
    w, g = pl.pallas_call(
        residual_kernel,
        grid=(nr // block_rows,),
        in_specs=[pl.BlockSpec((ns, nk), lambda j: (0, 0)),
                  pl.BlockSpec((nk, block_rows, nz), lambda j: (0, j, 0)),
                  pl.BlockSpec((ns, block_rows, nz), lambda j: (0, j, 0))],
        out_specs=[pl.BlockSpec((ns, block_rows, nz), lambda j: (0, j, 0)),
                   pl.BlockSpec((ns, ns), lambda j: (0, 0))],
        out_shape=[jax.ShapeDtypeStruct((ns, nr, nz), jnp.float32),
                   jax.ShapeDtypeStruct((ns, ns), jnp.float32)],
        scratch_shapes=[pltpu.VMEM((ns * ROWS, nk * ROWS), jnp.bfloat16),
                        pltpu.VMEM((pairs, ROWS // 2, nz), jnp.float32)],
        compiler_params=pltpu.CompilerParams(dimension_semantics=("arbitrary",)),
        cost_estimate=pl.CostEstimate(flops=2 * ns * ROWS * nk * ROWS * nz * (nr // ROWS), transcendentals=0,
                                      bytes_accessed=nk * nr * nz * 2 + 2 * ns * nr * nz * 4),
    )(coeffs_t, basis3, snaps3)
    return w, g


def factor_kernel(g_ref, w_ref, u_ref, d_ref):
    ns = g_ref.shape[0]
    gram = g_ref[...]
    row = lax.broadcasted_iota(jnp.int32, (ns, ns), 0)
    col = lax.broadcasted_iota(jnp.int32, (ns, ns), 1)
    upper = jnp.zeros((ns, ns), jnp.float32)
    for j in range(ns):
        grow = jnp.sum(jnp.where(row == j, gram, 0.0), axis=0, keepdims=True)
        ucol = jnp.sum(jnp.where(col == j, upper, 0.0), axis=1, keepdims=True)
        v = grow - jnp.sum(upper * ucol, axis=0, keepdims=True)
        root = jnp.sqrt(jnp.sum(jnp.where(col[:1] == j, v, 0.0)))
        newrow = jnp.where(col[:1] > j, v / root, jnp.where(col[:1] == j, root, 0.0))
        upper = jnp.where(row == j, newrow, upper)
    u_ref[...] = upper

    def entry(s, t):
        return jnp.sum(jnp.where((row == t) & (col == s), upper, 0.0))

    for s in range(ns):
        acc = w_ref[s]
        for t in range(s):
            acc = acc - entry(s, t) * d_ref[t]
        d_ref[s] = acc / entry(s, s)


def factor_and_solve(gram, residual3):
    ns = gram.shape[0]
    vmem = pl.BlockSpec(memory_space=pltpu.VMEM)
    return pl.pallas_call(
        factor_kernel,
        in_specs=[vmem, vmem],
        out_specs=[vmem, vmem],
        out_shape=[jax.ShapeDtypeStruct((ns, ns), jnp.float32),
                   jax.ShapeDtypeStruct(residual3.shape, jnp.float32)],
        cost_estimate=pl.CostEstimate(flops=ns * ns * residual3[0].size, transcendentals=ns,
                                      bytes_accessed=2 * residual3.size * 4),
    )(gram, residual3)


def offset_slice(padded, offset, dimension, length):
    return lax.slice_in_dim(padded, 2 + offset, 2 + offset + length, axis=dimension)


def second_diff(padded, center, dimension, length):
    return (
        -offset_slice(padded, 2, dimension, length)
        + 16.0 * offset_slice(padded, 1, dimension, length)
        - 30.0 * center
        + 16.0 * offset_slice(padded, -1, dimension, length)
        - offset_slice(padded, -2, dimension, length)
    ) / 12.0


def local_terms(center, ypadded, flow_rows, shear_rows):
    ny_loc = center.shape[2]
    nz_loc = center.shape[3]
    zpadded = jnp.concatenate([center[..., -2:], center, center[..., :2]], axis=3)
    local = viscosity * (second_diff(ypadded, center, 2, ny_loc) + second_diff(zpadded, center, 3, nz_loc))
    shear_term = shear_rows[None, None, :, None] * center[1:2]
    return jnp.concatenate([local[:1] - shear_term, local[1:]], axis=0)


def streamwise_terms(center, xpadded, flow_rows):
    nx_loc = center.shape[1]
    first_x = (
        -offset_slice(xpadded, 2, 1, nx_loc)
        + 8.0 * offset_slice(xpadded, 1, 1, nx_loc)
        - 8.0 * offset_slice(xpadded, -1, 1, nx_loc)
        + offset_slice(xpadded, -2, 1, nx_loc)
    ) / 12.0
    profile = flow_rows[None, None, :, None]
    return -profile * first_x + viscosity * second_diff(xpadded, center, 1, nx_loc)


def segmented_tendency(center, flow_rows, shear_rows):
    xpadded = extended(center, (("slab", 1),), 2, True)
    ypadded = extended(center, (("role", 2),), 2, False)
    local = local_terms(center, ypadded, flow_rows, shear_rows)
    return streamwise_terms(center, xpadded, flow_rows) + local


def on_device(velocity, basis, mean_flow, shear):
    ny_loc = velocity.shape[2]
    role_index = lax.axis_index("role")
    flow_rows = lax.dynamic_slice_in_dim(mean_flow, role_index * ny_loc, ny_loc)
    shear_rows = lax.dynamic_slice_in_dim(shear, role_index * ny_loc, ny_loc)
    tend_zero = segmented_tendency(velocity, flow_rows, shear_rows)
    segment_one = velocity + time_step * (8.0 / 15.0) * tend_zero
    tend_one = segmented_tendency(segment_one, flow_rows, shear_rows)
    advanced = segment_one + time_step * (5.0 / 12.0 * tend_one - 17.0 / 60.0 * tend_zero)
    snapshots = jnp.concatenate([segment_one, advanced], axis=0)
    ns = snapshots.shape[0]
    snaps3 = snapshots.reshape(ns, -1, snapshots.shape[3])
    basis3 = basis.reshape(basis.shape[0], -1, basis.shape[3])
    partial_proj = project(basis3, snaps3.astype(jnp.bfloat16))
    coeffs_t = allreduce(partial_proj, ("role", "slab"))
    coeffs = coeffs_t.T
    residual3, local_gram = residual(coeffs_t, basis3, snaps3)
    total_gram = allreduce(local_gram, ("role", "slab"))
    upper_factor, directions = factor_and_solve(total_gram, residual3)
    return (advanced, coeffs, upper_factor, directions.reshape(snapshots.shape))


def solution(mesh):
    return jax.shard_map(
        on_device,
        mesh=mesh,
        in_specs=(P(None, "slab", "role", None), P(None, "slab", "role", None), P(), P()),
        out_specs=(P(None, "slab", "role", None), P(), P(), P(None, "slab", "role", None)),
        check_vma=False,
    )
```

```python
import numpy as np
import jax
import jax.numpy as jnp
from jax import lax
from jax.experimental import pallas as pl
from jax.experimental.pallas import tpu as pltpu
from jax.sharding import PartitionSpec as P

viscosity = 0.1
ROWS = 16
time_step = 0.4


def extended(cells, sides, width, closed):
    for axis, dim in sides:
        count = lax.axis_size(axis)
        ends = count if closed else count - 1
        head = lax.slice_in_dim(cells, 0, width, axis=dim)
        tail = lax.slice_in_dim(cells, cells.shape[dim] - width, cells.shape[dim], axis=dim)
        if count == 2 and not closed:
            lower_side = lax.axis_index(axis) == 0
            got = lax.ppermute(jnp.where(lower_side, tail, head), axis, [(0, 1), (1, 0)])
            zeros = jnp.zeros_like(got)
            cells = jnp.concatenate(
                [jnp.where(lower_side, zeros, got), cells, jnp.where(lower_side, got, zeros)], axis=dim
            )
            continue
        cells = jnp.concatenate(
            [
                lax.ppermute(tail, axis, [(i, (i + 1) % count) for i in range(ends)]),
                cells,
                lax.ppermute(head, axis, [((i + 1) % count, i) for i in range(ends)]),
            ],
            axis=dim,
        )
    return cells


def ring_pairs(size, stride, count, second):
    pairs = []
    for i in range(count):
        digit = (i // stride) % size
        if size == 2 or not second:
            partner = digit ^ 1
        else:
            partner = (digit + 1) % size if digit % 2 else (digit - 1) % size
        pairs.append((i, i + (partner - digit) * stride))
    return pairs


def exchange_rounds(axis, count):
    rounds = []
    stride = 1
    while stride < count:
        size = 4 if count % (stride * 4) == 0 else 2
        rounds.append(ring_pairs(size, stride, count, False))
        if size == 4:
            rounds.append(ring_pairs(size, stride, count, True))
        stride *= size
    return [(axis, pairs) for pairs in rounds]


def allreduce(value, axes):
    sizes = [lax.axis_size(axis) for axis in axes]
    if any(size & (size - 1) for size in sizes):
        return lax.psum(value, axes)
    for axis, size in zip(axes, sizes):
        for name, pairs in exchange_rounds(axis, size):
            value = value + lax.ppermute(value, name, pairs)
    return value


def project_kernel(b_ref, s_ref, o_ref):
    tk, nr, nz = b_ref.shape
    ns = s_ref.shape[0]
    acc = jnp.zeros((tk * ROWS, ns * ROWS), jnp.float32)
    for j in range(nr // ROWS):
        rows = pl.ds(j * ROWS, ROWS)
        lhs = b_ref[:, rows, :].reshape(tk * ROWS, nz)
        rhs = s_ref[:, rows, :].reshape(ns * ROWS, nz)
        acc = acc + lax.dot_general(lhs, rhs, (((1,), (1,)), ((), ())), preferred_element_type=jnp.float32)
    row_t = lax.broadcasted_iota(jnp.int32, acc.shape, 0) % ROWS
    col_t = lax.broadcasted_iota(jnp.int32, acc.shape, 1) % ROWS
    acc = jnp.where(row_t == col_t, acc, 0.0)
    lanes = jnp.sum(acc.reshape(tk, ROWS, ns * ROWS), axis=1)
    group = lax.broadcasted_iota(jnp.int32, (ns, ns * ROWS), 1) // ROWS
    snapshot = lax.broadcasted_iota(jnp.int32, (ns, ns * ROWS), 0)
    gather = jnp.where(group == snapshot, 1.0, 0.0)
    result = lax.dot_general(gather, lanes, (((1,), (1,)), ((), ())),
                             precision=lax.Precision.HIGHEST, preferred_element_type=jnp.float32)
    halves = o_ref.shape[1] // tk
    step = pl.program_id(0) % halves
    for half in range(halves):
        @pl.when(step == half)
        def _():
            o_ref[:, half * tk:(half + 1) * tk] = result


def project(basis3, snaps3, tk=64, lanes=128):
    nk, nr, nz = basis3.shape
    ns = snaps3.shape[0]
    return pl.pallas_call(
        project_kernel,
        grid=(nk // tk,),
        in_specs=[pl.BlockSpec((tk, nr, nz), lambda i: (i, 0, 0)),
                  pl.BlockSpec((ns, nr, nz), lambda i: (0, 0, 0))],
        out_specs=pl.BlockSpec((ns, lanes), lambda i: (0, i * tk // lanes)),
        out_shape=jax.ShapeDtypeStruct((ns, nk), jnp.float32),
        cost_estimate=pl.CostEstimate(flops=2 * nk * nr * nz * ns * ROWS, transcendentals=0,
                                      bytes_accessed=nk * nr * nz * 2 + ns * nr * nz * 2 + nk * ns * 4),
    )(basis3, snaps3)


def residual_kernel(c_ref, b_ref, s_ref, o_ref, g_ref, spread_ref, acc_ref):
    nk, _, nz = b_ref.shape
    ns = s_ref.shape[0]
    rows = ROWS
    step = pl.program_id(0)

    @pl.when(step == 0)
    def _():
        col = lax.broadcasted_iota(jnp.int32, (nk, nk * rows), 1)
        row = lax.broadcasted_iota(jnp.int32, (nk, nk * rows), 0)
        expand = jnp.where(col // rows == row, 1.0, 0.0).astype(jnp.bfloat16)
        wide = jnp.dot(c_ref[...].astype(jnp.bfloat16), expand, preferred_element_type=jnp.float32)
        tall = jnp.broadcast_to(wide[:, None, :], (ns, rows, nk * rows)).reshape(ns * rows, nk * rows)
        r_t = lax.broadcasted_iota(jnp.int32, tall.shape, 0) % rows
        c_t = lax.broadcasted_iota(jnp.int32, tall.shape, 1) % rows
        spread_ref[...] = jnp.where(r_t == c_t, tall, 0.0).astype(jnp.bfloat16)
        acc_ref[...] = jnp.zeros_like(acc_ref)

    for part in range(b_ref.shape[1] // ROWS):
        window = pl.ds(part * ROWS, ROWS)
        block = b_ref[:, window, :].reshape(nk * ROWS, nz)
        prod = jnp.dot(spread_ref[...], block, preferred_element_type=jnp.float32)
        w = s_ref[:, window, :] - prod.reshape(ns, ROWS, nz)
        o_ref[:, window, :] = w
        p = 0
        for a in range(ns):
            for b in range(a, ns):
                term = w[a] * w[b]
                acc_ref[p] += term[: ROWS // 2] + term[ROWS // 2:]
                p += 1

    @pl.when(step == pl.num_programs(0) - 1)
    def _():
        row = lax.broadcasted_iota(jnp.int32, (ns, ns), 0)
        col = lax.broadcasted_iota(jnp.int32, (ns, ns), 1)
        gram = jnp.zeros((ns, ns), jnp.float32)
        p = 0
        for a in range(ns):
            for b in range(a, ns):
                total = jnp.sum(acc_ref[p])
                hit = ((row == a) & (col == b)) | ((row == b) & (col == a))
                gram = jnp.where(hit, total, gram)
                p += 1
        g_ref[...] = gram


def residual(coeffs_t, basis3, snaps3, block_rows=2 * ROWS):
    nk, nr, nz = basis3.shape
    ns = snaps3.shape[0]
    pairs = ns * (ns + 1) // 2
    w, g = pl.pallas_call(
        residual_kernel,
        grid=(nr // block_rows,),
        in_specs=[pl.BlockSpec((ns, nk), lambda j: (0, 0)),
                  pl.BlockSpec((nk, block_rows, nz), lambda j: (0, j, 0)),
                  pl.BlockSpec((ns, block_rows, nz), lambda j: (0, j, 0))],
        out_specs=[pl.BlockSpec((ns, block_rows, nz), lambda j: (0, j, 0)),
                   pl.BlockSpec((ns, ns), lambda j: (0, 0))],
        out_shape=[jax.ShapeDtypeStruct((ns, nr, nz), jnp.float32),
                   jax.ShapeDtypeStruct((ns, ns), jnp.float32)],
        scratch_shapes=[pltpu.VMEM((ns * ROWS, nk * ROWS), jnp.bfloat16),
                        pltpu.VMEM((pairs, ROWS // 2, nz), jnp.float32)],
        compiler_params=pltpu.CompilerParams(dimension_semantics=("arbitrary",)),
        cost_estimate=pl.CostEstimate(flops=2 * ns * ROWS * nk * ROWS * nz * (nr // ROWS), transcendentals=0,
                                      bytes_accessed=nk * nr * nz * 2 + 2 * ns * nr * nz * 4),
    )(coeffs_t, basis3, snaps3)
    return w, g


def factor_kernel(g_ref, w_ref, u_ref, d_ref):
    ns = g_ref.shape[0]
    gram = g_ref[...]
    row = lax.broadcasted_iota(jnp.int32, (ns, ns), 0)
    col = lax.broadcasted_iota(jnp.int32, (ns, ns), 1)
    upper = jnp.zeros((ns, ns), jnp.float32)
    for j in range(ns):
        grow = jnp.sum(jnp.where(row == j, gram, 0.0), axis=0, keepdims=True)
        ucol = jnp.sum(jnp.where(col == j, upper, 0.0), axis=1, keepdims=True)
        v = grow - jnp.sum(upper * ucol, axis=0, keepdims=True)
        root = jnp.sqrt(jnp.sum(jnp.where(col[:1] == j, v, 0.0)))
        newrow = jnp.where(col[:1] > j, v / root, jnp.where(col[:1] == j, root, 0.0))
        upper = jnp.where(row == j, newrow, upper)
    u_ref[...] = upper

    def entry(s, t):
        return jnp.sum(jnp.where((row == t) & (col == s), upper, 0.0))

    for s in range(ns):
        acc = w_ref[s]
        for t in range(s):
            acc = acc - entry(s, t) * d_ref[t]
        d_ref[s] = acc / entry(s, s)


def factor_and_solve(gram, residual3):
    ns = gram.shape[0]
    vmem = pl.BlockSpec(memory_space=pltpu.VMEM)
    return pl.pallas_call(
        factor_kernel,
        in_specs=[vmem, vmem],
        out_specs=[vmem, vmem],
        out_shape=[jax.ShapeDtypeStruct((ns, ns), jnp.float32),
                   jax.ShapeDtypeStruct(residual3.shape, jnp.float32)],
        cost_estimate=pl.CostEstimate(flops=ns * ns * residual3[0].size, transcendentals=ns,
                                      bytes_accessed=2 * residual3.size * 4),
    )(gram, residual3)


def offset_slice(padded, offset, dimension, length):
    return lax.slice_in_dim(padded, 2 + offset, 2 + offset + length, axis=dimension)


def second_diff(padded, center, dimension, length):
    return (
        -offset_slice(padded, 2, dimension, length)
        + 16.0 * offset_slice(padded, 1, dimension, length)
        - 30.0 * center
        + 16.0 * offset_slice(padded, -1, dimension, length)
        - offset_slice(padded, -2, dimension, length)
    ) / 12.0


def local_terms(center, ypadded, flow_rows, shear_rows):
    ny_loc = center.shape[2]
    nz_loc = center.shape[3]
    zpadded = jnp.concatenate([center[..., -2:], center, center[..., :2]], axis=3)
    local = viscosity * (second_diff(ypadded, center, 2, ny_loc) + second_diff(zpadded, center, 3, nz_loc))
    shear_term = shear_rows[None, None, :, None] * center[1:2]
    return jnp.concatenate([local[:1] - shear_term, local[1:]], axis=0)


def streamwise_terms(center, xpadded, flow_rows):
    nx_loc = center.shape[1]
    first_x = (
        -offset_slice(xpadded, 2, 1, nx_loc)
        + 8.0 * offset_slice(xpadded, 1, 1, nx_loc)
        - 8.0 * offset_slice(xpadded, -1, 1, nx_loc)
        + offset_slice(xpadded, -2, 1, nx_loc)
    ) / 12.0
    profile = flow_rows[None, None, :, None]
    return -profile * first_x + viscosity * second_diff(xpadded, center, 1, nx_loc)


def segmented_tendency(center, flow_rows, shear_rows):
    xpadded = extended(center, (("slab", 1),), 2, True)
    ypadded = extended(center, (("role", 2),), 2, False)
    local = local_terms(center, ypadded, flow_rows, shear_rows)
    return streamwise_terms(center, xpadded, flow_rows) + local


def on_device(velocity, basis, mean_flow, shear):
    ny_loc = velocity.shape[2]
    role_index = lax.axis_index("role")
    flow_rows = lax.dynamic_slice_in_dim(mean_flow, role_index * ny_loc, ny_loc)
    shear_rows = lax.dynamic_slice_in_dim(shear, role_index * ny_loc, ny_loc)
    tend_zero = segmented_tendency(velocity, flow_rows, shear_rows)
    segment_one = velocity + time_step * (8.0 / 15.0) * tend_zero
    tend_one = segmented_tendency(segment_one, flow_rows, shear_rows)
    advanced = segment_one + time_step * (5.0 / 12.0 * tend_one - 17.0 / 60.0 * tend_zero)
    snapshots = jnp.concatenate([segment_one, advanced], axis=0)
    ns = snapshots.shape[0]
    snaps3 = snapshots.reshape(ns, -1, snapshots.shape[3])
    basis3 = basis.reshape(basis.shape[0], -1, basis.shape[3])
    partial_proj = project(basis3, snaps3.astype(jnp.bfloat16))
    coeffs_t = allreduce(partial_proj, ("role", "slab"))
    coeffs = coeffs_t.T
    residual3, local_gram = residual(coeffs_t, basis3, snaps3)
    total_gram = allreduce(local_gram, ("role", "slab"))
    upper_factor, directions = factor_and_solve(total_gram, residual3)
    return (advanced, coeffs, upper_factor, directions.reshape(snapshots.shape))


def solution(mesh):
    return jax.shard_map(
        on_device,
        mesh=mesh,
        in_specs=(P(None, "slab", "role", None), P(None, "slab", "role", None), P(), P()),
        out_specs=(P(None, "slab", "role", None), P(), P(), P(None, "slab", "role", None)),
        check_vma=False,
    )
```

```python
import numpy as np
import jax
import jax.numpy as jnp
from jax import lax
from jax.experimental import pallas as pl
from jax.experimental.pallas import tpu as pltpu
from jax.sharding import PartitionSpec as P

viscosity = 0.1
ROWS = 16
time_step = 0.4


def extended(cells, sides, width, closed):
    for axis, dim in sides:
        count = lax.axis_size(axis)
        ends = count if closed else count - 1
        head = lax.slice_in_dim(cells, 0, width, axis=dim)
        tail = lax.slice_in_dim(cells, cells.shape[dim] - width, cells.shape[dim], axis=dim)
        if count == 2 and not closed:
            lower_side = lax.axis_index(axis) == 0
            got = lax.ppermute(jnp.where(lower_side, tail, head), axis, [(0, 1), (1, 0)])
            zeros = jnp.zeros_like(got)
            cells = jnp.concatenate(
                [jnp.where(lower_side, zeros, got), cells, jnp.where(lower_side, got, zeros)], axis=dim
            )
            continue
        cells = jnp.concatenate(
            [
                lax.ppermute(tail, axis, [(i, (i + 1) % count) for i in range(ends)]),
                cells,
                lax.ppermute(head, axis, [((i + 1) % count, i) for i in range(ends)]),
            ],
            axis=dim,
        )
    return cells


def ring_pairs(size, stride, count, second):
    pairs = []
    for i in range(count):
        digit = (i // stride) % size
        if size == 2 or not second:
            partner = digit ^ 1
        else:
            partner = (digit + 1) % size if digit % 2 else (digit - 1) % size
        pairs.append((i, i + (partner - digit) * stride))
    return pairs


def exchange_rounds(axis, count):
    rounds = []
    stride = 1
    while stride < count:
        size = 4 if count % (stride * 4) == 0 else 2
        rounds.append(ring_pairs(size, stride, count, False))
        if size == 4:
            rounds.append(ring_pairs(size, stride, count, True))
        stride *= size
    return [(axis, pairs) for pairs in rounds]


def allreduce(value, axes):
    sizes = [lax.axis_size(axis) for axis in axes]
    if any(size & (size - 1) for size in sizes):
        return lax.psum(value, axes)
    for axis, size in zip(axes, sizes):
        for name, pairs in exchange_rounds(axis, size):
            value = value + lax.ppermute(value, name, pairs)
    return value


def project_kernel(b_ref, s_ref, o_ref):
    tk, nr, nz = b_ref.shape
    ns = s_ref.shape[0]
    acc = jnp.zeros((tk * ROWS, ns * ROWS), jnp.float32)
    for j in range(nr // ROWS):
        rows = pl.ds(j * ROWS, ROWS)
        lhs = b_ref[:, rows, :].reshape(tk * ROWS, nz)
        rhs = s_ref[:, rows, :].reshape(ns * ROWS, nz)
        acc = acc + lax.dot_general(lhs, rhs, (((1,), (1,)), ((), ())), preferred_element_type=jnp.float32)
    row_t = lax.broadcasted_iota(jnp.int32, acc.shape, 0) % ROWS
    col_t = lax.broadcasted_iota(jnp.int32, acc.shape, 1) % ROWS
    acc = jnp.where(row_t == col_t, acc, 0.0)
    lanes = jnp.sum(acc.reshape(tk, ROWS, ns * ROWS), axis=1)
    group = lax.broadcasted_iota(jnp.int32, (ns, ns * ROWS), 1) // ROWS
    snapshot = lax.broadcasted_iota(jnp.int32, (ns, ns * ROWS), 0)
    gather = jnp.where(group == snapshot, 1.0, 0.0)
    o_ref[...] = lax.dot_general(gather, lanes, (((1,), (1,)), ((), ())),
                                 precision=lax.Precision.HIGHEST, preferred_element_type=jnp.float32)


def project(basis3, snaps3, tk=128):
    nk, nr, nz = basis3.shape
    ns = snaps3.shape[0]
    return pl.pallas_call(
        project_kernel,
        grid=(nk // tk,),
        in_specs=[pl.BlockSpec((tk, nr, nz), lambda i: (i, 0, 0)),
                  pl.BlockSpec((ns, nr, nz), lambda i: (0, 0, 0))],
        out_specs=pl.BlockSpec((ns, tk), lambda i: (0, i)),
        out_shape=jax.ShapeDtypeStruct((ns, nk), jnp.float32),
        cost_estimate=pl.CostEstimate(flops=2 * nk * nr * nz * ns * ROWS, transcendentals=0,
                                      bytes_accessed=nk * nr * nz * 2 + ns * nr * nz * 2 + nk * ns * 4),
    )(basis3, snaps3)


def residual_kernel(c_ref, b_ref, s_ref, o_ref, g_ref, spread_ref, acc_ref):
    nk, _, nz = b_ref.shape
    ns = s_ref.shape[0]
    rows = ROWS
    step = pl.program_id(0)

    @pl.when(step == 0)
    def _():
        col = lax.broadcasted_iota(jnp.int32, (nk, nk * rows), 1)
        row = lax.broadcasted_iota(jnp.int32, (nk, nk * rows), 0)
        expand = jnp.where(col // rows == row, 1.0, 0.0).astype(jnp.bfloat16)
        wide = jnp.dot(c_ref[...].astype(jnp.bfloat16), expand, preferred_element_type=jnp.float32)
        tall = jnp.broadcast_to(wide[:, None, :], (ns, rows, nk * rows)).reshape(ns * rows, nk * rows)
        r_t = lax.broadcasted_iota(jnp.int32, tall.shape, 0) % rows
        c_t = lax.broadcasted_iota(jnp.int32, tall.shape, 1) % rows
        spread_ref[...] = jnp.where(r_t == c_t, tall, 0.0).astype(jnp.bfloat16)
        acc_ref[...] = jnp.zeros_like(acc_ref)

    for part in range(b_ref.shape[1] // ROWS):
        window = pl.ds(part * ROWS, ROWS)
        block = b_ref[:, window, :].reshape(nk * ROWS, nz)
        prod = jnp.dot(spread_ref[...], block, preferred_element_type=jnp.float32)
        w = s_ref[:, window, :] - prod.reshape(ns, ROWS, nz)
        o_ref[:, window, :] = w
        p = 0
        for a in range(ns):
            for b in range(a, ns):
                term = w[a] * w[b]
                acc_ref[p] += term[: ROWS // 2] + term[ROWS // 2:]
                p += 1

    @pl.when(step == pl.num_programs(0) - 1)
    def _():
        row = lax.broadcasted_iota(jnp.int32, (ns, ns), 0)
        col = lax.broadcasted_iota(jnp.int32, (ns, ns), 1)
        gram = jnp.zeros((ns, ns), jnp.float32)
        p = 0
        for a in range(ns):
            for b in range(a, ns):
                total = jnp.sum(acc_ref[p])
                hit = ((row == a) & (col == b)) | ((row == b) & (col == a))
                gram = jnp.where(hit, total, gram)
                p += 1
        g_ref[...] = gram


def residual(coeffs_t, basis3, snaps3, block_rows=2 * ROWS):
    nk, nr, nz = basis3.shape
    ns = snaps3.shape[0]
    pairs = ns * (ns + 1) // 2
    w, g = pl.pallas_call(
        residual_kernel,
        grid=(nr // block_rows,),
        in_specs=[pl.BlockSpec((ns, nk), lambda j: (0, 0)),
                  pl.BlockSpec((nk, block_rows, nz), lambda j: (0, j, 0)),
                  pl.BlockSpec((ns, block_rows, nz), lambda j: (0, j, 0))],
        out_specs=[pl.BlockSpec((ns, block_rows, nz), lambda j: (0, j, 0)),
                   pl.BlockSpec((ns, ns), lambda j: (0, 0))],
        out_shape=[jax.ShapeDtypeStruct((ns, nr, nz), jnp.float32),
                   jax.ShapeDtypeStruct((ns, ns), jnp.float32)],
        scratch_shapes=[pltpu.VMEM((ns * ROWS, nk * ROWS), jnp.bfloat16),
                        pltpu.VMEM((pairs, ROWS // 2, nz), jnp.float32)],
        compiler_params=pltpu.CompilerParams(dimension_semantics=("arbitrary",)),
        cost_estimate=pl.CostEstimate(flops=2 * ns * ROWS * nk * ROWS * nz * (nr // ROWS), transcendentals=0,
                                      bytes_accessed=nk * nr * nz * 2 + 2 * ns * nr * nz * 4),
    )(coeffs_t, basis3, snaps3)
    return w, g


def factor_kernel(g_ref, w_ref, u_ref, d_ref):
    ns = g_ref.shape[0]
    gram = g_ref[...]
    row = lax.broadcasted_iota(jnp.int32, (ns, ns), 0)
    col = lax.broadcasted_iota(jnp.int32, (ns, ns), 1)
    upper = jnp.zeros((ns, ns), jnp.float32)
    for j in range(ns):
        grow = jnp.sum(jnp.where(row == j, gram, 0.0), axis=0, keepdims=True)
        ucol = jnp.sum(jnp.where(col == j, upper, 0.0), axis=1, keepdims=True)
        v = grow - jnp.sum(upper * ucol, axis=0, keepdims=True)
        root = jnp.sqrt(jnp.sum(jnp.where(col[:1] == j, v, 0.0)))
        newrow = jnp.where(col[:1] > j, v / root, jnp.where(col[:1] == j, root, 0.0))
        upper = jnp.where(row == j, newrow, upper)
    u_ref[...] = upper

    for s in range(ns):
        ucol = jnp.sum(jnp.where(col == s, upper, 0.0), axis=1, keepdims=True)
        acc = w_ref[s]
        for t in range(s):
            acc = acc - ucol[t:t + 1, :] * d_ref[t]
        d_ref[s] = acc / ucol[s:s + 1, :]


def factor_and_solve(gram, residual3):
    ns = gram.shape[0]
    vmem = pl.BlockSpec(memory_space=pltpu.VMEM)
    return pl.pallas_call(
        factor_kernel,
        in_specs=[vmem, vmem],
        out_specs=[vmem, vmem],
        out_shape=[jax.ShapeDtypeStruct((ns, ns), jnp.float32),
                   jax.ShapeDtypeStruct(residual3.shape, jnp.float32)],
        cost_estimate=pl.CostEstimate(flops=ns * ns * residual3[0].size, transcendentals=ns,
                                      bytes_accessed=2 * residual3.size * 4),
    )(gram, residual3)


def offset_slice(padded, offset, dimension, length):
    return lax.slice_in_dim(padded, 2 + offset, 2 + offset + length, axis=dimension)


def second_diff(padded, center, dimension, length):
    return (
        -offset_slice(padded, 2, dimension, length)
        + 16.0 * offset_slice(padded, 1, dimension, length)
        - 30.0 * center
        + 16.0 * offset_slice(padded, -1, dimension, length)
        - offset_slice(padded, -2, dimension, length)
    ) / 12.0


def local_terms(center, ypadded, flow_rows, shear_rows):
    ny_loc = center.shape[2]
    nz_loc = center.shape[3]
    zpadded = jnp.concatenate([center[..., -2:], center, center[..., :2]], axis=3)
    local = viscosity * (second_diff(ypadded, center, 2, ny_loc) + second_diff(zpadded, center, 3, nz_loc))
    shear_term = shear_rows[None, None, :, None] * center[1:2]
    return jnp.concatenate([local[:1] - shear_term, local[1:]], axis=0)


def streamwise_terms(center, xpadded, flow_rows):
    nx_loc = center.shape[1]
    first_x = (
        -offset_slice(xpadded, 2, 1, nx_loc)
        + 8.0 * offset_slice(xpadded, 1, 1, nx_loc)
        - 8.0 * offset_slice(xpadded, -1, 1, nx_loc)
        + offset_slice(xpadded, -2, 1, nx_loc)
    ) / 12.0
    profile = flow_rows[None, None, :, None]
    return -profile * first_x + viscosity * second_diff(xpadded, center, 1, nx_loc)


def segmented_tendency(center, flow_rows, shear_rows):
    xpadded = extended(center, (("slab", 1),), 2, True)
    ypadded = extended(center, (("role", 2),), 2, False)
    local = local_terms(center, ypadded, flow_rows, shear_rows)
    return streamwise_terms(center, xpadded, flow_rows) + local


def on_device(velocity, basis, mean_flow, shear):
    ny_loc = velocity.shape[2]
    role_index = lax.axis_index("role")
    flow_rows = lax.dynamic_slice_in_dim(mean_flow, role_index * ny_loc, ny_loc)
    shear_rows = lax.dynamic_slice_in_dim(shear, role_index * ny_loc, ny_loc)
    tend_zero = segmented_tendency(velocity, flow_rows, shear_rows)
    segment_one = velocity + time_step * (8.0 / 15.0) * tend_zero
    tend_one = segmented_tendency(segment_one, flow_rows, shear_rows)
    advanced = segment_one + time_step * (5.0 / 12.0 * tend_one - 17.0 / 60.0 * tend_zero)
    snapshots = jnp.concatenate([segment_one, advanced], axis=0)
    ns = snapshots.shape[0]
    snaps3 = snapshots.reshape(ns, -1, snapshots.shape[3])
    basis3 = basis.reshape(basis.shape[0], -1, basis.shape[3])
    partial_proj = project(basis3, snaps3.astype(jnp.bfloat16))
    coeffs_t = allreduce(partial_proj, ("role", "slab"))
    coeffs = coeffs_t.T
    residual3, local_gram = residual(coeffs_t, basis3, snaps3)
    total_gram = allreduce(local_gram, ("role", "slab"))
    upper_factor, directions = factor_and_solve(total_gram, residual3)
    return (advanced, coeffs, upper_factor, directions.reshape(snapshots.shape))


def solution(mesh):
    return jax.shard_map(
        on_device,
        mesh=mesh,
        in_specs=(P(None, "slab", "role", None), P(None, "slab", "role", None), P(), P()),
        out_specs=(P(None, "slab", "role", None), P(), P(), P(None, "slab", "role", None)),
        check_vma=False,
    )
```

```python
import numpy as np
import jax
import jax.numpy as jnp
from jax import lax
from jax.experimental import pallas as pl
from jax.experimental.pallas import tpu as pltpu
from jax.sharding import PartitionSpec as P

viscosity = 0.1
ROWS = 16
time_step = 0.4


def extended(cells, sides, width, closed):
    for axis, dim in sides:
        count = lax.axis_size(axis)
        ends = count if closed else count - 1
        head = lax.slice_in_dim(cells, 0, width, axis=dim)
        tail = lax.slice_in_dim(cells, cells.shape[dim] - width, cells.shape[dim], axis=dim)
        if count == 2 and not closed:
            lower_side = lax.axis_index(axis) == 0
            got = lax.ppermute(jnp.where(lower_side, tail, head), axis, [(0, 1), (1, 0)])
            zeros = jnp.zeros_like(got)
            cells = jnp.concatenate(
                [jnp.where(lower_side, zeros, got), cells, jnp.where(lower_side, got, zeros)], axis=dim
            )
            continue
        cells = jnp.concatenate(
            [
                lax.ppermute(tail, axis, [(i, (i + 1) % count) for i in range(ends)]),
                cells,
                lax.ppermute(head, axis, [((i + 1) % count, i) for i in range(ends)]),
            ],
            axis=dim,
        )
    return cells


def ring_pairs(size, stride, count, second):
    pairs = []
    for i in range(count):
        digit = (i // stride) % size
        if size == 2 or not second:
            partner = digit ^ 1
        else:
            partner = (digit + 1) % size if digit % 2 else (digit - 1) % size
        pairs.append((i, i + (partner - digit) * stride))
    return pairs


def exchange_rounds(axis, count):
    rounds = []
    stride = 1
    while stride < count:
        size = 4 if count % (stride * 4) == 0 else 2
        rounds.append(ring_pairs(size, stride, count, False))
        if size == 4:
            rounds.append(ring_pairs(size, stride, count, True))
        stride *= size
    return [(axis, pairs) for pairs in rounds]


def allreduce(value, axes):
    sizes = [lax.axis_size(axis) for axis in axes]
    if any(size & (size - 1) for size in sizes):
        return lax.psum(value, axes)
    for axis, size in zip(axes, sizes):
        for name, pairs in exchange_rounds(axis, size):
            value = value + lax.ppermute(value, name, pairs)
    return value


def project_kernel(b_ref, s_ref, o_ref):
    tk, nr, nz = b_ref.shape
    ns = s_ref.shape[0]
    acc = jnp.zeros((tk * ROWS, ns * ROWS), jnp.float32)
    for j in range(nr // ROWS):
        rows = pl.ds(j * ROWS, ROWS)
        lhs = b_ref[:, rows, :].reshape(tk * ROWS, nz)
        rhs = s_ref[:, rows, :].reshape(ns * ROWS, nz)
        acc = acc + lax.dot_general(lhs, rhs, (((1,), (1,)), ((), ())), preferred_element_type=jnp.float32)
    row_t = lax.broadcasted_iota(jnp.int32, acc.shape, 0) % ROWS
    col_t = lax.broadcasted_iota(jnp.int32, acc.shape, 1) % ROWS
    acc = jnp.where(row_t == col_t, acc, 0.0)
    lanes = jnp.sum(acc.reshape(tk, ROWS, ns * ROWS), axis=1)
    group = lax.broadcasted_iota(jnp.int32, (ns, ns * ROWS), 1) // ROWS
    snapshot = lax.broadcasted_iota(jnp.int32, (ns, ns * ROWS), 0)
    gather = jnp.where(group == snapshot, 1.0, 0.0)
    o_ref[...] = lax.dot_general(gather, lanes, (((1,), (1,)), ((), ())),
                                 precision=lax.Precision.HIGHEST, preferred_element_type=jnp.float32)


def project(basis3, snaps3, tk=128):
    nk, nr, nz = basis3.shape
    ns = snaps3.shape[0]
    return pl.pallas_call(
        project_kernel,
        grid=(nk // tk,),
        in_specs=[pl.BlockSpec((tk, nr, nz), lambda i: (i, 0, 0)),
                  pl.BlockSpec((ns, nr, nz), lambda i: (0, 0, 0))],
        out_specs=pl.BlockSpec((ns, tk), lambda i: (0, i)),
        out_shape=jax.ShapeDtypeStruct((ns, nk), jnp.float32),
        cost_estimate=pl.CostEstimate(flops=2 * nk * nr * nz * ns * ROWS, transcendentals=0,
                                      bytes_accessed=nk * nr * nz * 2 + ns * nr * nz * 2 + nk * ns * 4),
    )(basis3, snaps3)


def residual_kernel(c_ref, b_ref, s_ref, o_ref, g_ref, spread_ref, acc_ref):
    nk, _, nz = b_ref.shape
    ns = s_ref.shape[0]
    rows = ROWS
    step = pl.program_id(0)

    @pl.when(step == 0)
    def _():
        col = lax.broadcasted_iota(jnp.int32, (nk, nk * rows), 1)
        row = lax.broadcasted_iota(jnp.int32, (nk, nk * rows), 0)
        expand = jnp.where(col // rows == row, 1.0, 0.0).astype(jnp.bfloat16)
        wide = jnp.dot(c_ref[...].astype(jnp.bfloat16), expand, preferred_element_type=jnp.float32)
        tall = jnp.broadcast_to(wide[:, None, :], (ns, rows, nk * rows)).reshape(ns * rows, nk * rows)
        r_t = lax.broadcasted_iota(jnp.int32, tall.shape, 0) % rows
        c_t = lax.broadcasted_iota(jnp.int32, tall.shape, 1) % rows
        spread_ref[...] = jnp.where(r_t == c_t, tall, 0.0).astype(jnp.bfloat16)
        acc_ref[...] = jnp.zeros_like(acc_ref)

    for part in range(b_ref.shape[1] // ROWS):
        window = pl.ds(part * ROWS, ROWS)
        block = b_ref[:, window, :].reshape(nk * ROWS, nz)
        prod = jnp.dot(spread_ref[...], block, preferred_element_type=jnp.float32)
        w = s_ref[:, window, :] - prod.reshape(ns, ROWS, nz)
        o_ref[:, window, :] = w
        p = 0
        for a in range(ns):
            for b in range(a, ns):
                term = w[a] * w[b]
                acc_ref[p] += term[: ROWS // 2] + term[ROWS // 2:]
                p += 1

    @pl.when(step == pl.num_programs(0) - 1)
    def _():
        row = lax.broadcasted_iota(jnp.int32, (ns, ns), 0)
        col = lax.broadcasted_iota(jnp.int32, (ns, ns), 1)
        gram = jnp.zeros((ns, ns), jnp.float32)
        p = 0
        for a in range(ns):
            for b in range(a, ns):
                total = jnp.sum(acc_ref[p])
                hit = ((row == a) & (col == b)) | ((row == b) & (col == a))
                gram = jnp.where(hit, total, gram)
                p += 1
        g_ref[...] = gram


def residual(coeffs_t, basis3, snaps3, block_rows=4 * ROWS):
    nk, nr, nz = basis3.shape
    ns = snaps3.shape[0]
    pairs = ns * (ns + 1) // 2
    w, g = pl.pallas_call(
        residual_kernel,
        grid=(nr // block_rows,),
        in_specs=[pl.BlockSpec((ns, nk), lambda j: (0, 0)),
                  pl.BlockSpec((nk, block_rows, nz), lambda j: (0, j, 0)),
                  pl.BlockSpec((ns, block_rows, nz), lambda j: (0, j, 0))],
        out_specs=[pl.BlockSpec((ns, block_rows, nz), lambda j: (0, j, 0)),
                   pl.BlockSpec((ns, ns), lambda j: (0, 0))],
        out_shape=[jax.ShapeDtypeStruct((ns, nr, nz), jnp.float32),
                   jax.ShapeDtypeStruct((ns, ns), jnp.float32)],
        scratch_shapes=[pltpu.VMEM((ns * ROWS, nk * ROWS), jnp.bfloat16),
                        pltpu.VMEM((pairs, ROWS // 2, nz), jnp.float32)],
        compiler_params=pltpu.CompilerParams(dimension_semantics=("arbitrary",)),
        cost_estimate=pl.CostEstimate(flops=2 * ns * ROWS * nk * ROWS * nz * (nr // ROWS), transcendentals=0,
                                      bytes_accessed=nk * nr * nz * 2 + 2 * ns * nr * nz * 4),
    )(coeffs_t, basis3, snaps3)
    return w, g


def factor_kernel(g_ref, w_ref, u_ref, d_ref):
    ns = g_ref.shape[0]
    gram = g_ref[...]
    row = lax.broadcasted_iota(jnp.int32, (ns, ns), 0)
    col = lax.broadcasted_iota(jnp.int32, (ns, ns), 1)
    upper = jnp.zeros((ns, ns), jnp.float32)
    for j in range(ns):
        grow = jnp.sum(jnp.where(row == j, gram, 0.0), axis=0, keepdims=True)
        ucol = jnp.sum(jnp.where(col == j, upper, 0.0), axis=1, keepdims=True)
        v = grow - jnp.sum(upper * ucol, axis=0, keepdims=True)
        root = jnp.sqrt(jnp.sum(jnp.where(col[:1] == j, v, 0.0)))
        newrow = jnp.where(col[:1] > j, v / root, jnp.where(col[:1] == j, root, 0.0))
        upper = jnp.where(row == j, newrow, upper)
    u_ref[...] = upper

    def entry(s, t):
        return jnp.sum(jnp.where((row == t) & (col == s), upper, 0.0))

    for s in range(ns):
        acc = w_ref[s]
        for t in range(s):
            acc = acc - entry(s, t) * d_ref[t]
        d_ref[s] = acc / entry(s, s)


def factor_and_solve(gram, residual3):
    ns = gram.shape[0]
    vmem = pl.BlockSpec(memory_space=pltpu.VMEM)
    return pl.pallas_call(
        factor_kernel,
        in_specs=[vmem, vmem],
        out_specs=[vmem, vmem],
        out_shape=[jax.ShapeDtypeStruct((ns, ns), jnp.float32),
                   jax.ShapeDtypeStruct(residual3.shape, jnp.float32)],
        cost_estimate=pl.CostEstimate(flops=ns * ns * residual3[0].size, transcendentals=ns,
                                      bytes_accessed=2 * residual3.size * 4),
    )(gram, residual3)


def offset_slice(padded, offset, dimension, length):
    return lax.slice_in_dim(padded, 2 + offset, 2 + offset + length, axis=dimension)


def second_diff(padded, center, dimension, length):
    return (
        -offset_slice(padded, 2, dimension, length)
        + 16.0 * offset_slice(padded, 1, dimension, length)
        - 30.0 * center
        + 16.0 * offset_slice(padded, -1, dimension, length)
        - offset_slice(padded, -2, dimension, length)
    ) / 12.0


def local_terms(center, ypadded, flow_rows, shear_rows):
    ny_loc = center.shape[2]
    nz_loc = center.shape[3]
    zpadded = jnp.concatenate([center[..., -2:], center, center[..., :2]], axis=3)
    local = viscosity * (second_diff(ypadded, center, 2, ny_loc) + second_diff(zpadded, center, 3, nz_loc))
    shear_term = shear_rows[None, None, :, None] * center[1:2]
    return jnp.concatenate([local[:1] - shear_term, local[1:]], axis=0)


def streamwise_terms(center, xpadded, flow_rows):
    nx_loc = center.shape[1]
    first_x = (
        -offset_slice(xpadded, 2, 1, nx_loc)
        + 8.0 * offset_slice(xpadded, 1, 1, nx_loc)
        - 8.0 * offset_slice(xpadded, -1, 1, nx_loc)
        + offset_slice(xpadded, -2, 1, nx_loc)
    ) / 12.0
    profile = flow_rows[None, None, :, None]
    return -profile * first_x + viscosity * second_diff(xpadded, center, 1, nx_loc)


def segmented_tendency(center, flow_rows, shear_rows):
    xpadded = extended(center, (("slab", 1),), 2, True)
    ypadded = extended(center, (("role", 2),), 2, False)
    local = local_terms(center, ypadded, flow_rows, shear_rows)
    return streamwise_terms(center, xpadded, flow_rows) + local


def on_device(velocity, basis, mean_flow, shear):
    ny_loc = velocity.shape[2]
    role_index = lax.axis_index("role")
    flow_rows = lax.dynamic_slice_in_dim(mean_flow, role_index * ny_loc, ny_loc)
    shear_rows = lax.dynamic_slice_in_dim(shear, role_index * ny_loc, ny_loc)
    tend_zero = segmented_tendency(velocity, flow_rows, shear_rows)
    segment_one = velocity + time_step * (8.0 / 15.0) * tend_zero
    tend_one = segmented_tendency(segment_one, flow_rows, shear_rows)
    advanced = segment_one + time_step * (5.0 / 12.0 * tend_one - 17.0 / 60.0 * tend_zero)
    snapshots = jnp.concatenate([segment_one, advanced], axis=0)
    ns = snapshots.shape[0]
    snaps3 = snapshots.reshape(ns, -1, snapshots.shape[3])
    basis3 = basis.reshape(basis.shape[0], -1, basis.shape[3])
    partial_proj = project(basis3, snaps3.astype(jnp.bfloat16))
    coeffs_t = allreduce(partial_proj, ("role", "slab"))
    coeffs = coeffs_t.T
    residual3, local_gram = residual(coeffs_t, basis3, snaps3)
    total_gram = allreduce(local_gram, ("role", "slab"))
    upper_factor, directions = factor_and_solve(total_gram, residual3)
    return (advanced, coeffs, upper_factor, directions.reshape(snapshots.shape))


def solution(mesh):
    return jax.shard_map(
        on_device,
        mesh=mesh,
        in_specs=(P(None, "slab", "role", None), P(None, "slab", "role", None), P(), P()),
        out_specs=(P(None, "slab", "role", None), P(), P(), P(None, "slab", "role", None)),
        check_vma=False,
    )
```

```python
import numpy as np
import jax
import jax.numpy as jnp
from jax import lax
from jax.experimental import pallas as pl
from jax.experimental.pallas import tpu as pltpu
from jax.sharding import PartitionSpec as P

viscosity = 0.1
ROWS = 16
time_step = 0.4


def extended(cells, sides, width, closed):
    for axis, dim in sides:
        count = lax.axis_size(axis)
        ends = count if closed else count - 1
        head = lax.slice_in_dim(cells, 0, width, axis=dim)
        tail = lax.slice_in_dim(cells, cells.shape[dim] - width, cells.shape[dim], axis=dim)
        if count == 2 and not closed:
            lower_side = lax.axis_index(axis) == 0
            got = lax.ppermute(jnp.where(lower_side, tail, head), axis, [(0, 1), (1, 0)])
            zeros = jnp.zeros_like(got)
            cells = jnp.concatenate(
                [jnp.where(lower_side, zeros, got), cells, jnp.where(lower_side, got, zeros)], axis=dim
            )
            continue
        cells = jnp.concatenate(
            [
                lax.ppermute(tail, axis, [(i, (i + 1) % count) for i in range(ends)]),
                cells,
                lax.ppermute(head, axis, [((i + 1) % count, i) for i in range(ends)]),
            ],
            axis=dim,
        )
    return cells


def ring_pairs(size, stride, count, second):
    pairs = []
    for i in range(count):
        digit = (i // stride) % size
        if size == 2 or not second:
            partner = digit ^ 1
        else:
            partner = (digit + 1) % size if digit % 2 else (digit - 1) % size
        pairs.append((i, i + (partner - digit) * stride))
    return pairs


def exchange_rounds(axis, count):
    rounds = []
    stride = 1
    while stride < count:
        size = 4 if count % (stride * 4) == 0 else 2
        rounds.append(ring_pairs(size, stride, count, False))
        if size == 4:
            rounds.append(ring_pairs(size, stride, count, True))
        stride *= size
    return [(axis, pairs) for pairs in rounds]


def allreduce_halves(value, axes):
    sizes = [lax.axis_size(axis) for axis in axes]
    if any(size & (size - 1) for size in sizes):
        return lax.psum(value, axes), jnp.zeros_like(value)
    rounds = [step for axis, size in zip(axes, sizes) for step in exchange_rounds(axis, size)]
    for name, pairs in rounds[:-1]:
        value = value + lax.ppermute(value, name, pairs)
    name, pairs = rounds[-1]
    return value, lax.ppermute(value, name, pairs)


def project_kernel(b_ref, s_ref, o_ref):
    tk, nr, nz = b_ref.shape
    ns = s_ref.shape[0]
    acc = jnp.zeros((tk * ROWS, ns * ROWS), jnp.float32)
    for j in range(nr // ROWS):
        rows = pl.ds(j * ROWS, ROWS)
        lhs = b_ref[:, rows, :].reshape(tk * ROWS, nz)
        rhs = s_ref[:, rows, :].reshape(ns * ROWS, nz)
        acc = acc + lax.dot_general(lhs, rhs, (((1,), (1,)), ((), ())), preferred_element_type=jnp.float32)
    row_t = lax.broadcasted_iota(jnp.int32, acc.shape, 0) % ROWS
    col_t = lax.broadcasted_iota(jnp.int32, acc.shape, 1) % ROWS
    acc = jnp.where(row_t == col_t, acc, 0.0)
    lanes = jnp.sum(acc.reshape(tk, ROWS, ns * ROWS), axis=1)
    group = lax.broadcasted_iota(jnp.int32, (ns, ns * ROWS), 1) // ROWS
    snapshot = lax.broadcasted_iota(jnp.int32, (ns, ns * ROWS), 0)
    gather = jnp.where(group == snapshot, 1.0, 0.0)
    o_ref[...] = lax.dot_general(gather, lanes, (((1,), (1,)), ((), ())),
                                 precision=lax.Precision.HIGHEST, preferred_element_type=jnp.float32)


def project(basis3, snaps3, tk=128):
    nk, nr, nz = basis3.shape
    ns = snaps3.shape[0]
    return pl.pallas_call(
        project_kernel,
        grid=(nk // tk,),
        in_specs=[pl.BlockSpec((tk, nr, nz), lambda i: (i, 0, 0)),
                  pl.BlockSpec((ns, nr, nz), lambda i: (0, 0, 0))],
        out_specs=pl.BlockSpec((ns, tk), lambda i: (0, i)),
        out_shape=jax.ShapeDtypeStruct((ns, nk), jnp.float32),
        cost_estimate=pl.CostEstimate(flops=2 * nk * nr * nz * ns * ROWS, transcendentals=0,
                                      bytes_accessed=nk * nr * nz * 2 + ns * nr * nz * 2 + nk * ns * 4),
    )(basis3, snaps3)


def residual_kernel(c_ref, d_ref, b_ref, s_ref, o_ref, g_ref, spread_ref, acc_ref):
    nk, _, nz = b_ref.shape
    ns = s_ref.shape[0]
    rows = ROWS
    step = pl.program_id(0)

    @pl.when(step == 0)
    def _():
        col = lax.broadcasted_iota(jnp.int32, (nk, nk * rows), 1)
        row = lax.broadcasted_iota(jnp.int32, (nk, nk * rows), 0)
        expand = jnp.where(col // rows == row, 1.0, 0.0).astype(jnp.bfloat16)
        wide = jnp.dot((c_ref[...] + d_ref[...]).astype(jnp.bfloat16), expand, preferred_element_type=jnp.float32)
        tall = jnp.broadcast_to(wide[:, None, :], (ns, rows, nk * rows)).reshape(ns * rows, nk * rows)
        r_t = lax.broadcasted_iota(jnp.int32, tall.shape, 0) % rows
        c_t = lax.broadcasted_iota(jnp.int32, tall.shape, 1) % rows
        spread_ref[...] = jnp.where(r_t == c_t, tall, 0.0).astype(jnp.bfloat16)
        acc_ref[...] = jnp.zeros_like(acc_ref)

    for part in range(b_ref.shape[1] // ROWS):
        window = pl.ds(part * ROWS, ROWS)
        block = b_ref[:, window, :].reshape(nk * ROWS, nz)
        prod = jnp.dot(spread_ref[...], block, preferred_element_type=jnp.float32)
        w = s_ref[:, window, :] - prod.reshape(ns, ROWS, nz)
        o_ref[:, window, :] = w
        p = 0
        for a in range(ns):
            for b in range(a, ns):
                term = w[a] * w[b]
                acc_ref[p] += term[: ROWS // 2] + term[ROWS // 2:]
                p += 1

    @pl.when(step == pl.num_programs(0) - 1)
    def _():
        row = lax.broadcasted_iota(jnp.int32, (ns, ns), 0)
        col = lax.broadcasted_iota(jnp.int32, (ns, ns), 1)
        gram = jnp.zeros((ns, ns), jnp.float32)
        p = 0
        for a in range(ns):
            for b in range(a, ns):
                total = jnp.sum(acc_ref[p])
                hit = ((row == a) & (col == b)) | ((row == b) & (col == a))
                gram = jnp.where(hit, total, gram)
                p += 1
        g_ref[...] = gram


def residual(coeffs_t, coeffs_other, basis3, snaps3, block_rows=4 * ROWS):
    nk, nr, nz = basis3.shape
    ns = snaps3.shape[0]
    pairs = ns * (ns + 1) // 2
    w, g = pl.pallas_call(
        residual_kernel,
        grid=(nr // block_rows,),
        in_specs=[pl.BlockSpec((ns, nk), lambda j: (0, 0)),
                  pl.BlockSpec((ns, nk), lambda j: (0, 0)),
                  pl.BlockSpec((nk, block_rows, nz), lambda j: (0, j, 0)),
                  pl.BlockSpec((ns, block_rows, nz), lambda j: (0, j, 0))],
        out_specs=[pl.BlockSpec((ns, block_rows, nz), lambda j: (0, j, 0)),
                   pl.BlockSpec((ns, ns), lambda j: (0, 0))],
        out_shape=[jax.ShapeDtypeStruct((ns, nr, nz), jnp.float32),
                   jax.ShapeDtypeStruct((ns, ns), jnp.float32)],
        scratch_shapes=[pltpu.VMEM((ns * ROWS, nk * ROWS), jnp.bfloat16),
                        pltpu.VMEM((pairs, ROWS // 2, nz), jnp.float32)],
        compiler_params=pltpu.CompilerParams(dimension_semantics=("arbitrary",)),
        cost_estimate=pl.CostEstimate(flops=2 * ns * ROWS * nk * ROWS * nz * (nr // ROWS), transcendentals=0,
                                      bytes_accessed=nk * nr * nz * 2 + 2 * ns * nr * nz * 4),
    )(coeffs_t, coeffs_other, basis3, snaps3)
    return w, g


def factor_kernel(g_ref, h_ref, w_ref, u_ref, d_ref):
    ns = g_ref.shape[0]
    gram = g_ref[...] + h_ref[...]
    row = lax.broadcasted_iota(jnp.int32, (ns, ns), 0)
    col = lax.broadcasted_iota(jnp.int32, (ns, ns), 1)
    upper = jnp.zeros((ns, ns), jnp.float32)
    for j in range(ns):
        grow = jnp.sum(jnp.where(row == j, gram, 0.0), axis=0, keepdims=True)
        ucol = jnp.sum(jnp.where(col == j, upper, 0.0), axis=1, keepdims=True)
        v = grow - jnp.sum(upper * ucol, axis=0, keepdims=True)
        root = jnp.sqrt(jnp.sum(jnp.where(col[:1] == j, v, 0.0)))
        newrow = jnp.where(col[:1] > j, v / root, jnp.where(col[:1] == j, root, 0.0))
        upper = jnp.where(row == j, newrow, upper)
    u_ref[...] = upper

    def entry(s, t):
        return jnp.sum(jnp.where((row == t) & (col == s), upper, 0.0))

    for s in range(ns):
        acc = w_ref[s]
        for t in range(s):
            acc = acc - entry(s, t) * d_ref[t]
        d_ref[s] = acc / entry(s, s)


def factor_and_solve(gram, gram_other, residual3):
    ns = gram.shape[0]
    vmem = pl.BlockSpec(memory_space=pltpu.VMEM)
    return pl.pallas_call(
        factor_kernel,
        in_specs=[vmem, vmem, vmem],
        out_specs=[vmem, vmem],
        out_shape=[jax.ShapeDtypeStruct((ns, ns), jnp.float32),
                   jax.ShapeDtypeStruct(residual3.shape, jnp.float32)],
        cost_estimate=pl.CostEstimate(flops=ns * ns * residual3[0].size, transcendentals=ns,
                                      bytes_accessed=2 * residual3.size * 4),
    )(gram, gram_other, residual3)


def offset_slice(padded, offset, dimension, length):
    return lax.slice_in_dim(padded, 2 + offset, 2 + offset + length, axis=dimension)


def second_diff(padded, center, dimension, length):
    return (
        -offset_slice(padded, 2, dimension, length)
        + 16.0 * offset_slice(padded, 1, dimension, length)
        - 30.0 * center
        + 16.0 * offset_slice(padded, -1, dimension, length)
        - offset_slice(padded, -2, dimension, length)
    ) / 12.0


def local_terms(center, ypadded, flow_rows, shear_rows):
    ny_loc = center.shape[2]
    nz_loc = center.shape[3]
    zpadded = jnp.concatenate([center[..., -2:], center, center[..., :2]], axis=3)
    local = viscosity * (second_diff(ypadded, center, 2, ny_loc) + second_diff(zpadded, center, 3, nz_loc))
    shear_term = shear_rows[None, None, :, None] * center[1:2]
    return jnp.concatenate([local[:1] - shear_term, local[1:]], axis=0)


def streamwise_terms(center, xpadded, flow_rows):
    nx_loc = center.shape[1]
    first_x = (
        -offset_slice(xpadded, 2, 1, nx_loc)
        + 8.0 * offset_slice(xpadded, 1, 1, nx_loc)
        - 8.0 * offset_slice(xpadded, -1, 1, nx_loc)
        + offset_slice(xpadded, -2, 1, nx_loc)
    ) / 12.0
    profile = flow_rows[None, None, :, None]
    return -profile * first_x + viscosity * second_diff(xpadded, center, 1, nx_loc)


def segmented_tendency(center, flow_rows, shear_rows):
    xpadded = extended(center, (("slab", 1),), 2, True)
    ypadded = extended(center, (("role", 2),), 2, False)
    local = local_terms(center, ypadded, flow_rows, shear_rows)
    return streamwise_terms(center, xpadded, flow_rows) + local


def on_device(velocity, basis, mean_flow, shear):
    ny_loc = velocity.shape[2]
    role_index = lax.axis_index("role")
    flow_rows = lax.dynamic_slice_in_dim(mean_flow, role_index * ny_loc, ny_loc)
    shear_rows = lax.dynamic_slice_in_dim(shear, role_index * ny_loc, ny_loc)
    tend_zero = segmented_tendency(velocity, flow_rows, shear_rows)
    segment_one = velocity + time_step * (8.0 / 15.0) * tend_zero
    tend_one = segmented_tendency(segment_one, flow_rows, shear_rows)
    advanced = segment_one + time_step * (5.0 / 12.0 * tend_one - 17.0 / 60.0 * tend_zero)
    snapshots = jnp.concatenate([segment_one, advanced], axis=0)
    ns = snapshots.shape[0]
    snaps3 = snapshots.reshape(ns, -1, snapshots.shape[3])
    basis3 = basis.reshape(basis.shape[0], -1, basis.shape[3])
    partial_proj = project(basis3, snaps3.astype(jnp.bfloat16))
    coeffs_t, coeffs_other = allreduce_halves(partial_proj, ("role", "slab"))
    coeffs = (coeffs_t + coeffs_other).T
    residual3, local_gram = residual(coeffs_t, coeffs_other, basis3, snaps3)
    gram, gram_other = allreduce_halves(local_gram, ("role", "slab"))
    upper_factor, directions = factor_and_solve(gram, gram_other, residual3)
    return (advanced, coeffs, upper_factor, directions.reshape(snapshots.shape))


def solution(mesh):
    return jax.shard_map(
        on_device,
        mesh=mesh,
        in_specs=(P(None, "slab", "role", None), P(None, "slab", "role", None), P(), P()),
        out_specs=(P(None, "slab", "role", None), P(), P(), P(None, "slab", "role", None)),
        check_vma=False,
    )
```
